256 devices in a mesh: elem: 32 (over z, x), blk: 8 (over y, core).
Axes of the slice: x: 4, y: 4, z: 8, core: 2. Of those that a mesh axis runs over, the one named last changes fastest.
Arguments:
- basis: bfloat16 [32768, 3, 512], P('elem'), may hold values from -6 to 6
- send_rows: int32 [32, 8, 256], P('elem', 'blk'), may hold values from 0 to 1023
- elem_slot: int32 [8, 16384], P(None, ('elem', 'blk')), may hold values from 0 to 255, as said below
- set_size: int32 [32], replicated, may hold values from 1 to 512, 10240 in all
- elem_weight: float32 [16384], P(('elem', 'blk')), may hold values from 0.2 to 5
- element_stiffening: float32 [16384], P(('elem', 'blk')), may hold values from 1 to 8
- state: bfloat16 [512], replicated, may hold values from -0.25 to 0.25
- load: float32 [512], P('blk'), may hold values from -6 to 6
Outputs:
- tangent: float32 [512, 512], P('elem', 'blk')
- residual: float32 [512], P('blk')
The draws below stay inside these ranges and needn't reach their ends.
Inputs may be any that keep to these rules, and one draw needn't show every extreme that they name: `elem_slot`: for element column of device (s, b): p names slot p % 8 of what owner p // 8 sends to that device. From each owner only its first n slots are named, n at most 8; for every device exactly one owner gives 8, and the n over all owners sum to 128.
All inputs are finite; a program needn't handle non-finite values.
Results may differ from the reference program's by a relative error of at most 0.0003.
Values may be sent and summed in bfloat16 or wider, within the bound.
No kernel may reach another device: no remote copies, remote signals or barrier semaphores. Data moves between devices by JAX's collectives and lax.ppermute only.
A program may use at most 64 MiB of HBM per device.

```python
import math
import jax
import jax.numpy as jnp
import numpy as np
from jax import lax

MODE_COUNT = 512
ELEMENT_SLOTS = 64
SETS = 32
SET_ELEMS = 512
ELEMS = 16384
NODES_DEV = 1024
NODES = 32768
CAP = 8
LIVE = 10240
N_BLK = 8


def draw_elem_slot(key, part):
    units = SETS * N_BLK
    used = 2 * ELEMENT_SLOTS
    heavy_key, order_key, pick_key = jax.random.split(key, 3)
    source = lax.broadcasted_iota(jnp.int32, (units, SETS), 1)
    heavy = jax.random.randint(heavy_key, (units, 1), 0, SETS)
    scores = jax.random.randint(order_key, (units, SETS), 0, 1 << 20) * SETS + source
    scores = jnp.where(source == heavy, (1 << 20) * SETS + source, scores)
    rank = jnp.argsort(jnp.argsort(scores, axis=1), axis=1)
    base = (used - CAP) // (SETS - 1)
    extra = used - CAP - base * (SETS - 1)
    counts = jnp.where(source == heavy, CAP, base + (rank < extra).astype(jnp.int32))
    ends = jnp.cumsum(counts, axis=1)
    starts = ends - counts
    pick = jax.random.randint(pick_key, (units, 8 * ELEMENT_SLOTS), 0, used)
    owner = jnp.sum((ends[:, None, :] <= pick[:, :, None]).astype(jnp.int32), axis=2)
    first = jnp.take_along_axis(starts, owner, axis=1)
    slot = owner * CAP + pick - first
    return slot.reshape(units, ELEMENT_SLOTS, 8).transpose(2, 0, 1).reshape(8, units * ELEMENT_SLOTS).astype(jnp.int32)


def with_ends(values, stream_key, least, top_value):
    place = [jax.random.randint(jax.random.fold_in(stream_key, axis), (), 0, length) for axis, length in enumerate(values.shape)]
    widest = values.shape.index(max(values.shape))
    beside = place[:widest] + [(place[widest] + 1) % values.shape[widest]] + place[widest + 1:]
    return values.at[tuple(place)].set(least).at[tuple(beside)].set(top_value)


def block_levels(key, extent, shards, smallest, high):
    loudness, own = 1.0, jax.random.fold_in(key, 6)
    for dim, blocks in shards:
        draws = jnp.exp(jax.random.uniform(jax.random.fold_in(own, dim), (blocks,), jnp.float32, smallest / len(shards), high / len(shards)))
        loudness = loudness * jnp.repeat(draws, extent[dim] // blocks).reshape([-1 if axis == dim else 1 for axis in range(len(extent))])
    return loudness


def split_up(number_of, total, bound, lean):
    loads = [(1 << 20) // math.isqrt(standing ** lean) + 1 for standing in range(2, number_of + 1)]
    rest, given = total - bound - (number_of - 1), [1] * (number_of - 1)
    while rest > 0:
        free = [i for i in range(number_of - 1) if given[i] < bound]
        mass, remaining = sum([loads[i] for i in free]), rest
        for i in free:
            addition = min(bound - given[i], max(1, remaining * loads[i] // mass), rest)
            given[i] = given[i] + addition
            rest = rest - addition
    return np.array([bound] + given)


def ragged_sizes(own_key, number_of, total, bound, lean):
    if number_of == 2:
        one = jax.random.randint(own_key, (), max(1, total - bound), min(bound, total - 1) + 1)
        return jnp.stack([one, total - one])
    sizes = jnp.asarray(split_up(number_of, total, bound, lean), jnp.int32)
    pairs = (number_of - 1) // 2
    donor, taker = sizes[1:1 + 2 * pairs:2], sizes[2:2 + 2 * pairs:2]
    slack = jnp.minimum(donor - 1, bound - taker)
    moved = jax.random.randint(jax.random.fold_in(own_key, 1), (pairs,), 0, 1 << 20) % (slack + 1)
    sizes = sizes.at[1:1 + 2 * pairs:2].set(donor - moved).at[2:2 + 2 * pairs:2].set(taker + moved)
    return sizes[jax.random.permutation(jax.random.fold_in(own_key, 2), number_of)]


def gaussian(stream_key, shape, spread, most, cuts=(), held_as=jnp.bfloat16):
    level = block_levels(stream_key, shape, cuts, -0.22, 0.18) if cuts else 1.0
    array = jax.random.normal(stream_key, shape, jnp.float32) * spread * level
    return jnp.minimum(jnp.maximum(array, -most), most).astype(held_as)


def setup_inputs(seed: int = 0) -> dict:
    key_of = jax.random.split(jax.random.key(seed), 9)
    return {
        "basis": gaussian(key_of[0], (NODES, 3, MODE_COUNT), 1.0, 6.0, ((0, 32),)),
        "send_rows": with_ends(jax.random.randint(key_of[1], (SETS, N_BLK, SETS * CAP), 0, NODES_DEV), jax.random.fold_in(key_of[1], 1), 0, NODES_DEV - 1).astype(jnp.int32),
        "elem_slot": draw_elem_slot(jax.random.fold_in(key_of[8], 71), 0),
        "set_size": ragged_sizes(key_of[3], SETS, LIVE, SET_ELEMS, 2).astype(jnp.int32),
        "elem_weight": jnp.clip(jnp.exp(math.log(5.0) - 3.218876 * jax.random.uniform(key_of[4], (ELEMS,), jnp.float32) ** block_levels(key_of[4], (ELEMS,), ((0, 256),), -0.2, 0.2)), 0.2, 5.0),
        "element_stiffening": jnp.clip(jnp.exp(math.log(8.0) - 2.0794415 * jax.random.uniform(key_of[5], (ELEMS,), jnp.float32) ** block_levels(key_of[5], (ELEMS,), ((0, 256),), -0.2, 0.2)), 1.0, 8.0),
        "state": gaussian(key_of[6], (MODE_COUNT,), (0.4 / MODE_COUNT ** 0.5), 0.25),
        "load": gaussian(key_of[7], (MODE_COUNT,), 1.0, 6.0, ((0, 8),), jnp.float32),
    }


def corner_grads():
    corner = jnp.arange(8)[:, None]
    bit = corner // 2 ** jnp.arange(3)[None, :] % 2
    return (bit * 2 - 1).astype(jnp.float32) * 0.25

def element_contributions(basis_matrix, displacement, stiffening_power):
    grads = corner_grads()
    element_count = basis_matrix.shape[0]
    basis_modes = basis_matrix.shape[2]
    corner_nodes = basis_matrix.reshape(element_count, 8, 3, basis_modes)
    grad_basis = jnp.einsum('ak,eacm->ekcm', grads, corner_nodes, precision=lax.Precision.HIGHEST)
    moved = displacement.reshape(8, 3, element_count)
    hgrad = jnp.einsum('ak,ace->kce', grads, moved, precision=lax.Precision.HIGHEST)
    volume = hgrad[0, 0] + hgrad[1, 1] + hgrad[2, 2]
    stiff = 1.0 + stiffening_power * volume ** 2 - 2.0 / 3.0
    press = volume + stiffening_power * volume ** 3 / 3.0 - 2.0 / 3.0 * volume
    eye = jnp.eye(3, dtype=jnp.float32)
    stress = hgrad + jnp.transpose(hgrad, (1, 0, 2)) + press[None, None, :] * eye[:, :, None]
    force_vector = jnp.einsum('ak,kce->ace', grads, stress, precision=lax.Precision.HIGHEST).reshape(24, element_count) + 0.25 * displacement
    sym = grad_basis + jnp.transpose(grad_basis, (0, 2, 1, 3))
    trace_basis = grad_basis[:, 0, 0] + grad_basis[:, 1, 1] + grad_basis[:, 2, 2]
    mode_image = jnp.einsum('ak,ekcm->eacm', grads, sym, precision=lax.Precision.HIGHEST)
    mode_image = mode_image + stiff[:, None, None, None] * grads[None, :, :, None] * trace_basis[:, None, None, :] + 0.25 * corner_nodes
    return (mode_image.reshape(element_count, 24, basis_modes), force_vector)

def reference(basis, send_rows, elem_slot, set_size, elem_weight, element_stiffening, state, load):
    units = SETS * N_BLK
    full_state = state.astype(jnp.float32)

    def step(carry, unit):
        total_tangent, total_force = carry
        group = unit // N_BLK
        block = unit % N_BLK
        slots = lax.dynamic_slice_in_dim(elem_slot, unit * ELEMENT_SLOTS, ELEMENT_SLOTS, 1)
        source = slots // CAP
        local = send_rows[source, block, group * CAP + slots % CAP]
        node_index = source * NODES_DEV + local
        basis_matrix = basis[node_index.T].reshape(ELEMENT_SLOTS, 24, MODE_COUNT).astype(jnp.float32)
        position = block * ELEMENT_SLOTS + jnp.arange(ELEMENT_SLOTS).astype(jnp.int32)
        weights = lax.dynamic_slice_in_dim(elem_weight, unit * ELEMENT_SLOTS, ELEMENT_SLOTS, 0)
        weights = jnp.where(position < set_size[group], weights, jnp.zeros_like(weights))
        stiffening_power = lax.dynamic_slice_in_dim(element_stiffening, unit * ELEMENT_SLOTS, ELEMENT_SLOTS, 0)
        displacement = jnp.einsum('agd,d->ga', basis_matrix, full_state, precision=lax.Precision.HIGHEST)
        mode_image, force_vector = element_contributions(basis_matrix, displacement, stiffening_power)
        weighted_image = lax.optimization_barrier((weights[:, None, None] * mode_image).astype(jnp.bfloat16)).astype(jnp.float32)
        weighted_force = lax.optimization_barrier((force_vector * weights[None, :]).astype(jnp.bfloat16)).astype(jnp.float32)
        partial_tangent = lax.dot_general(basis_matrix, weighted_image, (((0, 1), (0, 1)), ((), ())), precision=lax.Precision.HIGHEST)
        partial_force = lax.dot_general(basis_matrix, weighted_force, (((0, 1), (1, 0)), ((), ())), precision=lax.Precision.HIGHEST)
        return ((total_tangent + partial_tangent, total_force + partial_force), None)
    start = (jnp.zeros((MODE_COUNT, MODE_COUNT), jnp.float32), jnp.zeros((MODE_COUNT,), jnp.float32))
    (tangent, force_vector), _ = lax.scan(step, start, jnp.arange(units).astype(jnp.int32))
    scale = lax.rsqrt(24.0 * jnp.sum(set_size).astype(jnp.float32))
    return (tangent * scale, force_vector * scale - load)
```

```python
import jax
import jax.numpy as jnp
from jax import lax
from jax.sharding import PartitionSpec as P


def corner_grads():
    corner = jnp.arange(8)[:, None]
    bit = corner // 2 ** jnp.arange(3)[None, :] % 2
    return (bit * 2 - 1).astype(jnp.float32) * 0.25


def element_contributions(basis_matrix, displacement, stiffening_power):
    grads = corner_grads()
    element_count = basis_matrix.shape[0]
    basis_modes = basis_matrix.shape[2]
    corner_nodes = basis_matrix.reshape(element_count, 8, 3, basis_modes)
    grad_basis = jnp.einsum(
        "ak,eacm->ekcm",
        grads.astype(jnp.bfloat16),
        corner_nodes,
        preferred_element_type=jnp.float32,
    )
    moved = displacement.reshape(8, 3, element_count)
    hgrad = jnp.einsum("ak,ace->kce", grads, moved, precision=lax.Precision.HIGHEST)
    volume = hgrad[0, 0] + hgrad[1, 1] + hgrad[2, 2]
    stiff = 1.0 + stiffening_power * volume**2 - 2.0 / 3.0
    press = volume + stiffening_power * volume**3 / 3.0 - 2.0 / 3.0 * volume
    eye = jnp.eye(3, dtype=jnp.float32)
    stress = hgrad + jnp.transpose(hgrad, (1, 0, 2)) + press[None, None, :] * eye[:, :, None]
    force_vector = (
        jnp.einsum("ak,kce->ace", grads, stress, precision=lax.Precision.HIGHEST).reshape(
            24, element_count
        )
        + 0.25 * displacement
    )
    sym = grad_basis + jnp.transpose(grad_basis, (0, 2, 1, 3))
    trace_basis = grad_basis[:, 0, 0] + grad_basis[:, 1, 1] + grad_basis[:, 2, 2]
    mode_image = jnp.einsum("ak,ekcm->eacm", grads, sym, precision=lax.Precision.HIGHEST)
    mode_image = (
        mode_image
        + stiff[:, None, None, None] * grads[None, :, :, None] * trace_basis[:, None, None, :]
        + 0.25 * corner_nodes.astype(jnp.float32)
    )
    return (mode_image.reshape(element_count, 24, basis_modes), force_vector)


def local(basis, send_rows, elem_slot, set_size, elem_weight, element_stiffening, state, load):
    nodes = basis.shape[0]
    basis_modes = basis.shape[2]
    n_elem = lax.psum(1, "elem")
    n_blk = lax.psum(1, "blk")
    flat = basis.reshape(nodes, 3 * basis_modes)
    outgoing = jnp.take(flat, send_rows[0, 0], axis=0)
    arrived = lax.all_to_all(outgoing, "elem", split_axis=0, concat_axis=0, tiled=True)
    element_count = elem_slot.shape[1]
    chosen_elements = jnp.take(arrived, elem_slot.T.reshape(-1), axis=0)
    basis_matrix = chosen_elements.reshape(element_count, 24, basis_modes)
    set_index = lax.axis_index("elem")
    block_index = lax.axis_index("blk")
    live = lax.dynamic_index_in_dim(set_size, set_index, keepdims=False)
    position = block_index * element_count + jnp.arange(element_count, dtype=jnp.int32)
    weights = jnp.where(position < live, elem_weight, jnp.zeros_like(elem_weight))
    displacement = jnp.einsum("agd,d->ga", basis_matrix, state, preferred_element_type=jnp.float32)
    mode_image, force_vector = element_contributions(basis_matrix, displacement, element_stiffening)
    weighted_image = (weights[:, None, None] * mode_image).astype(jnp.bfloat16)
    weighted_force = (force_vector * weights[None, :]).astype(jnp.bfloat16)
    rows = basis_modes // n_elem
    cols = basis_modes // n_blk
    tangent = jnp.einsum(
        "egri,egbc->rbic",
        basis_matrix.reshape(element_count, 24, n_elem, rows),
        weighted_image.reshape(element_count, 24, n_blk, cols),
        preferred_element_type=jnp.float32,
    )
    force_all = lax.dot_general(
        basis_matrix,
        weighted_force,
        (((0, 1), (1, 0)), ((), ())),
        preferred_element_type=jnp.float32,
    )
    force_rows = jnp.broadcast_to(force_all.reshape(1, n_blk, 1, cols), (n_elem, n_blk, 1, cols))
    both = jnp.concatenate([tangent, force_rows], axis=2).reshape(n_elem * n_blk * (rows + 1), cols)
    mine = lax.psum_scatter(both, ("elem", "blk"), scatter_dimension=0, tiled=True)
    scale = lax.rsqrt(24.0 * jnp.sum(set_size).astype(jnp.float32))
    return (mine[:rows] * scale, mine[rows] * scale - load)


def solution(mesh):
    in_specs = (
        P("elem", None, None),
        P("elem", "blk", None),
        P(None, ("elem", "blk")),
        P(),
        P(("elem", "blk")),
        P(("elem", "blk")),
        P(),
        P("blk"),
    )
    out_specs = (P("elem", "blk"), P("blk"))
    return jax.shard_map(local, mesh=mesh, in_specs=in_specs, out_specs=out_specs, check_vma=False)
```

```python
import jax
import jax.numpy as jnp
from jax import lax
from jax.sharding import PartitionSpec as P


def corner_grads():
    corner = jnp.arange(8)[:, None]
    bit = corner // 2 ** jnp.arange(3)[None, :] % 2
    return (bit * 2 - 1).astype(jnp.float32) * 0.25


def element_contributions(basis_matrix, displacement, stiffening_power):
    grads = corner_grads()
    element_count = basis_matrix.shape[0]
    basis_modes = basis_matrix.shape[2]
    corner_nodes = basis_matrix.reshape(element_count, 8, 3, basis_modes)
    grad_basis = jnp.einsum(
        "ak,eacm->ekcm",
        grads.astype(jnp.bfloat16),
        corner_nodes,
        preferred_element_type=jnp.float32,
    )
    moved = displacement.reshape(8, 3, element_count)
    hgrad = jnp.einsum("ak,ace->kce", grads, moved, precision=lax.Precision.HIGHEST)
    volume = hgrad[0, 0] + hgrad[1, 1] + hgrad[2, 2]
    stiff = 1.0 + stiffening_power * volume**2 - 2.0 / 3.0
    press = volume + stiffening_power * volume**3 / 3.0 - 2.0 / 3.0 * volume
    eye = jnp.eye(3, dtype=jnp.float32)
    stress = hgrad + jnp.transpose(hgrad, (1, 0, 2)) + press[None, None, :] * eye[:, :, None]
    force_vector = (
        jnp.einsum("ak,kce->ace", grads, stress, precision=lax.Precision.HIGHEST).reshape(
            24, element_count
        )
        + 0.25 * displacement
    )
    sym = grad_basis + jnp.transpose(grad_basis, (0, 2, 1, 3))
    trace_basis = grad_basis[:, 0, 0] + grad_basis[:, 1, 1] + grad_basis[:, 2, 2]
    mode_image = jnp.einsum("ak,ekcm->eacm", grads, sym, precision=lax.Precision.HIGHEST)
    mode_image = (
        mode_image
        + stiff[:, None, None, None] * grads[None, :, :, None] * trace_basis[:, None, None, :]
        + 0.25 * corner_nodes.astype(jnp.float32)
    )
    return (mode_image.reshape(element_count, 24, basis_modes), force_vector)


def local(basis, send_rows, elem_slot, set_size, elem_weight, element_stiffening, state, load):
    nodes = basis.shape[0]
    basis_modes = basis.shape[2]
    n_elem = lax.psum(1, "elem")
    n_blk = lax.psum(1, "blk")
    flat = basis.reshape(nodes, 3 * basis_modes)
    outgoing = jnp.take(flat, send_rows[0, 0], axis=0)
    arrived = lax.all_to_all(outgoing, "elem", split_axis=0, concat_axis=0, tiled=True)
    element_count = elem_slot.shape[1]
    chosen_elements = jnp.take(arrived, elem_slot.T.reshape(-1), axis=0)
    basis_matrix = chosen_elements.reshape(element_count, 24, basis_modes)
    set_index = lax.axis_index("elem")
    block_index = lax.axis_index("blk")
    live = lax.dynamic_index_in_dim(set_size, set_index, keepdims=False)
    position = block_index * element_count + jnp.arange(element_count, dtype=jnp.int32)
    weights = jnp.where(position < live, elem_weight, jnp.zeros_like(elem_weight))
    displacement = jnp.einsum("agd,d->ga", basis_matrix, state, preferred_element_type=jnp.float32)
    mode_image, force_vector = element_contributions(basis_matrix, displacement, element_stiffening)
    weighted_image = (weights[:, None, None] * mode_image).astype(jnp.bfloat16)
    weighted_force = (force_vector * weights[None, :]).astype(jnp.bfloat16)
    rows = basis_modes // n_elem
    cols = basis_modes // n_blk
    tangent = lax.dot_general(
        basis_matrix,
        weighted_image,
        (((0, 1), (0, 1)), ((), ())),
        preferred_element_type=jnp.float32,
    )
    force_all = lax.dot_general(
        basis_matrix,
        weighted_force,
        (((0, 1), (1, 0)), ((), ())),
        preferred_element_type=jnp.float32,
    )
    pad = jnp.zeros((7, basis_modes), jnp.float32)
    stacked = jnp.concatenate([tangent, force_all[None, :], pad], axis=0)
    parts = lax.all_to_all(stacked, "blk", split_axis=1, concat_axis=0, tiled=True)
    halfway = jnp.sum(parts.reshape(n_blk, basis_modes + 8, cols), axis=0)
    force_cols = halfway[basis_modes]
    tangent_rows = halfway[:basis_modes].reshape(n_elem, rows, cols)
    chunks = jnp.concatenate(
        [tangent_rows, jnp.broadcast_to(force_cols[None, None, :], (n_elem, 1, cols))], axis=1
    )
    arrived_chunks = lax.all_to_all(chunks, "elem", split_axis=0, concat_axis=0, tiled=True)
    mine = jnp.sum(arrived_chunks, axis=0)
    scale = lax.rsqrt(24.0 * jnp.sum(set_size).astype(jnp.float32))
    return (mine[:rows] * scale, mine[rows] * scale - load)


def solution(mesh):
    in_specs = (
        P("elem", None, None),
        P("elem", "blk", None),
        P(None, ("elem", "blk")),
        P(),
        P(("elem", "blk")),
        P(("elem", "blk")),
        P(),
        P("blk"),
    )
    out_specs = (P("elem", "blk"), P("blk"))
    return jax.shard_map(local, mesh=mesh, in_specs=in_specs, out_specs=out_specs, check_vma=False)
```

```python
import jax
import jax.numpy as jnp
from jax import lax
from jax.experimental import pallas as pl
from jax.experimental.pallas import tpu as pltpu
from jax.sharding import PartitionSpec as P

G = [[(2 * ((a >> k) & 1) - 1) * 0.25 for k in range(3)] for a in range(8)]


def element_body(arrived_ref, slot_ref, state_ref, omega_ref, stiff_ref, out_ref, v_ref, w_ref):
    n_el = slot_ref.shape[0]
    n_slot = arrived_ref.shape[1]
    modes = arrived_ref.shape[2]
    lane = lax.broadcasted_iota(jnp.int32, (n_el, n_slot), 1)
    state_pad = state_ref[...]
    disp = {}
    for a in range(8):
        onehot = (slot_ref[:, a:a + 1] == lane).astype(jnp.bfloat16)
        for c in range(3):
            va = jnp.dot(onehot, arrived_ref[c], preferred_element_type=jnp.float32).astype(jnp.bfloat16)
            v_ref[pl.ds((3 * a + c) * n_el, n_el), :] = va
            disp[a, c] = jnp.dot(va, state_pad, preferred_element_type=jnp.float32)[:, 0:1]
    h = {}
    for k in range(3):
        for c in range(3):
            acc = G[0][k] * disp[0, c]
            for a in range(1, 8):
                acc = acc + G[a][k] * disp[a, c]
            h[k, c] = acc
    stiff = stiff_ref[...]
    omega = omega_ref[...]
    vol = h[0, 0] + h[1, 1] + h[2, 2]
    lam = 1.0 + stiff * vol ** 2 - 2.0 / 3.0
    press = vol + stiff * vol ** 3 / 3.0 - 2.0 / 3.0 * vol
    stress = {}
    for k in range(3):
        for c in range(3):
            s = h[k, c] + h[c, k]
            if k == c:
                s = s + press
            stress[k, c] = s
    force_acc = jnp.zeros((n_el, modes), jnp.float32)
    for a in range(8):
        for c in range(3):
            f = G[a][0] * stress[0, c] + G[a][1] * stress[1, c] + G[a][2] * stress[2, c]
            f = f + 0.25 * disp[a, c]
            wf = (f * omega).astype(jnp.bfloat16).astype(jnp.float32)
            force_acc = force_acc + v_ref[pl.ds((3 * a + c) * n_el, n_el), :].astype(jnp.float32) * wf
    grad = {}
    for k in range(3):
        for c in range(3):
            acc = None
            for a in range(8):
                term = G[a][k] * v_ref[pl.ds((3 * a + c) * n_el, n_el), :].astype(jnp.float32)
                acc = term if acc is None else acc + term
            grad[k, c] = acc
    trace = grad[0, 0] + grad[1, 1] + grad[2, 2]
    for a in range(8):
        for c in range(3):
            img = G[a][0] * (grad[0, c] + grad[c, 0])
            img = img + G[a][1] * (grad[1, c] + grad[c, 1])
            img = img + G[a][2] * (grad[2, c] + grad[c, 2])
            img = img + (lam * G[a][c]) * trace
            img = img + 0.25 * v_ref[pl.ds((3 * a + c) * n_el, n_el), :].astype(jnp.float32)
            w_ref[pl.ds((3 * a + c) * n_el, n_el), :] = (omega * img).astype(jnp.bfloat16)
    tangent = lax.dot_general(
        v_ref[...], w_ref[...], (((0,), (0,)), ((), ())), preferred_element_type=jnp.float32
    )
    out_ref[pl.ds(0, modes), :] = tangent
    force_row = jnp.sum(force_acc, axis=0, keepdims=True)
    out_ref[pl.ds(modes, 8), :] = jnp.concatenate(
        [force_row, jnp.zeros((7, modes), jnp.float32)], axis=0
    )


def element_stage(arrived3, slot_t, state, omega, stiff):
    n_el = slot_t.shape[0]
    modes = arrived3.shape[2]
    state_pad = jnp.zeros((modes, 128), jnp.bfloat16).at[:, 0].set(state)
    vmem = pltpu.MemorySpace.VMEM if hasattr(pltpu, "MemorySpace") else pltpu.TPUMemorySpace.VMEM
    return pl.pallas_call(
        element_body,
        out_shape=jax.ShapeDtypeStruct((modes + 8, modes), jnp.float32),
        in_specs=[pl.BlockSpec(memory_space=vmem)] * 5,
        out_specs=pl.BlockSpec(memory_space=vmem),
        scratch_shapes=[
            pltpu.VMEM((24 * n_el, modes), jnp.bfloat16),
            pltpu.VMEM((24 * n_el, modes), jnp.bfloat16),
        ],
    )(arrived3, slot_t, state_pad, omega.reshape(n_el, 1), stiff.reshape(n_el, 1))


def local(basis, send_rows, elem_slot, set_size, elem_weight, element_stiffening, state, load):
    basis_modes = basis.shape[2]
    n_elem = lax.psum(1, "elem")
    n_blk = lax.psum(1, "blk")
    by_component = jnp.transpose(basis, (1, 0, 2))
    outgoing = jnp.take(by_component, send_rows[0, 0], axis=1)
    arrived = lax.all_to_all(outgoing, "elem", split_axis=1, concat_axis=1, tiled=True)
    element_count = elem_slot.shape[1]
    set_index = lax.axis_index("elem")
    block_index = lax.axis_index("blk")
    live = lax.dynamic_index_in_dim(set_size, set_index, keepdims=False)
    position = block_index * element_count + jnp.arange(element_count, dtype=jnp.int32)
    weights = jnp.where(position < live, elem_weight, jnp.zeros_like(elem_weight))
    stacked = element_stage(arrived, elem_slot.T, state, weights, element_stiffening)
    rows = basis_modes // n_elem
    cols = basis_modes // n_blk
    parts = lax.all_to_all(stacked, "blk", split_axis=1, concat_axis=0, tiled=True)
    halfway = jnp.sum(parts.reshape(n_blk, basis_modes + 8, cols), axis=0)
    force_cols = halfway[basis_modes]
    tangent_rows = halfway[:basis_modes].reshape(n_elem, rows, cols)
    chunks = jnp.concatenate(
        [tangent_rows, jnp.broadcast_to(force_cols[None, None, :], (n_elem, 1, cols))], axis=1
    )
    arrived_chunks = lax.all_to_all(chunks, "elem", split_axis=0, concat_axis=0, tiled=True)
    mine = jnp.sum(arrived_chunks, axis=0)
    scale = lax.rsqrt(24.0 * jnp.sum(set_size).astype(jnp.float32))
    return (mine[:rows] * scale, mine[rows] * scale - load)


def solution(mesh):
    in_specs = (
        P("elem", None, None),
        P("elem", "blk", None),
        P(None, ("elem", "blk")),
        P(),
        P(("elem", "blk")),
        P(("elem", "blk")),
        P(),
        P("blk"),
    )
    out_specs = (P("elem", "blk"), P("blk"))
    return jax.shard_map(local, mesh=mesh, in_specs=in_specs, out_specs=out_specs, check_vma=False)
```

```python
import jax
import jax.numpy as jnp
from jax import lax
from jax.experimental import pallas as pl
from jax.experimental.pallas import tpu as pltpu
from jax.sharding import PartitionSpec as P

G = [[(2 * ((a >> k) & 1) - 1) * 0.25 for k in range(3)] for a in range(8)]


def element_body(arrived_ref, slot_ref, state_ref, omega_ref, stiff_ref, out_ref, v_ref, w_ref):
    n_el = slot_ref.shape[0]
    n_slot = arrived_ref.shape[1]
    modes = arrived_ref.shape[2]
    lane = lax.broadcasted_iota(jnp.int32, (n_el, n_slot), 1)
    state_pad = state_ref[...]
    disp = {}
    for a in range(8):
        onehot = (slot_ref[:, a:a + 1] == lane).astype(jnp.bfloat16)
        for c in range(3):
            va = jnp.dot(onehot, arrived_ref[c], preferred_element_type=jnp.float32).astype(jnp.bfloat16)
            v_ref[pl.ds((3 * a + c) * n_el, n_el), :] = va
            disp[a, c] = jnp.dot(va, state_pad, preferred_element_type=jnp.float32)[:, 0:1]
    h = {}
    for k in range(3):
        for c in range(3):
            acc = G[0][k] * disp[0, c]
            for a in range(1, 8):
                acc = acc + G[a][k] * disp[a, c]
            h[k, c] = acc
    stiff = stiff_ref[...]
    omega = omega_ref[...]
    vol = h[0, 0] + h[1, 1] + h[2, 2]
    lam = 1.0 + stiff * vol ** 2 - 2.0 / 3.0
    press = vol + stiff * vol ** 3 / 3.0 - 2.0 / 3.0 * vol
    stress = {}
    for k in range(3):
        for c in range(3):
            s = h[k, c] + h[c, k]
            if k == c:
                s = s + press
            stress[k, c] = s
    force_acc = jnp.zeros((n_el, modes), jnp.float32)
    for a in range(8):
        for c in range(3):
            f = G[a][0] * stress[0, c] + G[a][1] * stress[1, c] + G[a][2] * stress[2, c]
            f = f + 0.25 * disp[a, c]
            wf = (f * omega).astype(jnp.bfloat16).astype(jnp.float32)
            force_acc = force_acc + v_ref[pl.ds((3 * a + c) * n_el, n_el), :].astype(jnp.float32) * wf
    grad = {}
    for k in range(3):
        for c in range(3):
            acc = None
            for a in range(8):
                term = G[a][k] * v_ref[pl.ds((3 * a + c) * n_el, n_el), :].astype(jnp.float32)
                acc = term if acc is None else acc + term
            grad[k, c] = acc
    trace = grad[0, 0] + grad[1, 1] + grad[2, 2]
    for a in range(8):
        for c in range(3):
            img = G[a][0] * (grad[0, c] + grad[c, 0])
            img = img + G[a][1] * (grad[1, c] + grad[c, 1])
            img = img + G[a][2] * (grad[2, c] + grad[c, 2])
            img = img + (lam * G[a][c]) * trace
            img = img + 0.25 * v_ref[pl.ds((3 * a + c) * n_el, n_el), :].astype(jnp.float32)
            w_ref[pl.ds((3 * a + c) * n_el, n_el), :] = (omega * img).astype(jnp.bfloat16)
    tangent = lax.dot_general(
        v_ref[...], w_ref[...], (((0,), (0,)), ((), ())), preferred_element_type=jnp.float32
    )
    out_ref[pl.ds(0, modes), :] = tangent
    force_row = jnp.sum(force_acc, axis=0, keepdims=True)
    out_ref[pl.ds(modes, 8), :] = jnp.concatenate(
        [force_row, jnp.zeros((7, modes), jnp.float32)], axis=0
    )


def element_stage(arrived3, slot_t, state, omega, stiff):
    n_el = slot_t.shape[0]
    modes = arrived3.shape[2]
    state_pad = jnp.zeros((modes, 128), jnp.bfloat16).at[:, 0].set(state)
    vmem = pltpu.MemorySpace.VMEM if hasattr(pltpu, "MemorySpace") else pltpu.TPUMemorySpace.VMEM
    return pl.pallas_call(
        element_body,
        out_shape=jax.ShapeDtypeStruct((modes + 8, modes), jnp.float32),
        in_specs=[pl.BlockSpec(memory_space=vmem)] * 5,
        out_specs=pl.BlockSpec(memory_space=vmem),
        scratch_shapes=[
            pltpu.VMEM((24 * n_el, modes), jnp.bfloat16),
            pltpu.VMEM((24 * n_el, modes), jnp.bfloat16),
        ],
    )(arrived3, slot_t, state_pad, omega.reshape(n_el, 1), stiff.reshape(n_el, 1))


def local(basis, send_rows, elem_slot, set_size, elem_weight, element_stiffening, state, load):
    basis_modes = basis.shape[2]
    n_elem = lax.psum(1, "elem")
    n_blk = lax.psum(1, "blk")
    by_component = jnp.transpose(basis, (1, 0, 2))
    outgoing = jnp.take(by_component, send_rows[0, 0], axis=1)
    arrived = lax.all_to_all(outgoing, "elem", split_axis=1, concat_axis=1, tiled=True)
    element_count = elem_slot.shape[1]
    set_index = lax.axis_index("elem")
    block_index = lax.axis_index("blk")
    live = lax.dynamic_index_in_dim(set_size, set_index, keepdims=False)
    position = block_index * element_count + jnp.arange(element_count, dtype=jnp.int32)
    weights = jnp.where(position < live, elem_weight, jnp.zeros_like(elem_weight))
    stacked = element_stage(arrived, elem_slot.T, state, weights, element_stiffening)
    rows = basis_modes // n_elem
    cols = basis_modes // n_blk
    n_y = n_blk // 2
    core = block_index % 2
    chip = block_index // 2
    by_dest = stacked.reshape(basis_modes + 8, n_y, 2, cols)
    pair = [(b, b ^ 1) for b in range(n_blk)]
    sent = lax.dynamic_index_in_dim(by_dest, 1 - core, axis=2, keepdims=False)
    kept = lax.dynamic_index_in_dim(by_dest, core, axis=2, keepdims=False)
    chip_sum = kept + lax.ppermute(sent, "blk", pair)
    halfway = lax.dynamic_index_in_dim(chip_sum, chip, axis=1, keepdims=False)
    for shift in range(1, n_y):
        ring = [(2 * y + c, 2 * ((y + shift) % n_y) + c) for y in range(n_y) for c in range(2)]
        piece = lax.dynamic_index_in_dim(chip_sum, (chip + shift) % n_y, axis=1, keepdims=False)
        halfway = halfway + lax.ppermute(piece, "blk", ring)
    force_cols = halfway[basis_modes]
    tangent_rows = halfway[:basis_modes].reshape(n_elem, rows, cols)
    chunks = jnp.concatenate(
        [tangent_rows, jnp.broadcast_to(force_cols[None, None, :], (n_elem, 1, cols))], axis=1
    )
    arrived_chunks = lax.all_to_all(chunks, "elem", split_axis=0, concat_axis=0, tiled=True)
    mine = jnp.sum(arrived_chunks, axis=0)
    scale = lax.rsqrt(24.0 * jnp.sum(set_size).astype(jnp.float32))
    return (mine[:rows] * scale, mine[rows] * scale - load)


def solution(mesh):
    in_specs = (
        P("elem", None, None),
        P("elem", "blk", None),
        P(None, ("elem", "blk")),
        P(),
        P(("elem", "blk")),
        P(("elem", "blk")),
        P(),
        P("blk"),
    )
    out_specs = (P("elem", "blk"), P("blk"))
    return jax.shard_map(local, mesh=mesh, in_specs=in_specs, out_specs=out_specs, check_vma=False)
```

```python
import jax
import jax.numpy as jnp
from jax import lax
from jax.experimental import pallas as pl
from jax.experimental.pallas import tpu as pltpu
from jax.sharding import PartitionSpec as P

G = [[(2 * ((a >> k) & 1) - 1) * 0.25 for k in range(3)] for a in range(8)]


def element_body(arrived_ref, slot_ref, state_ref, omega_ref, stiff_ref, out_ref, v_ref, w_ref):
    n_el = slot_ref.shape[0]
    n_slot = arrived_ref.shape[0]
    modes = out_ref.shape[1]
    lane = lax.broadcasted_iota(jnp.int32, (n_el, n_slot), 1)
    state_pad = state_ref[...]
    disp = {}
    for a in range(8):
        onehot = (slot_ref[:, a:a + 1] == lane).astype(jnp.bfloat16)
        corner = jnp.dot(onehot, arrived_ref[...], preferred_element_type=jnp.float32).astype(jnp.bfloat16)
        for c in range(3):
            va = corner[:, c * modes:(c + 1) * modes]
            v_ref[pl.ds((3 * a + c) * n_el, n_el), :] = va
            disp[a, c] = jnp.dot(va, state_pad, preferred_element_type=jnp.float32)[:, 0:1]
    h = {}
    for k in range(3):
        for c in range(3):
            acc = G[0][k] * disp[0, c]
            for a in range(1, 8):
                acc = acc + G[a][k] * disp[a, c]
            h[k, c] = acc
    stiff = stiff_ref[...]
    omega = omega_ref[...]
    vol = h[0, 0] + h[1, 1] + h[2, 2]
    lam = 1.0 + stiff * vol ** 2 - 2.0 / 3.0
    press = vol + stiff * vol ** 3 / 3.0 - 2.0 / 3.0 * vol
    stress = {}
    for k in range(3):
        for c in range(3):
            s = h[k, c] + h[c, k]
            if k == c:
                s = s + press
            stress[k, c] = s
    force_acc = jnp.zeros((n_el, modes), jnp.float32)
    for a in range(8):
        for c in range(3):
            f = G[a][0] * stress[0, c] + G[a][1] * stress[1, c] + G[a][2] * stress[2, c]
            f = f + 0.25 * disp[a, c]
            wf = (f * omega).astype(jnp.bfloat16).astype(jnp.float32)
            force_acc = force_acc + v_ref[pl.ds((3 * a + c) * n_el, n_el), :].astype(jnp.float32) * wf
    grad = {}
    for k in range(3):
        for c in range(3):
            acc = None
            for a in range(8):
                term = G[a][k] * v_ref[pl.ds((3 * a + c) * n_el, n_el), :].astype(jnp.float32)
                acc = term if acc is None else acc + term
            grad[k, c] = acc
    trace = grad[0, 0] + grad[1, 1] + grad[2, 2]
    for a in range(8):
        for c in range(3):
            img = G[a][0] * (grad[0, c] + grad[c, 0])
            img = img + G[a][1] * (grad[1, c] + grad[c, 1])
            img = img + G[a][2] * (grad[2, c] + grad[c, 2])
            img = img + (lam * G[a][c]) * trace
            img = img + 0.25 * v_ref[pl.ds((3 * a + c) * n_el, n_el), :].astype(jnp.float32)
            w_ref[pl.ds((3 * a + c) * n_el, n_el), :] = (omega * img).astype(jnp.bfloat16)
    tangent = lax.dot_general(
        v_ref[...], w_ref[...], (((0,), (0,)), ((), ())), preferred_element_type=jnp.float32
    )
    out_ref[pl.ds(0, modes), :] = tangent
    force_row = jnp.sum(force_acc, axis=0, keepdims=True)
    out_ref[pl.ds(modes, 8), :] = jnp.concatenate(
        [force_row, jnp.zeros((7, modes), jnp.float32)], axis=0
    )


def element_stage(arrived3, slot_t, state, omega, stiff):
    n_el = slot_t.shape[0]
    modes = arrived3.shape[1] // 3
    state_pad = jnp.zeros((modes, 128), jnp.bfloat16).at[:, 0].set(state)
    vmem = pltpu.MemorySpace.VMEM if hasattr(pltpu, "MemorySpace") else pltpu.TPUMemorySpace.VMEM
    return pl.pallas_call(
        element_body,
        out_shape=jax.ShapeDtypeStruct((modes + 8, modes), jnp.float32),
        in_specs=[pl.BlockSpec(memory_space=vmem)] * 5,
        out_specs=pl.BlockSpec(memory_space=vmem),
        scratch_shapes=[
            pltpu.VMEM((24 * n_el, modes), jnp.bfloat16),
            pltpu.VMEM((24 * n_el, modes), jnp.bfloat16),
        ],
    )(arrived3, slot_t, state_pad, omega.reshape(n_el, 1), stiff.reshape(n_el, 1))


def gather_body(basis_ref, rows_ref, out_ref):
    n_rows = rows_ref.shape[0]
    nodes = basis_ref.shape[1]
    modes = basis_ref.shape[2]
    lane = lax.broadcasted_iota(jnp.int32, (n_rows, nodes), 1)
    onehot = (rows_ref[...] == lane).astype(jnp.bfloat16)
    for c in range(basis_ref.shape[0]):
        picked = jnp.dot(onehot, basis_ref[c], preferred_element_type=jnp.float32)
        out_ref[:, pl.ds(c * modes, modes)] = picked.astype(jnp.bfloat16)


def gather_rows(by_component, rows):
    comps, nodes, modes = by_component.shape
    n_rows = rows.shape[0]
    vmem = pltpu.MemorySpace.VMEM if hasattr(pltpu, "MemorySpace") else pltpu.TPUMemorySpace.VMEM
    return pl.pallas_call(
        gather_body,
        out_shape=jax.ShapeDtypeStruct((n_rows, comps * modes), jnp.bfloat16),
        in_specs=[pl.BlockSpec(memory_space=vmem)] * 2,
        out_specs=pl.BlockSpec(memory_space=vmem),
    )(by_component, rows.reshape(n_rows, 1))


def local(basis, send_rows, elem_slot, set_size, elem_weight, element_stiffening, state, load):
    basis_modes = basis.shape[2]
    n_elem = lax.psum(1, "elem")
    n_blk = lax.psum(1, "blk")
    by_component = jnp.transpose(basis, (1, 0, 2))
    outgoing = gather_rows(by_component, send_rows[0, 0])
    arrived = lax.all_to_all(outgoing, "elem", split_axis=0, concat_axis=0, tiled=True)
    element_count = elem_slot.shape[1]
    set_index = lax.axis_index("elem")
    block_index = lax.axis_index("blk")
    live = lax.dynamic_index_in_dim(set_size, set_index, keepdims=False)
    position = block_index * element_count + jnp.arange(element_count, dtype=jnp.int32)
    weights = jnp.where(position < live, elem_weight, jnp.zeros_like(elem_weight))
    stacked = element_stage(arrived, elem_slot.T, state, weights, element_stiffening)
    rows = basis_modes // n_elem
    cols = basis_modes // n_blk
    n_y = n_blk // 2
    core = block_index % 2
    chip = block_index // 2
    by_dest = stacked.reshape(basis_modes + 8, n_y, 2, cols)
    pair = [(b, b ^ 1) for b in range(n_blk)]
    sent = lax.dynamic_index_in_dim(by_dest, 1 - core, axis=2, keepdims=False)
    kept = lax.dynamic_index_in_dim(by_dest, core, axis=2, keepdims=False)
    chip_sum = kept + lax.ppermute(sent, "blk", pair)
    halfway = lax.dynamic_index_in_dim(chip_sum, chip, axis=1, keepdims=False)
    for shift in range(1, n_y):
        ring = [(2 * y + c, 2 * ((y + shift) % n_y) + c) for y in range(n_y) for c in range(2)]
        piece = lax.dynamic_index_in_dim(chip_sum, (chip + shift) % n_y, axis=1, keepdims=False)
        halfway = halfway + lax.ppermute(piece, "blk", ring)
    force_cols = halfway[basis_modes]
    tangent_rows = halfway[:basis_modes].reshape(n_elem, rows, cols)
    chunks = jnp.concatenate(
        [tangent_rows, jnp.broadcast_to(force_cols[None, None, :], (n_elem, 1, cols))], axis=1
    )
    arrived_chunks = lax.all_to_all(chunks, "elem", split_axis=0, concat_axis=0, tiled=True)
    mine = jnp.sum(arrived_chunks, axis=0)
    scale = lax.rsqrt(24.0 * jnp.sum(set_size).astype(jnp.float32))
    return (mine[:rows] * scale, mine[rows] * scale - load)


def solution(mesh):
    in_specs = (
        P("elem", None, None),
        P("elem", "blk", None),
        P(None, ("elem", "blk")),
        P(),
        P(("elem", "blk")),
        P(("elem", "blk")),
        P(),
        P("blk"),
    )
    out_specs = (P("elem", "blk"), P("blk"))
    return jax.shard_map(local, mesh=mesh, in_specs=in_specs, out_specs=out_specs, check_vma=False)
```

```python
import jax
import jax.numpy as jnp
from jax import lax
from jax.experimental import pallas as pl
from jax.experimental.pallas import tpu as pltpu
from jax.sharding import PartitionSpec as P

G = [[(2 * ((a >> k) & 1) - 1) * 0.25 for k in range(3)] for a in range(8)]


def element_body(arrived_ref, slot_ref, state_ref, omega_ref, stiff_ref, out_ref, v_ref, w_ref):
    n_el = slot_ref.shape[0]
    n_slot = arrived_ref.shape[0]
    modes = out_ref.shape[1]
    lane = lax.broadcasted_iota(jnp.int32, (n_el, n_slot), 1)
    state_pad = state_ref[...]
    disp = {}
    for a in range(8):
        onehot = (slot_ref[:, a:a + 1] == lane).astype(jnp.bfloat16)
        corner = jnp.dot(onehot, arrived_ref[...], preferred_element_type=jnp.float32).astype(jnp.bfloat16)
        for c in range(3):
            va = corner[:, c * modes:(c + 1) * modes]
            v_ref[pl.ds((3 * a + c) * n_el, n_el), :] = va
            disp[a, c] = jnp.dot(va, state_pad, preferred_element_type=jnp.float32)[:, 0:1]
    h = {}
    for k in range(3):
        for c in range(3):
            acc = G[0][k] * disp[0, c]
            for a in range(1, 8):
                acc = acc + G[a][k] * disp[a, c]
            h[k, c] = acc
    stiff = stiff_ref[...]
    omega = omega_ref[...]
    vol = h[0, 0] + h[1, 1] + h[2, 2]
    lam = 1.0 + stiff * vol ** 2 - 2.0 / 3.0
    press = vol + stiff * vol ** 3 / 3.0 - 2.0 / 3.0 * vol
    stress = {}
    for k in range(3):
        for c in range(3):
            s = h[k, c] + h[c, k]
            if k == c:
                s = s + press
            stress[k, c] = s
    force_acc = jnp.zeros((n_el, modes), jnp.float32)
    for a in range(8):
        for c in range(3):
            f = G[a][0] * stress[0, c] + G[a][1] * stress[1, c] + G[a][2] * stress[2, c]
            f = f + 0.25 * disp[a, c]
            wf = (f * omega).astype(jnp.bfloat16).astype(jnp.float32)
            force_acc = force_acc + v_ref[pl.ds((3 * a + c) * n_el, n_el), :].astype(jnp.float32) * wf
    grad = {}
    for k in range(3):
        for c in range(3):
            acc = None
            for a in range(8):
                term = G[a][k] * v_ref[pl.ds((3 * a + c) * n_el, n_el), :].astype(jnp.float32)
                acc = term if acc is None else acc + term
            grad[k, c] = acc
    trace = grad[0, 0] + grad[1, 1] + grad[2, 2]
    for a in range(8):
        for c in range(3):
            img = G[a][0] * (grad[0, c] + grad[c, 0])
            img = img + G[a][1] * (grad[1, c] + grad[c, 1])
            img = img + G[a][2] * (grad[2, c] + grad[c, 2])
            img = img + (lam * G[a][c]) * trace
            img = img + 0.25 * v_ref[pl.ds((3 * a + c) * n_el, n_el), :].astype(jnp.float32)
            w_ref[pl.ds((3 * a + c) * n_el, n_el), :] = (omega * img).astype(jnp.bfloat16)
    tangent = lax.dot_general(
        v_ref[...], w_ref[...], (((0,), (0,)), ((), ())), preferred_element_type=jnp.float32
    )
    out_ref[pl.ds(0, modes), :] = tangent
    force_row = jnp.sum(force_acc, axis=0, keepdims=True)
    out_ref[pl.ds(modes, 8), :] = jnp.concatenate(
        [force_row, jnp.zeros((7, modes), jnp.float32)], axis=0
    )


def element_stage(arrived3, slot_t, state, omega, stiff):
    n_el = slot_t.shape[0]
    modes = arrived3.shape[1] // 3
    state_pad = jnp.zeros((modes, 128), jnp.bfloat16).at[:, 0].set(state)
    vmem = pltpu.MemorySpace.VMEM if hasattr(pltpu, "MemorySpace") else pltpu.TPUMemorySpace.VMEM
    return pl.pallas_call(
        element_body,
        out_shape=jax.ShapeDtypeStruct((modes + 8, modes), jnp.float32),
        in_specs=[pl.BlockSpec(memory_space=vmem)] * 5,
        out_specs=pl.BlockSpec(memory_space=vmem),
        scratch_shapes=[
            pltpu.VMEM((24 * n_el, modes), jnp.bfloat16),
            pltpu.VMEM((24 * n_el, modes), jnp.bfloat16),
        ],
    )(arrived3, slot_t, state_pad, omega.reshape(n_el, 1), stiff.reshape(n_el, 1))


def gather_body(basis_ref, rows_ref, out_ref):
    nodes = basis_ref.shape[1]
    n_rows = rows_ref.shape[1]
    node = lax.broadcasted_iota(jnp.int32, (nodes, n_rows), 0)
    onehot_t = (node == rows_ref[...]).astype(jnp.bfloat16)
    picked = lax.dot_general(
        onehot_t, basis_ref[0], (((0,), (0,)), ((), ())), preferred_element_type=jnp.float32
    )
    out_ref[...] = picked.astype(jnp.bfloat16)


def gather_rows(by_component, rows):
    comps, nodes, modes = by_component.shape
    n_rows = rows.shape[0]
    return pl.pallas_call(
        gather_body,
        out_shape=jax.ShapeDtypeStruct((n_rows, comps * modes), jnp.bfloat16),
        grid=(comps,),
        in_specs=[
            pl.BlockSpec((1, nodes, modes), lambda c: (c, 0, 0)),
            pl.BlockSpec((1, n_rows), lambda c: (0, 0)),
        ],
        out_specs=pl.BlockSpec((n_rows, modes), lambda c: (0, c)),
    )(by_component, rows.reshape(1, n_rows))

def local(basis, send_rows, elem_slot, set_size, elem_weight, element_stiffening, state, load):
    basis_modes = basis.shape[2]
    n_elem = lax.psum(1, "elem")
    n_blk = lax.psum(1, "blk")
    by_component = jnp.transpose(basis, (1, 0, 2))
    outgoing = gather_rows(by_component, send_rows[0, 0])
    arrived = lax.all_to_all(outgoing, "elem", split_axis=0, concat_axis=0, tiled=True)
    element_count = elem_slot.shape[1]
    set_index = lax.axis_index("elem")
    block_index = lax.axis_index("blk")
    live = lax.dynamic_index_in_dim(set_size, set_index, keepdims=False)
    position = block_index * element_count + jnp.arange(element_count, dtype=jnp.int32)
    weights = jnp.where(position < live, elem_weight, jnp.zeros_like(elem_weight))
    stacked = element_stage(arrived, elem_slot.T, state, weights, element_stiffening)
    rows = basis_modes // n_elem
    cols = basis_modes // n_blk
    n_y = n_blk // 2
    core = block_index % 2
    chip = block_index // 2
    by_dest = stacked.reshape(basis_modes + 8, n_y, 2, cols)
    pair = [(b, b ^ 1) for b in range(n_blk)]
    sent = lax.dynamic_index_in_dim(by_dest, 1 - core, axis=2, keepdims=False)
    kept = lax.dynamic_index_in_dim(by_dest, core, axis=2, keepdims=False)
    chip_sum = kept + lax.ppermute(sent, "blk", pair)
    halfway = lax.dynamic_index_in_dim(chip_sum, chip, axis=1, keepdims=False)
    for shift in range(1, n_y):
        ring = [(2 * y + c, 2 * ((y + shift) % n_y) + c) for y in range(n_y) for c in range(2)]
        piece = lax.dynamic_index_in_dim(chip_sum, (chip + shift) % n_y, axis=1, keepdims=False)
        halfway = halfway + lax.ppermute(piece, "blk", ring)
    force_cols = halfway[basis_modes]
    tangent_rows = halfway[:basis_modes].reshape(n_elem, rows, cols)
    chunks = jnp.concatenate(
        [tangent_rows, jnp.broadcast_to(force_cols[None, None, :], (n_elem, 1, cols))], axis=1
    )
    arrived_chunks = lax.all_to_all(chunks, "elem", split_axis=0, concat_axis=0, tiled=True)
    mine = jnp.sum(arrived_chunks, axis=0)
    scale = lax.rsqrt(24.0 * jnp.sum(set_size).astype(jnp.float32))
    return (mine[:rows] * scale, mine[rows] * scale - load)


def solution(mesh):
    in_specs = (
        P("elem", None, None),
        P("elem", "blk", None),
        P(None, ("elem", "blk")),
        P(),
        P(("elem", "blk")),
        P(("elem", "blk")),
        P(),
        P("blk"),
    )
    out_specs = (P("elem", "blk"), P("blk"))
    return jax.shard_map(local, mesh=mesh, in_specs=in_specs, out_specs=out_specs, check_vma=False)
```

```python
import jax
import jax.numpy as jnp
from jax import lax
from jax.experimental import pallas as pl
from jax.experimental.pallas import tpu as pltpu
from jax.sharding import PartitionSpec as P

G = [[(2 * ((a >> k) & 1) - 1) * 0.25 for k in range(3)] for a in range(8)]


def element_body(arrived_ref, slot_ref, state_ref, omega_ref, stiff_ref, out_ref, v_ref, w_ref):
    n_el = slot_ref.shape[0]
    n_slot = arrived_ref.shape[0]
    modes = out_ref.shape[1]
    lane = lax.broadcasted_iota(jnp.int32, (n_el, n_slot), 1)
    state_pad = state_ref[...]
    disp = {}
    for a in range(8):
        onehot = (slot_ref[:, a:a + 1] == lane).astype(jnp.bfloat16)
        corner = jnp.dot(onehot, arrived_ref[...], preferred_element_type=jnp.float32).astype(jnp.bfloat16)
        for c in range(3):
            va = corner[:, c * modes:(c + 1) * modes]
            v_ref[pl.ds((3 * a + c) * n_el, n_el), :] = va
            disp[a, c] = jnp.dot(va, state_pad, preferred_element_type=jnp.float32)[:, 0:1]
    h = {}
    for k in range(3):
        for c in range(3):
            acc = G[0][k] * disp[0, c]
            for a in range(1, 8):
                acc = acc + G[a][k] * disp[a, c]
            h[k, c] = acc
    stiff = stiff_ref[...]
    omega = omega_ref[...]
    vol = h[0, 0] + h[1, 1] + h[2, 2]
    lam = 1.0 + stiff * vol ** 2 - 2.0 / 3.0
    press = vol + stiff * vol ** 3 / 3.0 - 2.0 / 3.0 * vol
    stress = {}
    for k in range(3):
        for c in range(3):
            s = h[k, c] + h[c, k]
            if k == c:
                s = s + press
            stress[k, c] = s
    force_acc = jnp.zeros((n_el, modes), jnp.float32)
    for a in range(8):
        for c in range(3):
            f = G[a][0] * stress[0, c] + G[a][1] * stress[1, c] + G[a][2] * stress[2, c]
            f = f + 0.25 * disp[a, c]
            wf = (f * omega).astype(jnp.bfloat16).astype(jnp.float32)
            force_acc = force_acc + v_ref[pl.ds((3 * a + c) * n_el, n_el), :].astype(jnp.float32) * wf
    grad = {}
    for k in range(3):
        for c in range(3):
            acc = None
            for a in range(8):
                term = G[a][k] * v_ref[pl.ds((3 * a + c) * n_el, n_el), :].astype(jnp.float32)
                acc = term if acc is None else acc + term
            grad[k, c] = acc
    trace = grad[0, 0] + grad[1, 1] + grad[2, 2]
    for a in range(8):
        for c in range(3):
            img = G[a][0] * (grad[0, c] + grad[c, 0])
            img = img + G[a][1] * (grad[1, c] + grad[c, 1])
            img = img + G[a][2] * (grad[2, c] + grad[c, 2])
            img = img + (lam * G[a][c]) * trace
            img = img + 0.25 * v_ref[pl.ds((3 * a + c) * n_el, n_el), :].astype(jnp.float32)
            w_ref[pl.ds((3 * a + c) * n_el, n_el), :] = (omega * img).astype(jnp.bfloat16)
    tangent = lax.dot_general(
        v_ref[...], w_ref[...], (((0,), (0,)), ((), ())), preferred_element_type=jnp.float32
    )
    out_ref[pl.ds(0, modes), :] = tangent
    force_row = jnp.sum(force_acc, axis=0, keepdims=True)
    out_ref[pl.ds(modes, 8), :] = jnp.concatenate(
        [force_row, jnp.zeros((7, modes), jnp.float32)], axis=0
    )


def element_stage(arrived3, slot_t, state, omega, stiff):
    n_el = slot_t.shape[0]
    modes = arrived3.shape[1] // 3
    state_pad = jnp.zeros((modes, 128), jnp.bfloat16).at[:, 0].set(state)
    vmem = pltpu.MemorySpace.VMEM if hasattr(pltpu, "MemorySpace") else pltpu.TPUMemorySpace.VMEM
    return pl.pallas_call(
        element_body,
        out_shape=jax.ShapeDtypeStruct((modes + 8, modes), jnp.float32),
        in_specs=[pl.BlockSpec(memory_space=vmem)] * 5,
        out_specs=pl.BlockSpec(memory_space=vmem),
        scratch_shapes=[
            pltpu.VMEM((24 * n_el, modes), jnp.bfloat16),
            pltpu.VMEM((24 * n_el, modes), jnp.bfloat16),
        ],
    )(arrived3, slot_t, state_pad, omega.reshape(n_el, 1), stiff.reshape(n_el, 1))


def gather_body(basis_ref, rows_ref, out_ref):
    nodes = basis_ref.shape[1]
    n_rows = rows_ref.shape[1]
    node = lax.broadcasted_iota(jnp.int32, (nodes, n_rows), 0)
    onehot_t = (node == rows_ref[...]).astype(jnp.bfloat16)
    picked = lax.dot_general(
        onehot_t, basis_ref[0], (((0,), (0,)), ((), ())), preferred_element_type=jnp.float32
    )
    out_ref[...] = picked.astype(jnp.bfloat16)


def gather_rows(by_component, rows):
    comps, nodes, modes = by_component.shape
    n_rows = rows.shape[0]
    return pl.pallas_call(
        gather_body,
        out_shape=jax.ShapeDtypeStruct((n_rows, comps * modes), jnp.bfloat16),
        grid=(comps,),
        in_specs=[
            pl.BlockSpec((1, nodes, modes), lambda c: (c, 0, 0)),
            pl.BlockSpec((1, n_rows), lambda c: (0, 0)),
        ],
        out_specs=pl.BlockSpec((n_rows, modes), lambda c: (0, c)),
    )(by_component, rows.reshape(1, n_rows))

def local(basis, send_rows, elem_slot, set_size, elem_weight, element_stiffening, state, load):
    basis_modes = basis.shape[2]
    n_elem = lax.psum(1, "elem")
    n_blk = lax.psum(1, "blk")
    by_component = jnp.transpose(basis, (1, 0, 2))
    outgoing = gather_rows(by_component, send_rows[0, 0])
    arrived = lax.all_to_all(outgoing, "elem", split_axis=0, concat_axis=0, tiled=True)
    element_count = elem_slot.shape[1]
    set_index = lax.axis_index("elem")
    block_index = lax.axis_index("blk")
    live = lax.dynamic_index_in_dim(set_size, set_index, keepdims=False)
    position = block_index * element_count + jnp.arange(element_count, dtype=jnp.int32)
    weights = jnp.where(position < live, elem_weight, jnp.zeros_like(elem_weight))
    stacked = element_stage(arrived, elem_slot.T, state, weights, element_stiffening)
    rows = basis_modes // n_elem
    cols = basis_modes // n_blk
    n_y = n_blk // 2
    core = block_index % 2
    chip = block_index // 2
    by_dest = stacked.reshape(basis_modes + 8, n_y, 2, cols)
    pair = [(b, b ^ 1) for b in range(n_blk)]
    sent = lax.dynamic_index_in_dim(by_dest, 1 - core, axis=2, keepdims=False)
    kept = lax.dynamic_index_in_dim(by_dest, core, axis=2, keepdims=False)
    chip_sum = kept + lax.ppermute(sent, "blk", pair)
    halfway = lax.dynamic_index_in_dim(chip_sum, chip, axis=1, keepdims=False)
    for shift in range(1, n_y):
        ring = [(2 * y + c, 2 * ((y + shift) % n_y) + c) for y in range(n_y) for c in range(2)]
        piece = lax.dynamic_index_in_dim(chip_sum, (chip + shift) % n_y, axis=1, keepdims=False)
        halfway = halfway + lax.ppermute(piece, "blk", ring)
    force_cols = halfway[basis_modes]
    tangent_rows = halfway[:basis_modes].reshape(n_elem, rows, cols)
    chunks = jnp.concatenate(
        [tangent_rows, jnp.broadcast_to(force_cols[None, None, :], (n_elem, 1, cols))], axis=1
    )
    elem_index = lax.axis_index("elem")
    rest = chunks
    bit = 1
    while bit < n_elem:
        mine_bit = (elem_index // bit) % 2
        split = rest.reshape(rest.shape[0] // 2, 2, rest.shape[1], cols)
        kept = lax.dynamic_index_in_dim(split, mine_bit, axis=1, keepdims=False)
        sent = lax.dynamic_index_in_dim(split, 1 - mine_bit, axis=1, keepdims=False)
        rest = kept + lax.ppermute(sent, "elem", [(e, e ^ bit) for e in range(n_elem)])
        bit *= 2
    mine = rest[0]
    scale = lax.rsqrt(24.0 * jnp.sum(set_size).astype(jnp.float32))
    return (mine[:rows] * scale, mine[rows] * scale - load)


def solution(mesh):
    in_specs = (
        P("elem", None, None),
        P("elem", "blk", None),
        P(None, ("elem", "blk")),
        P(),
        P(("elem", "blk")),
        P(("elem", "blk")),
        P(),
        P("blk"),
    )
    out_specs = (P("elem", "blk"), P("blk"))
    return jax.shard_map(local, mesh=mesh, in_specs=in_specs, out_specs=out_specs, check_vma=False)
```

```python
import jax
import jax.numpy as jnp
from jax import lax
from jax.experimental import pallas as pl
from jax.experimental.pallas import tpu as pltpu
from jax.sharding import PartitionSpec as P

G = [[(2 * ((a >> k) & 1) - 1) * 0.25 for k in range(3)] for a in range(8)]


def element_body(arrived_ref, slot_ref, state_ref, omega_ref, stiff_ref, out_ref, v_ref, w_ref):
    n_el = slot_ref.shape[0]
    n_slot = arrived_ref.shape[0]
    modes = out_ref.shape[1]
    lane = lax.broadcasted_iota(jnp.int32, (n_el, n_slot), 1)
    state_pad = state_ref[...]
    disp = {}
    for a in range(8):
        onehot = (slot_ref[:, a:a + 1] == lane).astype(jnp.bfloat16)
        corner = jnp.dot(onehot, arrived_ref[...], preferred_element_type=jnp.float32).astype(jnp.bfloat16)
        for c in range(3):
            va = corner[:, c * modes:(c + 1) * modes]
            v_ref[pl.ds((3 * a + c) * n_el, n_el), :] = va
            disp[a, c] = jnp.dot(va, state_pad, preferred_element_type=jnp.float32)[:, 0:1]
    h = {}
    for k in range(3):
        for c in range(3):
            acc = G[0][k] * disp[0, c]
            for a in range(1, 8):
                acc = acc + G[a][k] * disp[a, c]
            h[k, c] = acc
    stiff = stiff_ref[...]
    omega = omega_ref[...]
    vol = h[0, 0] + h[1, 1] + h[2, 2]
    lam = 1.0 + stiff * vol ** 2 - 2.0 / 3.0
    press = vol + stiff * vol ** 3 / 3.0 - 2.0 / 3.0 * vol
    stress = {}
    for k in range(3):
        for c in range(3):
            s = h[k, c] + h[c, k]
            if k == c:
                s = s + press
            stress[k, c] = s
    force_acc = jnp.zeros((n_el, modes), jnp.float32)
    for a in range(8):
        for c in range(3):
            f = G[a][0] * stress[0, c] + G[a][1] * stress[1, c] + G[a][2] * stress[2, c]
            f = f + 0.25 * disp[a, c]
            wf = (f * omega).astype(jnp.bfloat16).astype(jnp.float32)
            force_acc = force_acc + v_ref[pl.ds((3 * a + c) * n_el, n_el), :].astype(jnp.float32) * wf
    grad = {}
    for k in range(3):
        signed = None
        for a in range(8):
            term = jnp.where(slot_ref[:, a:a + 1] == lane, G[a][k], 0.0)
            signed = term if signed is None else signed + term
        full = jnp.dot(signed.astype(jnp.bfloat16), arrived_ref[...], preferred_element_type=jnp.float32)
        for c in range(3):
            grad[k, c] = full[:, c * modes:(c + 1) * modes]
    trace = grad[0, 0] + grad[1, 1] + grad[2, 2]
    for a in range(8):
        for c in range(3):
            img = G[a][0] * (grad[0, c] + grad[c, 0])
            img = img + G[a][1] * (grad[1, c] + grad[c, 1])
            img = img + G[a][2] * (grad[2, c] + grad[c, 2])
            img = img + (lam * G[a][c]) * trace
            img = img + 0.25 * v_ref[pl.ds((3 * a + c) * n_el, n_el), :].astype(jnp.float32)
            w_ref[pl.ds((3 * a + c) * n_el, n_el), :] = (omega * img).astype(jnp.bfloat16)
    tangent = lax.dot_general(
        v_ref[...], w_ref[...], (((0,), (0,)), ((), ())), preferred_element_type=jnp.float32
    )
    out_ref[pl.ds(0, modes), :] = tangent
    force_row = jnp.sum(force_acc, axis=0, keepdims=True)
    out_ref[pl.ds(modes, 8), :] = jnp.concatenate(
        [force_row, jnp.zeros((7, modes), jnp.float32)], axis=0
    )


def element_stage(arrived3, slot_t, state, omega, stiff):
    n_el = slot_t.shape[0]
    modes = arrived3.shape[1] // 3
    state_pad = jnp.zeros((modes, 128), jnp.bfloat16).at[:, 0].set(state)
    vmem = pltpu.MemorySpace.VMEM if hasattr(pltpu, "MemorySpace") else pltpu.TPUMemorySpace.VMEM
    return pl.pallas_call(
        element_body,
        out_shape=jax.ShapeDtypeStruct((modes + 8, modes), jnp.float32),
        in_specs=[pl.BlockSpec(memory_space=vmem)] * 5,
        out_specs=pl.BlockSpec(memory_space=vmem),
        scratch_shapes=[
            pltpu.VMEM((24 * n_el, modes), jnp.bfloat16),
            pltpu.VMEM((24 * n_el, modes), jnp.bfloat16),
        ],
    )(arrived3, slot_t, state_pad, omega.reshape(n_el, 1), stiff.reshape(n_el, 1))


def gather_body(basis_ref, rows_ref, out_ref):
    nodes = basis_ref.shape[1]
    n_rows = rows_ref.shape[1]
    node = lax.broadcasted_iota(jnp.int32, (nodes, n_rows), 0)
    onehot_t = (node == rows_ref[...]).astype(jnp.bfloat16)
    picked = lax.dot_general(
        onehot_t, basis_ref[0], (((0,), (0,)), ((), ())), preferred_element_type=jnp.float32
    )
    out_ref[...] = picked.astype(jnp.bfloat16)


def gather_rows(by_component, rows):
    comps, nodes, modes = by_component.shape
    n_rows = rows.shape[0]
    return pl.pallas_call(
        gather_body,
        out_shape=jax.ShapeDtypeStruct((n_rows, comps * modes), jnp.bfloat16),
        grid=(comps,),
        in_specs=[
            pl.BlockSpec((1, nodes, modes), lambda c: (c, 0, 0)),
            pl.BlockSpec((1, n_rows), lambda c: (0, 0)),
        ],
        out_specs=pl.BlockSpec((n_rows, modes), lambda c: (0, c)),
    )(by_component, rows.reshape(1, n_rows))

def local(basis, send_rows, elem_slot, set_size, elem_weight, element_stiffening, state, load):
    basis_modes = basis.shape[2]
    n_elem = lax.psum(1, "elem")
    n_blk = lax.psum(1, "blk")
    by_component = jnp.transpose(basis, (1, 0, 2))
    outgoing = gather_rows(by_component, send_rows[0, 0])
    arrived = lax.all_to_all(outgoing, "elem", split_axis=0, concat_axis=0, tiled=True)
    element_count = elem_slot.shape[1]
    set_index = lax.axis_index("elem")
    block_index = lax.axis_index("blk")
    live = lax.dynamic_index_in_dim(set_size, set_index, keepdims=False)
    position = block_index * element_count + jnp.arange(element_count, dtype=jnp.int32)
    weights = jnp.where(position < live, elem_weight, jnp.zeros_like(elem_weight))
    stacked = element_stage(arrived, elem_slot.T, state, weights, element_stiffening)
    rows = basis_modes // n_elem
    cols = basis_modes // n_blk
    n_y = n_blk // 2
    core = block_index % 2
    chip = block_index // 2
    by_dest = stacked.reshape(basis_modes + 8, n_y, 2, cols)
    pair = [(b, b ^ 1) for b in range(n_blk)]
    sent = lax.dynamic_index_in_dim(by_dest, 1 - core, axis=2, keepdims=False)
    kept = lax.dynamic_index_in_dim(by_dest, core, axis=2, keepdims=False)
    chip_sum = kept + lax.ppermute(sent, "blk", pair)
    halfway = lax.dynamic_index_in_dim(chip_sum, chip, axis=1, keepdims=False)
    for shift in range(1, n_y):
        ring = [(2 * y + c, 2 * ((y + shift) % n_y) + c) for y in range(n_y) for c in range(2)]
        piece = lax.dynamic_index_in_dim(chip_sum, (chip + shift) % n_y, axis=1, keepdims=False)
        halfway = halfway + lax.ppermute(piece, "blk", ring)
    force_cols = halfway[basis_modes]
    tangent_rows = halfway[:basis_modes].reshape(n_elem, rows, cols)
    chunks = jnp.concatenate(
        [tangent_rows, jnp.broadcast_to(force_cols[None, None, :], (n_elem, 1, cols))], axis=1
    )
    arrived_chunks = lax.all_to_all(chunks, "elem", split_axis=0, concat_axis=0, tiled=True)
    mine = jnp.sum(arrived_chunks, axis=0)
    scale = lax.rsqrt(24.0 * jnp.sum(set_size).astype(jnp.float32))
    return (mine[:rows] * scale, mine[rows] * scale - load)


def solution(mesh):
    in_specs = (
        P("elem", None, None),
        P("elem", "blk", None),
        P(None, ("elem", "blk")),
        P(),
        P(("elem", "blk")),
        P(("elem", "blk")),
        P(),
        P("blk"),
    )
    out_specs = (P("elem", "blk"), P("blk"))
    return jax.shard_map(local, mesh=mesh, in_specs=in_specs, out_specs=out_specs, check_vma=False)
```

```python
import jax
import jax.numpy as jnp
from jax import lax
from jax.experimental import pallas as pl
from jax.experimental.pallas import tpu as pltpu
from jax.sharding import PartitionSpec as P

G = [[(2 * ((a >> k) & 1) - 1) * 0.25 for k in range(3)] for a in range(8)]


def element_body(arrived_ref, slot_ref, state_ref, omega_ref, stiff_ref, out_ref, v_ref, w_ref):
    n_el = omega_ref.shape[0]
    n_slot = arrived_ref.shape[0]
    modes = out_ref.shape[1]
    slots = slot_ref[...]
    lane = lax.broadcasted_iota(jnp.int32, (8 * n_el, n_slot), 1)
    onehot = (slots == lane).astype(jnp.bfloat16)
    corners = jnp.dot(onehot, arrived_ref[...], preferred_element_type=jnp.float32).astype(jnp.bfloat16)
    for c in range(3):
        v_ref[pl.ds(c * 8 * n_el, 8 * n_el), :] = corners[:, c * modes:(c + 1) * modes]
    disp_all = jnp.dot(corners, state_ref[...], preferred_element_type=jnp.float32)
    disp = {}
    for a in range(8):
        for c in range(3):
            disp[a, c] = disp_all[a * n_el:(a + 1) * n_el, c:c + 1]
    lane_el = lane[:n_el]
    signed_rows = []
    for k in range(3):
        signed = None
        for a in range(8):
            term = jnp.where(slots[a * n_el:(a + 1) * n_el] == lane_el, G[a][k], 0.0)
            signed = term if signed is None else signed + term
        signed_rows.append(signed)
    signed_all = jnp.concatenate(signed_rows, axis=0).astype(jnp.bfloat16)
    grad_all = jnp.dot(signed_all, arrived_ref[...], preferred_element_type=jnp.float32)
    grad = {}
    for k in range(3):
        for c in range(3):
            grad[k, c] = grad_all[k * n_el:(k + 1) * n_el, c * modes:(c + 1) * modes]

    def corner_rows(a, c):
        return pl.ds(c * 8 * n_el + a * n_el, n_el)

    h = {}
    for k in range(3):
        for c in range(3):
            acc = G[0][k] * disp[0, c]
            for a in range(1, 8):
                acc = acc + G[a][k] * disp[a, c]
            h[k, c] = acc
    stiff = stiff_ref[...]
    omega = omega_ref[...]
    vol = h[0, 0] + h[1, 1] + h[2, 2]
    lam = 1.0 + stiff * vol ** 2 - 2.0 / 3.0
    press = vol + stiff * vol ** 3 / 3.0 - 2.0 / 3.0 * vol
    stress = {}
    for k in range(3):
        for c in range(3):
            s = h[k, c] + h[c, k]
            if k == c:
                s = s + press
            stress[k, c] = s
    force_acc = jnp.zeros((n_el, modes), jnp.float32)
    for a in range(8):
        for c in range(3):
            f = G[a][0] * stress[0, c] + G[a][1] * stress[1, c] + G[a][2] * stress[2, c]
            f = f + 0.25 * disp[a, c]
            wf = (f * omega).astype(jnp.bfloat16).astype(jnp.float32)
            force_acc = force_acc + v_ref[corner_rows(a, c), :].astype(jnp.float32) * wf
    trace = grad[0, 0] + grad[1, 1] + grad[2, 2]
    for a in range(8):
        for c in range(3):
            img = G[a][0] * (grad[0, c] + grad[c, 0])
            img = img + G[a][1] * (grad[1, c] + grad[c, 1])
            img = img + G[a][2] * (grad[2, c] + grad[c, 2])
            img = img + (lam * G[a][c]) * trace
            img = img + 0.25 * v_ref[corner_rows(a, c), :].astype(jnp.float32)
            w_ref[corner_rows(a, c), :] = (omega * img).astype(jnp.bfloat16)
    tangent = lax.dot_general(
        v_ref[...], w_ref[...], (((0,), (0,)), ((), ())), preferred_element_type=jnp.float32
    )
    out_ref[pl.ds(0, modes), :] = tangent
    force_row = jnp.sum(force_acc, axis=0, keepdims=True)
    out_ref[pl.ds(modes, 8), :] = jnp.concatenate(
        [force_row, jnp.zeros((7, modes), jnp.float32)], axis=0
    )


def element_stage(arrived3, slot, state, omega, stiff):
    n_el = slot.shape[1]
    modes = arrived3.shape[1] // 3
    comp = jnp.arange(3 * modes) // modes
    state_blocks = jnp.where(
        comp[:, None] == jnp.arange(128)[None, :], jnp.tile(state, 3)[:, None], jnp.zeros((), state.dtype)
    )
    vmem = pltpu.MemorySpace.VMEM if hasattr(pltpu, "MemorySpace") else pltpu.TPUMemorySpace.VMEM
    return pl.pallas_call(
        element_body,
        out_shape=jax.ShapeDtypeStruct((modes + 8, modes), jnp.float32),
        in_specs=[pl.BlockSpec(memory_space=vmem)] * 5,
        out_specs=pl.BlockSpec(memory_space=vmem),
        scratch_shapes=[
            pltpu.VMEM((24 * n_el, modes), jnp.bfloat16),
            pltpu.VMEM((24 * n_el, modes), jnp.bfloat16),
        ],
    )(arrived3, slot.reshape(8 * n_el, 1), state_blocks, omega.reshape(n_el, 1), stiff.reshape(n_el, 1))


def gather_body(basis_ref, rows_ref, out_ref):
    nodes = basis_ref.shape[1]
    n_rows = rows_ref.shape[1]
    node = lax.broadcasted_iota(jnp.int32, (nodes, n_rows), 0)
    onehot_t = (node == rows_ref[...]).astype(jnp.bfloat16)
    picked = lax.dot_general(
        onehot_t, basis_ref[0], (((0,), (0,)), ((), ())), preferred_element_type=jnp.float32
    )
    out_ref[...] = picked.astype(jnp.bfloat16)


def gather_rows(by_component, rows):
    comps, nodes, modes = by_component.shape
    n_rows = rows.shape[0]
    return pl.pallas_call(
        gather_body,
        out_shape=jax.ShapeDtypeStruct((n_rows, comps * modes), jnp.bfloat16),
        grid=(comps,),
        in_specs=[
            pl.BlockSpec((1, nodes, modes), lambda c: (c, 0, 0)),
            pl.BlockSpec((1, n_rows), lambda c: (0, 0)),
        ],
        out_specs=pl.BlockSpec((n_rows, modes), lambda c: (0, c)),
    )(by_component, rows.reshape(1, n_rows))

def local(basis, send_rows, elem_slot, set_size, elem_weight, element_stiffening, state, load):
    basis_modes = basis.shape[2]
    n_elem = lax.psum(1, "elem")
    n_blk = lax.psum(1, "blk")
    by_component = jnp.transpose(basis, (1, 0, 2))
    outgoing = gather_rows(by_component, send_rows[0, 0])
    arrived = lax.all_to_all(outgoing, "elem", split_axis=0, concat_axis=0, tiled=True)
    element_count = elem_slot.shape[1]
    set_index = lax.axis_index("elem")
    block_index = lax.axis_index("blk")
    live = lax.dynamic_index_in_dim(set_size, set_index, keepdims=False)
    position = block_index * element_count + jnp.arange(element_count, dtype=jnp.int32)
    weights = jnp.where(position < live, elem_weight, jnp.zeros_like(elem_weight))
    stacked = element_stage(arrived, elem_slot, state, weights, element_stiffening)
    rows = basis_modes // n_elem
    cols = basis_modes // n_blk
    n_y = n_blk // 2
    core = block_index % 2
    chip = block_index // 2
    by_dest = stacked.reshape(basis_modes + 8, n_y, 2, cols)
    pair = [(b, b ^ 1) for b in range(n_blk)]
    sent = lax.dynamic_index_in_dim(by_dest, 1 - core, axis=2, keepdims=False)
    kept = lax.dynamic_index_in_dim(by_dest, core, axis=2, keepdims=False)
    chip_sum = kept + lax.ppermute(sent, "blk", pair)
    halfway = lax.dynamic_index_in_dim(chip_sum, chip, axis=1, keepdims=False)
    for shift in range(1, n_y):
        ring = [(2 * y + c, 2 * ((y + shift) % n_y) + c) for y in range(n_y) for c in range(2)]
        piece = lax.dynamic_index_in_dim(chip_sum, (chip + shift) % n_y, axis=1, keepdims=False)
        halfway = halfway + lax.ppermute(piece, "blk", ring)
    force_cols = halfway[basis_modes]
    tangent_rows = halfway[:basis_modes].reshape(n_elem, rows, cols)
    chunks = jnp.concatenate(
        [tangent_rows, jnp.broadcast_to(force_cols[None, None, :], (n_elem, 1, cols))], axis=1
    )
    arrived_chunks = lax.all_to_all(chunks, "elem", split_axis=0, concat_axis=0, tiled=True)
    mine = jnp.sum(arrived_chunks, axis=0)
    scale = lax.rsqrt(24.0 * jnp.sum(set_size).astype(jnp.float32))
    return (mine[:rows] * scale, mine[rows] * scale - load)


def solution(mesh):
    in_specs = (
        P("elem", None, None),
        P("elem", "blk", None),
        P(None, ("elem", "blk")),
        P(),
        P(("elem", "blk")),
        P(("elem", "blk")),
        P(),
        P("blk"),
    )
    out_specs = (P("elem", "blk"), P("blk"))
    return jax.shard_map(local, mesh=mesh, in_specs=in_specs, out_specs=out_specs, check_vma=False)
```

```python
import jax
import jax.numpy as jnp
from jax import lax
from jax.experimental import pallas as pl
from jax.experimental.pallas import tpu as pltpu
from jax.sharding import PartitionSpec as P

G = [[(2 * ((a >> k) & 1) - 1) * 0.25 for k in range(3)] for a in range(8)]


def element_body(arrived_ref, slot_ref, state_ref, omega_ref, stiff_ref, out_ref, v_ref, w_ref):
    n_el = omega_ref.shape[0]
    n_slot = arrived_ref.shape[0]
    modes = out_ref.shape[0]
    slots = slot_ref[...]
    lane = lax.broadcasted_iota(jnp.int32, (8 * n_el, n_slot), 1)
    onehot = (slots == lane).astype(jnp.bfloat16)
    corners = jnp.dot(onehot, arrived_ref[...], preferred_element_type=jnp.float32).astype(jnp.bfloat16)
    for c in range(3):
        v_ref[pl.ds(c * 8 * n_el, 8 * n_el), :] = corners[:, c * modes:(c + 1) * modes]
    disp_all = jnp.dot(corners, state_ref[...], preferred_element_type=jnp.float32)
    disp = {}
    for a in range(8):
        for c in range(3):
            disp[a, c] = disp_all[a * n_el:(a + 1) * n_el, c:c + 1]
    lane_el = lane[:n_el]
    signed_rows = []
    for k in range(3):
        signed = None
        for a in range(8):
            term = jnp.where(slots[a * n_el:(a + 1) * n_el] == lane_el, G[a][k], 0.0)
            signed = term if signed is None else signed + term
        signed_rows.append(signed)
    signed_all = jnp.concatenate(signed_rows, axis=0).astype(jnp.bfloat16)
    grad_all = jnp.dot(signed_all, arrived_ref[...], preferred_element_type=jnp.float32)
    grad = {}
    for k in range(3):
        for c in range(3):
            grad[k, c] = grad_all[k * n_el:(k + 1) * n_el, c * modes:(c + 1) * modes]

    def corner_rows(a, c):
        return pl.ds(c * 8 * n_el + a * n_el, n_el)

    h = {}
    for k in range(3):
        for c in range(3):
            acc = G[0][k] * disp[0, c]
            for a in range(1, 8):
                acc = acc + G[a][k] * disp[a, c]
            h[k, c] = acc
    stiff = stiff_ref[...]
    omega = omega_ref[...]
    vol = h[0, 0] + h[1, 1] + h[2, 2]
    lam = 1.0 + stiff * vol ** 2 - 2.0 / 3.0
    press = vol + stiff * vol ** 3 / 3.0 - 2.0 / 3.0 * vol
    stress = {}
    for k in range(3):
        for c in range(3):
            s = h[k, c] + h[c, k]
            if k == c:
                s = s + press
            stress[k, c] = s
    force_acc = jnp.zeros((n_el, modes), jnp.float32)
    for a in range(8):
        for c in range(3):
            f = G[a][0] * stress[0, c] + G[a][1] * stress[1, c] + G[a][2] * stress[2, c]
            f = f + 0.25 * disp[a, c]
            wf = (f * omega).astype(jnp.bfloat16).astype(jnp.float32)
            force_acc = force_acc + v_ref[corner_rows(a, c), :].astype(jnp.float32) * wf
    trace = grad[0, 0] + grad[1, 1] + grad[2, 2]
    for a in range(8):
        for c in range(3):
            img = G[a][0] * (grad[0, c] + grad[c, 0])
            img = img + G[a][1] * (grad[1, c] + grad[c, 1])
            img = img + G[a][2] * (grad[2, c] + grad[c, 2])
            img = img + (lam * G[a][c]) * trace
            img = img + 0.25 * v_ref[corner_rows(a, c), :].astype(jnp.float32)
            w_ref[corner_rows(a, c), :] = (omega * img).astype(jnp.bfloat16)
    tangent_t = lax.dot_general(
        w_ref[...], v_ref[...], (((0,), (0,)), ((), ())), preferred_element_type=jnp.float32
    )
    out_ref[:, pl.ds(0, modes)] = tangent_t
    force_rows = jnp.concatenate(
        [jnp.sum(force_acc, axis=0, keepdims=True), jnp.zeros((7, modes), jnp.float32)], axis=0
    )
    out_ref[:, pl.ds(modes, 8)] = jnp.transpose(force_rows)


def element_stage(arrived3, slot, state, omega, stiff):
    n_el = slot.shape[1]
    modes = arrived3.shape[1] // 3
    comp = jnp.arange(3 * modes) // modes
    state_blocks = jnp.where(
        comp[:, None] == jnp.arange(128)[None, :], jnp.tile(state, 3)[:, None], jnp.zeros((), state.dtype)
    )
    vmem = pltpu.MemorySpace.VMEM if hasattr(pltpu, "MemorySpace") else pltpu.TPUMemorySpace.VMEM
    return pl.pallas_call(
        element_body,
        out_shape=jax.ShapeDtypeStruct((modes, modes + 8), jnp.float32),
        in_specs=[pl.BlockSpec(memory_space=vmem)] * 5,
        out_specs=pl.BlockSpec(memory_space=vmem),
        scratch_shapes=[
            pltpu.VMEM((24 * n_el, modes), jnp.bfloat16),
            pltpu.VMEM((24 * n_el, modes), jnp.bfloat16),
        ],
    )(arrived3, slot.reshape(8 * n_el, 1), state_blocks, omega.reshape(n_el, 1), stiff.reshape(n_el, 1))


def gather_body(basis_ref, rows_ref, out_ref):
    nodes = basis_ref.shape[1]
    n_rows = rows_ref.shape[1]
    node = lax.broadcasted_iota(jnp.int32, (nodes, n_rows), 0)
    onehot_t = (node == rows_ref[...]).astype(jnp.bfloat16)
    picked = lax.dot_general(
        onehot_t, basis_ref[0], (((0,), (0,)), ((), ())), preferred_element_type=jnp.float32
    )
    out_ref[...] = picked.astype(jnp.bfloat16)


def gather_rows(by_component, rows):
    comps, nodes, modes = by_component.shape
    n_rows = rows.shape[0]
    return pl.pallas_call(
        gather_body,
        out_shape=jax.ShapeDtypeStruct((n_rows, comps * modes), jnp.bfloat16),
        grid=(comps,),
        in_specs=[
            pl.BlockSpec((1, nodes, modes), lambda c: (c, 0, 0)),
            pl.BlockSpec((1, n_rows), lambda c: (0, 0)),
        ],
        out_specs=pl.BlockSpec((n_rows, modes), lambda c: (0, c)),
    )(by_component, rows.reshape(1, n_rows))

def local(basis, send_rows, elem_slot, set_size, elem_weight, element_stiffening, state, load):
    basis_modes = basis.shape[2]
    n_elem = lax.psum(1, "elem")
    n_blk = lax.psum(1, "blk")
    by_component = jnp.transpose(basis, (1, 0, 2))
    outgoing = gather_rows(by_component, send_rows[0, 0])
    arrived = lax.all_to_all(outgoing, "elem", split_axis=0, concat_axis=0, tiled=True)
    element_count = elem_slot.shape[1]
    set_index = lax.axis_index("elem")
    block_index = lax.axis_index("blk")
    live = lax.dynamic_index_in_dim(set_size, set_index, keepdims=False)
    position = block_index * element_count + jnp.arange(element_count, dtype=jnp.int32)
    weights = jnp.where(position < live, elem_weight, jnp.zeros_like(elem_weight))
    stacked = element_stage(arrived, elem_slot, state, weights, element_stiffening).T
    rows = basis_modes // n_elem
    cols = basis_modes // n_blk
    n_y = n_blk // 2
    core = block_index % 2
    chip = block_index // 2
    by_dest = stacked.reshape(basis_modes + 8, n_y, 2, cols)
    pair = [(b, b ^ 1) for b in range(n_blk)]
    sent = lax.dynamic_index_in_dim(by_dest, 1 - core, axis=2, keepdims=False)
    kept = lax.dynamic_index_in_dim(by_dest, core, axis=2, keepdims=False)
    chip_sum = kept + lax.ppermute(sent, "blk", pair)
    halfway = lax.dynamic_index_in_dim(chip_sum, chip, axis=1, keepdims=False)
    for shift in range(1, n_y):
        ring = [(2 * y + c, 2 * ((y + shift) % n_y) + c) for y in range(n_y) for c in range(2)]
        piece = lax.dynamic_index_in_dim(chip_sum, (chip + shift) % n_y, axis=1, keepdims=False)
        halfway = halfway + lax.ppermute(piece, "blk", ring)
    force_cols = halfway[basis_modes]
    tangent_rows = halfway[:basis_modes].reshape(n_elem, rows, cols)
    chunks = jnp.concatenate(
        [tangent_rows, jnp.broadcast_to(force_cols[None, None, :], (n_elem, 1, cols))], axis=1
    )
    arrived_chunks = lax.all_to_all(chunks, "elem", split_axis=0, concat_axis=0, tiled=True)
    mine = jnp.sum(arrived_chunks, axis=0)
    scale = lax.rsqrt(24.0 * jnp.sum(set_size).astype(jnp.float32))
    return (mine[:rows] * scale, mine[rows] * scale - load)


def solution(mesh):
    in_specs = (
        P("elem", None, None),
        P("elem", "blk", None),
        P(None, ("elem", "blk")),
        P(),
        P(("elem", "blk")),
        P(("elem", "blk")),
        P(),
        P("blk"),
    )
    out_specs = (P("elem", "blk"), P("blk"))
    return jax.shard_map(local, mesh=mesh, in_specs=in_specs, out_specs=out_specs, check_vma=False)
```

```python
import jax
import jax.numpy as jnp
from jax import lax
from jax.experimental import pallas as pl
from jax.experimental.pallas import tpu as pltpu
from jax.sharding import PartitionSpec as P

G = [[(2 * ((a >> k) & 1) - 1) * 0.25 for k in range(3)] for a in range(8)]


def element_body(arrived_ref, slot_ref, state_ref, omega_ref, stiff_ref, out_ref, v_ref, w_ref):
    n_el = omega_ref.shape[0]
    n_slot = arrived_ref.shape[0]
    modes = out_ref.shape[1]
    slots = slot_ref[...]
    lane = lax.broadcasted_iota(jnp.int32, (8 * n_el, n_slot), 1)
    onehot = (slots == lane).astype(jnp.bfloat16)
    corners = jnp.dot(onehot, arrived_ref[...], preferred_element_type=jnp.float32).astype(jnp.bfloat16)
    for c in range(3):
        v_ref[pl.ds(c * 8 * n_el, 8 * n_el), :] = corners[:, c * modes:(c + 1) * modes]
    disp_all = jnp.dot(corners, state_ref[...], preferred_element_type=jnp.float32)
    disp = {}
    for a in range(8):
        for c in range(3):
            disp[a, c] = disp_all[a * n_el:(a + 1) * n_el, c:c + 1]
    lane_el = lane[:n_el]
    signed_rows = []
    for k in range(3):
        signed = None
        for a in range(8):
            term = jnp.where(slots[a * n_el:(a + 1) * n_el] == lane_el, G[a][k], 0.0)
            signed = term if signed is None else signed + term
        signed_rows.append(signed)
    signed_all = jnp.concatenate(signed_rows, axis=0).astype(jnp.bfloat16)
    grad_all = jnp.dot(signed_all, arrived_ref[...], preferred_element_type=jnp.float32)
    grad = {}
    for k in range(3):
        for c in range(3):
            grad[k, c] = grad_all[k * n_el:(k + 1) * n_el, c * modes:(c + 1) * modes]

    def corner_rows(a, c):
        return pl.ds(c * 8 * n_el + a * n_el, n_el)

    h = {}
    for k in range(3):
        for c in range(3):
            acc = G[0][k] * disp[0, c]
            for a in range(1, 8):
                acc = acc + G[a][k] * disp[a, c]
            h[k, c] = acc
    stiff = stiff_ref[...]
    omega = omega_ref[...]
    vol = h[0, 0] + h[1, 1] + h[2, 2]
    lam = 1.0 + stiff * vol ** 2 - 2.0 / 3.0
    press = vol + stiff * vol ** 3 / 3.0 - 2.0 / 3.0 * vol
    stress = {}
    for k in range(3):
        for c in range(3):
            s = h[k, c] + h[c, k]
            if k == c:
                s = s + press
            stress[k, c] = s
    force_acc = jnp.zeros((n_el, modes), jnp.float32)
    for a in range(8):
        for c in range(3):
            f = G[a][0] * stress[0, c] + G[a][1] * stress[1, c] + G[a][2] * stress[2, c]
            f = f + 0.25 * disp[a, c]
            wf = (f * omega).astype(jnp.bfloat16).astype(jnp.float32)
            force_acc = force_acc + v_ref[corner_rows(a, c), :].astype(jnp.float32) * wf
    trace = grad[0, 0] + grad[1, 1] + grad[2, 2]
    for a in range(8):
        for c in range(3):
            img = G[a][0] * (grad[0, c] + grad[c, 0])
            img = img + G[a][1] * (grad[1, c] + grad[c, 1])
            img = img + G[a][2] * (grad[2, c] + grad[c, 2])
            img = img + (lam * G[a][c]) * trace
            img = img + 0.25 * v_ref[corner_rows(a, c), :].astype(jnp.float32)
            w_ref[corner_rows(a, c), :] = (omega * img).astype(jnp.bfloat16)
    tangent = lax.dot_general(
        v_ref[...], w_ref[...], (((0,), (0,)), ((), ())), preferred_element_type=jnp.float32
    )
    out_ref[pl.ds(0, modes), :] = tangent
    force_row = jnp.sum(force_acc, axis=0, keepdims=True)
    out_ref[pl.ds(modes, 8), :] = jnp.concatenate(
        [force_row, jnp.zeros((7, modes), jnp.float32)], axis=0
    )


def element_stage(arrived3, slot, state, omega, stiff):
    n_el = slot.shape[1]
    modes = arrived3.shape[1] // 3
    comp = jnp.arange(3 * modes) // modes
    state_blocks = jnp.where(
        comp[:, None] == jnp.arange(128)[None, :], jnp.tile(state, 3)[:, None], jnp.zeros((), state.dtype)
    )
    vmem = pltpu.MemorySpace.VMEM if hasattr(pltpu, "MemorySpace") else pltpu.TPUMemorySpace.VMEM
    return pl.pallas_call(
        element_body,
        out_shape=jax.ShapeDtypeStruct((modes + 8, modes), jnp.float32),
        in_specs=[pl.BlockSpec(memory_space=vmem)] * 5,
        out_specs=pl.BlockSpec(memory_space=vmem),
        scratch_shapes=[
            pltpu.VMEM((24 * n_el, modes), jnp.bfloat16),
            pltpu.VMEM((24 * n_el, modes), jnp.bfloat16),
        ],
    )(arrived3, slot.reshape(8 * n_el, 1), state_blocks, omega.reshape(n_el, 1), stiff.reshape(n_el, 1))


def gather_body(basis_ref, rows_ref, out_ref):
    nodes = basis_ref.shape[1]
    n_rows = rows_ref.shape[1]
    node = lax.broadcasted_iota(jnp.int32, (nodes, n_rows), 0)
    onehot_t = (node == rows_ref[...]).astype(jnp.bfloat16)
    picked = lax.dot_general(
        onehot_t, basis_ref[0], (((0,), (0,)), ((), ())), preferred_element_type=jnp.float32
    )
    out_ref[...] = picked.astype(jnp.bfloat16)


def gather_rows(by_component, rows):
    comps, nodes, modes = by_component.shape
    n_rows = rows.shape[0]
    return pl.pallas_call(
        gather_body,
        out_shape=jax.ShapeDtypeStruct((n_rows, comps * modes), jnp.bfloat16),
        grid=(comps,),
        in_specs=[
            pl.BlockSpec((1, nodes, modes), lambda c: (c, 0, 0)),
            pl.BlockSpec((1, n_rows), lambda c: (0, 0)),
        ],
        out_specs=pl.BlockSpec((n_rows, modes), lambda c: (0, c)),
    )(by_component, rows.reshape(1, n_rows))

def local(basis, send_rows, elem_slot, set_size, elem_weight, element_stiffening, state, load):
    basis_modes = basis.shape[2]
    n_elem = lax.psum(1, "elem")
    n_blk = lax.psum(1, "blk")
    by_component = jnp.transpose(basis, (1, 0, 2))
    outgoing = gather_rows(by_component, send_rows[0, 0])
    arrived = lax.all_to_all(outgoing, "elem", split_axis=0, concat_axis=0, tiled=True)
    element_count = elem_slot.shape[1]
    set_index = lax.axis_index("elem")
    block_index = lax.axis_index("blk")
    live = lax.dynamic_index_in_dim(set_size, set_index, keepdims=False)
    position = block_index * element_count + jnp.arange(element_count, dtype=jnp.int32)
    weights = jnp.where(position < live, elem_weight, jnp.zeros_like(elem_weight))
    stacked = element_stage(arrived, elem_slot, state, weights, element_stiffening)
    rows = basis_modes // n_elem
    cols = basis_modes // n_blk
    n_y = n_blk // 2
    core = block_index % 2
    chip = block_index // 2
    by_dest = stacked.reshape(basis_modes + 8, n_y, 2, cols)
    pair = [(b, b ^ 1) for b in range(n_blk)]
    sent = lax.dynamic_index_in_dim(by_dest, 1 - core, axis=2, keepdims=False)
    kept = lax.dynamic_index_in_dim(by_dest, core, axis=2, keepdims=False)
    chip_sum = kept + lax.ppermute(sent, "blk", pair)
    tang = chip_sum[:basis_modes].reshape(n_elem, rows, n_y, cols).transpose(0, 2, 1, 3)
    force_part = jnp.broadcast_to(chip_sum[basis_modes][None, :, None, :], (n_elem, n_y, 1, cols))
    chunks = jnp.concatenate([tang, force_part], axis=2).reshape(n_elem * n_y, rows + 1, cols)
    groups = [[e * n_blk + 2 * y + c for e in range(n_elem) for y in range(n_y)] for c in range(2)]
    arrived_chunks = lax.all_to_all(
        chunks, ("elem", "blk"), split_axis=0, concat_axis=0, axis_index_groups=groups, tiled=True
    )
    mine = jnp.sum(arrived_chunks, axis=0)
    scale = lax.rsqrt(24.0 * jnp.sum(set_size).astype(jnp.float32))
    return (mine[:rows] * scale, mine[rows] * scale - load)


def solution(mesh):
    in_specs = (
        P("elem", None, None),
        P("elem", "blk", None),
        P(None, ("elem", "blk")),
        P(),
        P(("elem", "blk")),
        P(("elem", "blk")),
        P(),
        P("blk"),
    )
    out_specs = (P("elem", "blk"), P("blk"))
    return jax.shard_map(local, mesh=mesh, in_specs=in_specs, out_specs=out_specs, check_vma=False)
```

```python
import jax
import jax.numpy as jnp
from jax import lax
from jax.experimental import pallas as pl
from jax.experimental.pallas import tpu as pltpu
from jax.sharding import PartitionSpec as P

G = [[(2 * ((a >> k) & 1) - 1) * 0.25 for k in range(3)] for a in range(8)]


def element_body(arrived_ref, slot_ref, state_ref, omega_ref, stiff_ref, out_ref, v_ref, w_ref):
    n_el = omega_ref.shape[0]
    n_slot = arrived_ref.shape[0]
    modes = out_ref.shape[1]
    slots = slot_ref[...]
    lane = lax.broadcasted_iota(jnp.int32, (8 * n_el, n_slot), 1)
    onehot = (slots == lane).astype(jnp.bfloat16)
    corners = jnp.dot(onehot, arrived_ref[...], preferred_element_type=jnp.float32).astype(jnp.bfloat16)
    for c in range(3):
        v_ref[pl.ds(c * 8 * n_el, 8 * n_el), :] = corners[:, c * modes:(c + 1) * modes]
    disp_all = jnp.dot(corners, state_ref[...], preferred_element_type=jnp.float32)
    disp = {}
    for a in range(8):
        for c in range(3):
            disp[a, c] = disp_all[a * n_el:(a + 1) * n_el, c:c + 1]
    lane_el = lane[:n_el]
    signed_rows = []
    for k in range(3):
        signed = None
        for a in range(8):
            term = jnp.where(slots[a * n_el:(a + 1) * n_el] == lane_el, G[a][k], 0.0)
            signed = term if signed is None else signed + term
        signed_rows.append(signed)
    signed_all = jnp.concatenate(signed_rows, axis=0).astype(jnp.bfloat16)
    grad_all = jnp.dot(signed_all, arrived_ref[...], preferred_element_type=jnp.float32)
    grad = {}
    for k in range(3):
        for c in range(3):
            grad[k, c] = grad_all[k * n_el:(k + 1) * n_el, c * modes:(c + 1) * modes]

    def corner_rows(a, c):
        return pl.ds(c * 8 * n_el + a * n_el, n_el)

    h = {}
    for k in range(3):
        for c in range(3):
            acc = G[0][k] * disp[0, c]
            for a in range(1, 8):
                acc = acc + G[a][k] * disp[a, c]
            h[k, c] = acc
    stiff = stiff_ref[...]
    omega = omega_ref[...]
    vol = h[0, 0] + h[1, 1] + h[2, 2]
    lam = 1.0 + stiff * vol ** 2 - 2.0 / 3.0
    press = vol + stiff * vol ** 3 / 3.0 - 2.0 / 3.0 * vol
    stress = {}
    for k in range(3):
        for c in range(3):
            s = h[k, c] + h[c, k]
            if k == c:
                s = s + press
            stress[k, c] = s
    force_acc = jnp.zeros((n_el, modes), jnp.float32)
    for a in range(8):
        for c in range(3):
            f = G[a][0] * stress[0, c] + G[a][1] * stress[1, c] + G[a][2] * stress[2, c]
            f = f + 0.25 * disp[a, c]
            wf = (f * omega).astype(jnp.bfloat16).astype(jnp.float32)
            force_acc = force_acc + v_ref[corner_rows(a, c), :].astype(jnp.float32) * wf
    trace = grad[0, 0] + grad[1, 1] + grad[2, 2]
    for a in range(8):
        for c in range(3):
            img = G[a][0] * (grad[0, c] + grad[c, 0])
            img = img + G[a][1] * (grad[1, c] + grad[c, 1])
            img = img + G[a][2] * (grad[2, c] + grad[c, 2])
            img = img + (lam * G[a][c]) * trace
            img = img + 0.25 * v_ref[corner_rows(a, c), :].astype(jnp.float32)
            w_ref[corner_rows(a, c), :] = (omega * img).astype(jnp.bfloat16)
    tangent = lax.dot_general(
        v_ref[...], w_ref[...], (((0,), (0,)), ((), ())), preferred_element_type=jnp.float32
    )
    out_ref[pl.ds(0, modes), :] = tangent
    force_row = jnp.sum(force_acc, axis=0, keepdims=True)
    out_ref[pl.ds(modes, 8), :] = jnp.concatenate(
        [force_row, jnp.zeros((7, modes), jnp.float32)], axis=0
    )


def element_stage(arrived3, slot, state, omega, stiff):
    n_el = slot.shape[1]
    modes = arrived3.shape[1] // 3
    comp = jnp.arange(3 * modes) // modes
    state_blocks = jnp.where(
        comp[:, None] == jnp.arange(128)[None, :], jnp.tile(state, 3)[:, None], jnp.zeros((), state.dtype)
    )
    vmem = pltpu.MemorySpace.VMEM if hasattr(pltpu, "MemorySpace") else pltpu.TPUMemorySpace.VMEM
    return pl.pallas_call(
        element_body,
        out_shape=jax.ShapeDtypeStruct((modes + 8, modes), jnp.float32),
        in_specs=[pl.BlockSpec(memory_space=vmem)] * 5,
        out_specs=pl.BlockSpec(memory_space=vmem),
        scratch_shapes=[
            pltpu.VMEM((24 * n_el, modes), jnp.bfloat16),
            pltpu.VMEM((24 * n_el, modes), jnp.bfloat16),
        ],
    )(arrived3, slot.reshape(8 * n_el, 1), state_blocks, omega.reshape(n_el, 1), stiff.reshape(n_el, 1))


def gather_body(basis_ref, rows_ref, out_ref):
    nodes = basis_ref.shape[1]
    n_rows = rows_ref.shape[1]
    node = lax.broadcasted_iota(jnp.int32, (nodes, n_rows), 0)
    onehot_t = (node == rows_ref[...]).astype(jnp.bfloat16)
    picked = lax.dot_general(
        onehot_t, basis_ref[0], (((0,), (0,)), ((), ())), preferred_element_type=jnp.float32
    )
    out_ref[...] = picked.astype(jnp.bfloat16)


def gather_rows(by_component, rows):
    comps, nodes, modes = by_component.shape
    n_rows = rows.shape[0]
    return pl.pallas_call(
        gather_body,
        out_shape=jax.ShapeDtypeStruct((n_rows, comps * modes), jnp.bfloat16),
        grid=(comps,),
        in_specs=[
            pl.BlockSpec((1, nodes, modes), lambda c: (c, 0, 0)),
            pl.BlockSpec((1, n_rows), lambda c: (0, 0)),
        ],
        out_specs=pl.BlockSpec((n_rows, modes), lambda c: (0, c)),
    )(by_component, rows.reshape(1, n_rows))

def local(basis, send_rows, elem_slot, set_size, elem_weight, element_stiffening, state, load):
    basis_modes = basis.shape[2]
    n_elem = lax.psum(1, "elem")
    n_blk = lax.psum(1, "blk")
    by_component = jnp.transpose(basis, (1, 0, 2))
    outgoing = gather_rows(by_component, send_rows[0, 0])
    arrived = lax.all_to_all(outgoing, "elem", split_axis=0, concat_axis=0, tiled=True)
    element_count = elem_slot.shape[1]
    set_index = lax.axis_index("elem")
    block_index = lax.axis_index("blk")
    live = lax.dynamic_index_in_dim(set_size, set_index, keepdims=False)
    position = block_index * element_count + jnp.arange(element_count, dtype=jnp.int32)
    weights = jnp.where(position < live, elem_weight, jnp.zeros_like(elem_weight))
    stacked = element_stage(arrived, elem_slot, state, weights, element_stiffening)
    rows = basis_modes // n_elem
    cols = basis_modes // n_blk
    n_y = n_blk // 2
    core = block_index % 2
    chip = block_index // 2
    by_dest = stacked.reshape(basis_modes + 8, n_y, 2, cols)
    pair = [(b, b ^ 1) for b in range(n_blk)]
    sent = lax.dynamic_index_in_dim(by_dest, 1 - core, axis=2, keepdims=False)
    kept = lax.dynamic_index_in_dim(by_dest, core, axis=2, keepdims=False)
    chip_sum = kept + lax.ppermute(sent, "blk", pair)
    halfway = lax.dynamic_index_in_dim(chip_sum, chip, axis=1, keepdims=False)
    for shift in range(1, n_y):
        ring = [(2 * y + c, 2 * ((y + shift) % n_y) + c) for y in range(n_y) for c in range(2)]
        piece = lax.dynamic_index_in_dim(chip_sum, (chip + shift) % n_y, axis=1, keepdims=False)
        halfway = halfway + lax.ppermute(piece, "blk", ring)
    force_cols = halfway[basis_modes]
    tangent_rows = halfway[:basis_modes].reshape(n_elem, rows, cols)
    chunks = jnp.concatenate(
        [tangent_rows, jnp.broadcast_to(force_cols[None, None, :], (n_elem, 1, cols))], axis=1
    )
    n_x = 4
    n_z = n_elem // n_x
    by_x = chunks.reshape(n_z, n_x, rows + 1, cols).transpose(1, 0, 2, 3)
    x_groups = [[z * n_x + x for x in range(n_x)] for z in range(n_z)]
    z_groups = [[z * n_x + x for z in range(n_z)] for x in range(n_x)]
    along_x = lax.all_to_all(by_x, "elem", 0, 0, axis_index_groups=x_groups, tiled=True)
    partial = jnp.sum(along_x.reshape(n_x, n_z, rows + 1, cols), axis=0)
    along_z = lax.all_to_all(partial, "elem", 0, 0, axis_index_groups=z_groups, tiled=True)
    mine = jnp.sum(along_z, axis=0)
    scale = lax.rsqrt(24.0 * jnp.sum(set_size).astype(jnp.float32))
    return (mine[:rows] * scale, mine[rows] * scale - load)


def solution(mesh):
    in_specs = (
        P("elem", None, None),
        P("elem", "blk", None),
        P(None, ("elem", "blk")),
        P(),
        P(("elem", "blk")),
        P(("elem", "blk")),
        P(),
        P("blk"),
    )
    out_specs = (P("elem", "blk"), P("blk"))
    return jax.shard_map(local, mesh=mesh, in_specs=in_specs, out_specs=out_specs, check_vma=False)
```

```python
import jax
import jax.numpy as jnp
from jax import lax
from jax.experimental import pallas as pl
from jax.experimental.pallas import tpu as pltpu
from jax.sharding import PartitionSpec as P

G = [[(2 * ((a >> k) & 1) - 1) * 0.25 for k in range(3)] for a in range(8)]


def element_body(arrived_ref, slot_ref, state_ref, omega_ref, stiff_ref, out_ref, v_ref, w_ref):
    n_el = omega_ref.shape[0]
    n_slot = arrived_ref.shape[0]
    modes = out_ref.shape[1]
    slots = slot_ref[...]
    lane = lax.broadcasted_iota(jnp.int32, (8 * n_el, n_slot), 1)
    onehot = (slots == lane).astype(jnp.bfloat16)
    corners = jnp.dot(onehot, arrived_ref[...], preferred_element_type=jnp.float32).astype(jnp.bfloat16)
    for c in range(3):
        v_ref[pl.ds(c * 8 * n_el, 8 * n_el), :] = corners[:, c * modes:(c + 1) * modes]
    disp_all = jnp.dot(corners, state_ref[...], preferred_element_type=jnp.float32)
    disp = {}
    for a in range(8):
        for c in range(3):
            disp[a, c] = disp_all[a * n_el:(a + 1) * n_el, c:c + 1]
    lane_el = lane[:n_el]
    signed_rows = []
    for k in range(3):
        signed = None
        for a in range(8):
            term = jnp.where(slots[a * n_el:(a + 1) * n_el] == lane_el, G[a][k], 0.0)
            signed = term if signed is None else signed + term
        signed_rows.append(signed)
    signed_all = jnp.concatenate(signed_rows, axis=0).astype(jnp.bfloat16)
    grad_all = jnp.dot(signed_all, arrived_ref[...], preferred_element_type=jnp.float32)
    grad = {}
    for k in range(3):
        for c in range(3):
            grad[k, c] = grad_all[k * n_el:(k + 1) * n_el, c * modes:(c + 1) * modes]

    def corner_rows(a, c):
        return pl.ds(c * 8 * n_el + a * n_el, n_el)

    h = {}
    for k in range(3):
        for c in range(3):
            acc = G[0][k] * disp[0, c]
            for a in range(1, 8):
                acc = acc + G[a][k] * disp[a, c]
            h[k, c] = acc
    stiff = stiff_ref[...]
    omega = omega_ref[...]
    vol = h[0, 0] + h[1, 1] + h[2, 2]
    lam = 1.0 + stiff * vol ** 2 - 2.0 / 3.0
    press = vol + stiff * vol ** 3 / 3.0 - 2.0 / 3.0 * vol
    stress = {}
    for k in range(3):
        for c in range(3):
            s = h[k, c] + h[c, k]
            if k == c:
                s = s + press
            stress[k, c] = s
    force_acc = jnp.zeros((n_el, modes), jnp.float32)
    for a in range(8):
        for c in range(3):
            f = G[a][0] * stress[0, c] + G[a][1] * stress[1, c] + G[a][2] * stress[2, c]
            f = f + 0.25 * disp[a, c]
            wf = (f * omega).astype(jnp.bfloat16).astype(jnp.float32)
            force_acc = force_acc + v_ref[corner_rows(a, c), :].astype(jnp.float32) * wf
    trace = grad[0, 0] + grad[1, 1] + grad[2, 2]
    for a in range(8):
        for c in range(3):
            img = G[a][0] * (grad[0, c] + grad[c, 0])
            img = img + G[a][1] * (grad[1, c] + grad[c, 1])
            img = img + G[a][2] * (grad[2, c] + grad[c, 2])
            img = img + (lam * G[a][c]) * trace
            img = img + 0.25 * v_ref[corner_rows(a, c), :].astype(jnp.float32)
            w_ref[corner_rows(a, c), :] = (omega * img).astype(jnp.bfloat16)
    tangent = lax.dot_general(
        v_ref[...], w_ref[...], (((0,), (0,)), ((), ())), preferred_element_type=jnp.float32
    )
    out_ref[pl.ds(0, modes), :] = tangent
    force_row = jnp.sum(force_acc, axis=0, keepdims=True)
    out_ref[pl.ds(modes, 8), :] = jnp.concatenate(
        [force_row, jnp.zeros((7, modes), jnp.float32)], axis=0
    )


def element_stage(arrived3, slot, state, omega, stiff):
    n_el = slot.shape[1]
    modes = arrived3.shape[1] // 3
    comp = jnp.arange(3 * modes) // modes
    state_blocks = jnp.where(
        comp[:, None] == jnp.arange(128)[None, :], jnp.tile(state, 3)[:, None], jnp.zeros((), state.dtype)
    )
    vmem = pltpu.MemorySpace.VMEM if hasattr(pltpu, "MemorySpace") else pltpu.TPUMemorySpace.VMEM
    return pl.pallas_call(
        element_body,
        out_shape=jax.ShapeDtypeStruct((modes + 8, modes), jnp.float32),
        in_specs=[pl.BlockSpec(memory_space=vmem)] * 5,
        out_specs=pl.BlockSpec(memory_space=vmem),
        scratch_shapes=[
            pltpu.VMEM((24 * n_el, modes), jnp.bfloat16),
            pltpu.VMEM((24 * n_el, modes), jnp.bfloat16),
        ],
    )(arrived3, slot.reshape(8 * n_el, 1), state_blocks, omega.reshape(n_el, 1), stiff.reshape(n_el, 1))


def gather_body(basis_ref, rows_ref, out_ref):
    nodes = basis_ref.shape[1]
    n_rows = rows_ref.shape[1]
    node = lax.broadcasted_iota(jnp.int32, (nodes, n_rows), 0)
    onehot_t = (node == rows_ref[...]).astype(jnp.bfloat16)
    picked = lax.dot_general(
        onehot_t, basis_ref[0], (((0,), (0,)), ((), ())), preferred_element_type=jnp.float32
    )
    out_ref[...] = picked.astype(jnp.bfloat16)


def gather_rows(by_component, rows):
    comps, nodes, modes = by_component.shape
    n_rows = rows.shape[0]
    return pl.pallas_call(
        gather_body,
        out_shape=jax.ShapeDtypeStruct((n_rows, comps * modes), jnp.bfloat16),
        grid=(comps,),
        in_specs=[
            pl.BlockSpec((1, nodes, modes), lambda c: (c, 0, 0)),
            pl.BlockSpec((1, n_rows), lambda c: (0, 0)),
        ],
        out_specs=pl.BlockSpec((n_rows, modes), lambda c: (0, c)),
    )(by_component, rows.reshape(1, n_rows))

def local(basis, send_rows, elem_slot, set_size, elem_weight, element_stiffening, state, load):
    basis_modes = basis.shape[2]
    n_elem = lax.psum(1, "elem")
    n_blk = lax.psum(1, "blk")
    by_component = jnp.transpose(basis, (1, 0, 2))
    outgoing = jnp.concatenate(
        [jnp.take(by_component[c], send_rows[0, 0], axis=0) for c in range(by_component.shape[0])], axis=1
    )
    arrived = lax.all_to_all(outgoing, "elem", split_axis=0, concat_axis=0, tiled=True)
    element_count = elem_slot.shape[1]
    set_index = lax.axis_index("elem")
    block_index = lax.axis_index("blk")
    live = lax.dynamic_index_in_dim(set_size, set_index, keepdims=False)
    position = block_index * element_count + jnp.arange(element_count, dtype=jnp.int32)
    weights = jnp.where(position < live, elem_weight, jnp.zeros_like(elem_weight))
    stacked = element_stage(arrived, elem_slot, state, weights, element_stiffening)
    rows = basis_modes // n_elem
    cols = basis_modes // n_blk
    n_y = n_blk // 2
    core = block_index % 2
    chip = block_index // 2
    by_dest = stacked.reshape(basis_modes + 8, n_y, 2, cols)
    pair = [(b, b ^ 1) for b in range(n_blk)]
    sent = lax.dynamic_index_in_dim(by_dest, 1 - core, axis=2, keepdims=False)
    kept = lax.dynamic_index_in_dim(by_dest, core, axis=2, keepdims=False)
    chip_sum = kept + lax.ppermute(sent, "blk", pair)
    halfway = lax.dynamic_index_in_dim(chip_sum, chip, axis=1, keepdims=False)
    for shift in range(1, n_y):
        ring = [(2 * y + c, 2 * ((y + shift) % n_y) + c) for y in range(n_y) for c in range(2)]
        piece = lax.dynamic_index_in_dim(chip_sum, (chip + shift) % n_y, axis=1, keepdims=False)
        halfway = halfway + lax.ppermute(piece, "blk", ring)
    force_cols = halfway[basis_modes]
    tangent_rows = halfway[:basis_modes].reshape(n_elem, rows, cols)
    chunks = jnp.concatenate(
        [tangent_rows, jnp.broadcast_to(force_cols[None, None, :], (n_elem, 1, cols))], axis=1
    )
    arrived_chunks = lax.all_to_all(chunks, "elem", split_axis=0, concat_axis=0, tiled=True)
    mine = jnp.sum(arrived_chunks, axis=0)
    scale = lax.rsqrt(24.0 * jnp.sum(set_size).astype(jnp.float32))
    return (mine[:rows] * scale, mine[rows] * scale - load)


def solution(mesh):
    in_specs = (
        P("elem", None, None),
        P("elem", "blk", None),
        P(None, ("elem", "blk")),
        P(),
        P(("elem", "blk")),
        P(("elem", "blk")),
        P(),
        P("blk"),
    )
    out_specs = (P("elem", "blk"), P("blk"))
    return jax.shard_map(local, mesh=mesh, in_specs=in_specs, out_specs=out_specs, check_vma=False)
```

```python
import jax
import jax.numpy as jnp
from jax import lax
from jax.experimental import pallas as pl
from jax.experimental.pallas import tpu as pltpu
from jax.sharding import PartitionSpec as P

G = [[(2 * ((a >> k) & 1) - 1) * 0.25 for k in range(3)] for a in range(8)]


def element_body(arrived_ref, slot_ref, state_ref, omega_ref, stiff_ref, out_ref, v_ref, w_ref):
    n_el = omega_ref.shape[0]
    n_slot = arrived_ref.shape[0]
    modes = out_ref.shape[1]
    slots = slot_ref[...]
    lane = lax.broadcasted_iota(jnp.int32, (8 * n_el, n_slot), 1)
    onehot = (slots == lane).astype(jnp.bfloat16)
    corners = jnp.dot(onehot, arrived_ref[...], preferred_element_type=jnp.float32).astype(jnp.bfloat16)
    for c in range(3):
        v_ref[pl.ds(c * 8 * n_el, 8 * n_el), :] = corners[:, c * modes:(c + 1) * modes]
    disp_all = jnp.dot(corners, state_ref[...], preferred_element_type=jnp.float32)
    disp = {}
    for a in range(8):
        for c in range(3):
            disp[a, c] = disp_all[a * n_el:(a + 1) * n_el, c:c + 1]
    lane_el = lane[:n_el]
    signed_rows = []
    for k in range(3):
        signed = None
        for a in range(8):
            term = jnp.where(slots[a * n_el:(a + 1) * n_el] == lane_el, G[a][k], 0.0)
            signed = term if signed is None else signed + term
        signed_rows.append(signed)
    signed_all = jnp.concatenate(signed_rows, axis=0).astype(jnp.bfloat16)
    grad_all = jnp.dot(signed_all, arrived_ref[...], preferred_element_type=jnp.float32)
    grad = {}
    for k in range(3):
        for c in range(3):
            grad[k, c] = grad_all[k * n_el:(k + 1) * n_el, c * modes:(c + 1) * modes]

    def corner_rows(a, c):
        return pl.ds(c * 8 * n_el + a * n_el, n_el)

    h = {}
    for k in range(3):
        for c in range(3):
            acc = G[0][k] * disp[0, c]
            for a in range(1, 8):
                acc = acc + G[a][k] * disp[a, c]
            h[k, c] = acc
    stiff = stiff_ref[...]
    omega = omega_ref[...]
    vol = h[0, 0] + h[1, 1] + h[2, 2]
    lam = 1.0 + stiff * vol ** 2 - 2.0 / 3.0
    press = vol + stiff * vol ** 3 / 3.0 - 2.0 / 3.0 * vol
    stress = {}
    for k in range(3):
        for c in range(3):
            s = h[k, c] + h[c, k]
            if k == c:
                s = s + press
            stress[k, c] = s
    force_acc = jnp.zeros((n_el, modes), jnp.float32)
    for a in range(8):
        for c in range(3):
            f = G[a][0] * stress[0, c] + G[a][1] * stress[1, c] + G[a][2] * stress[2, c]
            f = f + 0.25 * disp[a, c]
            wf = (f * omega).astype(jnp.bfloat16).astype(jnp.float32)
            force_acc = force_acc + v_ref[corner_rows(a, c), :].astype(jnp.float32) * wf
    trace = grad[0, 0] + grad[1, 1] + grad[2, 2]
    for a in range(8):
        for c in range(3):
            img = G[a][0] * (grad[0, c] + grad[c, 0])
            img = img + G[a][1] * (grad[1, c] + grad[c, 1])
            img = img + G[a][2] * (grad[2, c] + grad[c, 2])
            img = img + (lam * G[a][c]) * trace
            img = img + 0.25 * v_ref[corner_rows(a, c), :].astype(jnp.float32)
            w_ref[corner_rows(a, c), :] = (omega * img).astype(jnp.bfloat16)
    tangent = lax.dot_general(
        v_ref[...], w_ref[...], (((0,), (0,)), ((), ())), preferred_element_type=jnp.float32
    )
    out_ref[pl.ds(0, modes), :] = tangent
    force_row = jnp.sum(force_acc, axis=0, keepdims=True)
    out_ref[pl.ds(modes, 8), :] = jnp.concatenate(
        [force_row, jnp.zeros((7, modes), jnp.float32)], axis=0
    )


def element_stage(arrived3, slot, state, omega, stiff):
    n_el = slot.shape[1]
    modes = arrived3.shape[1] // 3
    comp = jnp.arange(3 * modes) // modes
    state_blocks = jnp.where(
        comp[:, None] == jnp.arange(128)[None, :], jnp.tile(state, 3)[:, None], jnp.zeros((), state.dtype)
    )
    vmem = pltpu.MemorySpace.VMEM if hasattr(pltpu, "MemorySpace") else pltpu.TPUMemorySpace.VMEM
    return pl.pallas_call(
        element_body,
        out_shape=jax.ShapeDtypeStruct((modes + 8, modes), jnp.float32),
        in_specs=[pl.BlockSpec(memory_space=vmem)] * 5,
        out_specs=pl.BlockSpec(memory_space=vmem),
        scratch_shapes=[
            pltpu.VMEM((24 * n_el, modes), jnp.bfloat16),
            pltpu.VMEM((24 * n_el, modes), jnp.bfloat16),
        ],
    )(arrived3, slot.reshape(8 * n_el, 1), state_blocks, omega.reshape(n_el, 1), stiff.reshape(n_el, 1))


def gather_body(basis_hbm, rows_ref, out_ref, buf, sem):
    comps, nodes, modes = buf.shape
    n_rows = rows_ref.shape[1]
    copies = [pltpu.make_async_copy(basis_hbm.at[c], buf.at[c], sem.at[c]) for c in range(comps)]
    for copy in copies:
        copy.start()
    node = lax.broadcasted_iota(jnp.int32, (nodes, n_rows), 0)
    onehot_t = (node == rows_ref[...]).astype(jnp.bfloat16)
    for c in range(comps):
        copies[c].wait()
        picked = lax.dot_general(
            onehot_t, buf[c], (((0,), (0,)), ((), ())), preferred_element_type=jnp.float32
        )
        out_ref[:, pl.ds(c * modes, modes)] = picked.astype(jnp.bfloat16)


def gather_rows(by_component, rows):
    comps, nodes, modes = by_component.shape
    n_rows = rows.shape[0]
    vmem = pltpu.MemorySpace.VMEM if hasattr(pltpu, "MemorySpace") else pltpu.TPUMemorySpace.VMEM
    return pl.pallas_call(
        gather_body,
        out_shape=jax.ShapeDtypeStruct((n_rows, comps * modes), jnp.bfloat16),
        in_specs=[pl.BlockSpec(memory_space=pl.ANY), pl.BlockSpec(memory_space=vmem)],
        out_specs=pl.BlockSpec(memory_space=vmem),
        scratch_shapes=[
            pltpu.VMEM((comps, nodes, modes), jnp.bfloat16),
            pltpu.SemaphoreType.DMA((comps,)),
        ],
    )(by_component, rows.reshape(1, n_rows))

def local(basis, send_rows, elem_slot, set_size, elem_weight, element_stiffening, state, load):
    basis_modes = basis.shape[2]
    n_elem = lax.psum(1, "elem")
    n_blk = lax.psum(1, "blk")
    by_component = jnp.transpose(basis, (1, 0, 2))
    outgoing = gather_rows(by_component, send_rows[0, 0])
    arrived = lax.all_to_all(outgoing, "elem", split_axis=0, concat_axis=0, tiled=True)
    element_count = elem_slot.shape[1]
    set_index = lax.axis_index("elem")
    block_index = lax.axis_index("blk")
    live = lax.dynamic_index_in_dim(set_size, set_index, keepdims=False)
    position = block_index * element_count + jnp.arange(element_count, dtype=jnp.int32)
    weights = jnp.where(position < live, elem_weight, jnp.zeros_like(elem_weight))
    stacked = element_stage(arrived, elem_slot, state, weights, element_stiffening)
    rows = basis_modes // n_elem
    cols = basis_modes // n_blk
    n_y = n_blk // 2
    core = block_index % 2
    chip = block_index // 2
    by_dest = stacked.reshape(basis_modes + 8, n_y, 2, cols)
    pair = [(b, b ^ 1) for b in range(n_blk)]
    sent = lax.dynamic_index_in_dim(by_dest, 1 - core, axis=2, keepdims=False)
    kept = lax.dynamic_index_in_dim(by_dest, core, axis=2, keepdims=False)
    chip_sum = kept + lax.ppermute(sent, "blk", pair)
    halfway = lax.dynamic_index_in_dim(chip_sum, chip, axis=1, keepdims=False)
    for shift in range(1, n_y):
        ring = [(2 * y + c, 2 * ((y + shift) % n_y) + c) for y in range(n_y) for c in range(2)]
        piece = lax.dynamic_index_in_dim(chip_sum, (chip + shift) % n_y, axis=1, keepdims=False)
        halfway = halfway + lax.ppermute(piece, "blk", ring)
    force_cols = halfway[basis_modes]
    tangent_rows = halfway[:basis_modes].reshape(n_elem, rows, cols)
    chunks = jnp.concatenate(
        [tangent_rows, jnp.broadcast_to(force_cols[None, None, :], (n_elem, 1, cols))], axis=1
    )
    arrived_chunks = lax.all_to_all(chunks, "elem", split_axis=0, concat_axis=0, tiled=True)
    mine = jnp.sum(arrived_chunks, axis=0)
    scale = lax.rsqrt(24.0 * jnp.sum(set_size).astype(jnp.float32))
    return (mine[:rows] * scale, mine[rows] * scale - load)


def solution(mesh):
    in_specs = (
        P("elem", None, None),
        P("elem", "blk", None),
        P(None, ("elem", "blk")),
        P(),
        P(("elem", "blk")),
        P(("elem", "blk")),
        P(),
        P("blk"),
    )
    out_specs = (P("elem", "blk"), P("blk"))
    return jax.shard_map(local, mesh=mesh, in_specs=in_specs, out_specs=out_specs, check_vma=False)
```

```python
import jax
import jax.numpy as jnp
from jax import lax
from jax.experimental import pallas as pl
from jax.experimental.pallas import tpu as pltpu
from jax.sharding import PartitionSpec as P

G = [[(2 * ((a >> k) & 1) - 1) * 0.25 for k in range(3)] for a in range(8)]


def element_body(arrived_hbm, slot_ref, state_ref, omega_ref, stiff_ref, out_ref, v_ref, w_ref, arrived_ref, sem):
    n_el = omega_ref.shape[0]
    n_slot = arrived_ref.shape[0]
    modes = out_ref.shape[1]
    fetch = pltpu.make_async_copy(arrived_hbm, arrived_ref, sem.at[0])
    fetch.start()
    slots = slot_ref[...]
    lane = lax.broadcasted_iota(jnp.int32, (8 * n_el, n_slot), 1)
    onehot = (slots == lane).astype(jnp.bfloat16)
    lane_el = lane[:n_el]
    signed_rows = []
    for k in range(3):
        signed = None
        for a in range(8):
            term = jnp.where(slots[a * n_el:(a + 1) * n_el] == lane_el, G[a][k], 0.0)
            signed = term if signed is None else signed + term
        signed_rows.append(signed)
    signed_all = jnp.concatenate(signed_rows, axis=0).astype(jnp.bfloat16)
    fetch.wait()
    corners = jnp.dot(onehot, arrived_ref[...], preferred_element_type=jnp.float32).astype(jnp.bfloat16)
    for c in range(3):
        v_ref[pl.ds(c * 8 * n_el, 8 * n_el), :] = corners[:, c * modes:(c + 1) * modes]
    disp_all = jnp.dot(corners, state_ref[...], preferred_element_type=jnp.float32)
    disp = {}
    for a in range(8):
        for c in range(3):
            disp[a, c] = disp_all[a * n_el:(a + 1) * n_el, c:c + 1]
    grad_all = jnp.dot(signed_all, arrived_ref[...], preferred_element_type=jnp.float32)
    grad = {}
    for k in range(3):
        for c in range(3):
            grad[k, c] = grad_all[k * n_el:(k + 1) * n_el, c * modes:(c + 1) * modes]

    def corner_rows(a, c):
        return pl.ds(c * 8 * n_el + a * n_el, n_el)

    h = {}
    for k in range(3):
        for c in range(3):
            acc = G[0][k] * disp[0, c]
            for a in range(1, 8):
                acc = acc + G[a][k] * disp[a, c]
            h[k, c] = acc
    stiff = stiff_ref[...]
    omega = omega_ref[...]
    vol = h[0, 0] + h[1, 1] + h[2, 2]
    lam = 1.0 + stiff * vol ** 2 - 2.0 / 3.0
    press = vol + stiff * vol ** 3 / 3.0 - 2.0 / 3.0 * vol
    stress = {}
    for k in range(3):
        for c in range(3):
            s = h[k, c] + h[c, k]
            if k == c:
                s = s + press
            stress[k, c] = s
    force_acc = jnp.zeros((n_el, modes), jnp.float32)
    for a in range(8):
        for c in range(3):
            f = G[a][0] * stress[0, c] + G[a][1] * stress[1, c] + G[a][2] * stress[2, c]
            f = f + 0.25 * disp[a, c]
            wf = (f * omega).astype(jnp.bfloat16).astype(jnp.float32)
            force_acc = force_acc + v_ref[corner_rows(a, c), :].astype(jnp.float32) * wf
    trace = grad[0, 0] + grad[1, 1] + grad[2, 2]
    for a in range(8):
        for c in range(3):
            img = G[a][0] * (grad[0, c] + grad[c, 0])
            img = img + G[a][1] * (grad[1, c] + grad[c, 1])
            img = img + G[a][2] * (grad[2, c] + grad[c, 2])
            img = img + (lam * G[a][c]) * trace
            img = img + 0.25 * v_ref[corner_rows(a, c), :].astype(jnp.float32)
            w_ref[corner_rows(a, c), :] = (omega * img).astype(jnp.bfloat16)
    tangent = lax.dot_general(
        v_ref[...], w_ref[...], (((0,), (0,)), ((), ())), preferred_element_type=jnp.float32
    )
    out_ref[pl.ds(0, modes), :] = tangent
    force_row = jnp.sum(force_acc, axis=0, keepdims=True)
    out_ref[pl.ds(modes, 8), :] = jnp.concatenate(
        [force_row, jnp.zeros((7, modes), jnp.float32)], axis=0
    )


def element_stage(arrived3, slot, state, omega, stiff):
    n_el = slot.shape[1]
    modes = arrived3.shape[1] // 3
    comp = jnp.arange(3 * modes) // modes
    state_blocks = jnp.where(
        comp[:, None] == jnp.arange(128)[None, :], jnp.tile(state, 3)[:, None], jnp.zeros((), state.dtype)
    )
    vmem = pltpu.MemorySpace.VMEM if hasattr(pltpu, "MemorySpace") else pltpu.TPUMemorySpace.VMEM
    return pl.pallas_call(
        element_body,
        out_shape=jax.ShapeDtypeStruct((modes + 8, modes), jnp.float32),
        in_specs=[pl.BlockSpec(memory_space=pl.ANY)] + [pl.BlockSpec(memory_space=vmem)] * 4,
        out_specs=pl.BlockSpec(memory_space=vmem),
        scratch_shapes=[
            pltpu.VMEM((24 * n_el, modes), jnp.bfloat16),
            pltpu.VMEM((24 * n_el, modes), jnp.bfloat16),
            pltpu.VMEM(arrived3.shape, arrived3.dtype),
            pltpu.SemaphoreType.DMA((1,)),
        ],
    )(arrived3, slot.reshape(8 * n_el, 1), state_blocks, omega.reshape(n_el, 1), stiff.reshape(n_el, 1))


def gather_body(basis_ref, rows_ref, out_ref):
    nodes = basis_ref.shape[1]
    n_rows = rows_ref.shape[1]
    node = lax.broadcasted_iota(jnp.int32, (nodes, n_rows), 0)
    onehot_t = (node == rows_ref[...]).astype(jnp.bfloat16)
    picked = lax.dot_general(
        onehot_t, basis_ref[0], (((0,), (0,)), ((), ())), preferred_element_type=jnp.float32
    )
    out_ref[...] = picked.astype(jnp.bfloat16)


def gather_rows(by_component, rows):
    comps, nodes, modes = by_component.shape
    n_rows = rows.shape[0]
    return pl.pallas_call(
        gather_body,
        out_shape=jax.ShapeDtypeStruct((n_rows, comps * modes), jnp.bfloat16),
        grid=(comps,),
        in_specs=[
            pl.BlockSpec((1, nodes, modes), lambda c: (c, 0, 0)),
            pl.BlockSpec((1, n_rows), lambda c: (0, 0)),
        ],
        out_specs=pl.BlockSpec((n_rows, modes), lambda c: (0, c)),
    )(by_component, rows.reshape(1, n_rows))

def local(basis, send_rows, elem_slot, set_size, elem_weight, element_stiffening, state, load):
    basis_modes = basis.shape[2]
    n_elem = lax.psum(1, "elem")
    n_blk = lax.psum(1, "blk")
    by_component = jnp.transpose(basis, (1, 0, 2))
    outgoing = gather_rows(by_component, send_rows[0, 0])
    arrived = lax.all_to_all(outgoing, "elem", split_axis=0, concat_axis=0, tiled=True)
    element_count = elem_slot.shape[1]
    set_index = lax.axis_index("elem")
    block_index = lax.axis_index("blk")
    live = lax.dynamic_index_in_dim(set_size, set_index, keepdims=False)
    position = block_index * element_count + jnp.arange(element_count, dtype=jnp.int32)
    weights = jnp.where(position < live, elem_weight, jnp.zeros_like(elem_weight))
    stacked = element_stage(arrived, elem_slot, state, weights, element_stiffening)
    rows = basis_modes // n_elem
    cols = basis_modes // n_blk
    n_y = n_blk // 2
    core = block_index % 2
    chip = block_index // 2
    by_dest = stacked.reshape(basis_modes + 8, n_y, 2, cols)
    pair = [(b, b ^ 1) for b in range(n_blk)]
    sent = lax.dynamic_index_in_dim(by_dest, 1 - core, axis=2, keepdims=False)
    kept = lax.dynamic_index_in_dim(by_dest, core, axis=2, keepdims=False)
    chip_sum = kept + lax.ppermute(sent, "blk", pair)
    halfway = lax.dynamic_index_in_dim(chip_sum, chip, axis=1, keepdims=False)
    for shift in range(1, n_y):
        ring = [(2 * y + c, 2 * ((y + shift) % n_y) + c) for y in range(n_y) for c in range(2)]
        piece = lax.dynamic_index_in_dim(chip_sum, (chip + shift) % n_y, axis=1, keepdims=False)
        halfway = halfway + lax.ppermute(piece, "blk", ring)
    force_cols = halfway[basis_modes]
    tangent_rows = halfway[:basis_modes].reshape(n_elem, rows, cols)
    chunks = jnp.concatenate(
        [tangent_rows, jnp.broadcast_to(force_cols[None, None, :], (n_elem, 1, cols))], axis=1
    )
    arrived_chunks = lax.all_to_all(chunks, "elem", split_axis=0, concat_axis=0, tiled=True)
    mine = jnp.sum(arrived_chunks, axis=0)
    scale = lax.rsqrt(24.0 * jnp.sum(set_size).astype(jnp.float32))
    return (mine[:rows] * scale, mine[rows] * scale - load)


def solution(mesh):
    in_specs = (
        P("elem", None, None),
        P("elem", "blk", None),
        P(None, ("elem", "blk")),
        P(),
        P(("elem", "blk")),
        P(("elem", "blk")),
        P(),
        P("blk"),
    )
    out_specs = (P("elem", "blk"), P("blk"))
    return jax.shard_map(local, mesh=mesh, in_specs=in_specs, out_specs=out_specs, check_vma=False)
```

```python
import jax
import jax.numpy as jnp
from jax import lax
from jax.experimental import pallas as pl
from jax.experimental.pallas import tpu as pltpu
from jax.sharding import PartitionSpec as P

G = [[(2 * ((a >> k) & 1) - 1) * 0.25 for k in range(3)] for a in range(8)]


def element_body(arrived_ref, slot_ref, state_ref, omega_ref, stiff_ref, scale_ref, out_ref, v_ref, w_ref):
    n_el = omega_ref.shape[0]
    n_slot = arrived_ref.shape[0]
    modes = out_ref.shape[1]
    slots = slot_ref[...]
    lane = lax.broadcasted_iota(jnp.int32, (8 * n_el, n_slot), 1)
    onehot = (slots == lane).astype(jnp.bfloat16)
    corners = jnp.dot(onehot, arrived_ref[...], preferred_element_type=jnp.float32).astype(jnp.bfloat16)
    for c in range(3):
        v_ref[pl.ds(c * 8 * n_el, 8 * n_el), :] = corners[:, c * modes:(c + 1) * modes]
    disp_all = jnp.dot(corners, state_ref[...], preferred_element_type=jnp.float32)
    disp = {}
    for a in range(8):
        for c in range(3):
            disp[a, c] = disp_all[a * n_el:(a + 1) * n_el, c:c + 1]
    lane_el = lane[:n_el]
    signed_rows = []
    for k in range(3):
        signed = None
        for a in range(8):
            term = jnp.where(slots[a * n_el:(a + 1) * n_el] == lane_el, G[a][k], 0.0)
            signed = term if signed is None else signed + term
        signed_rows.append(signed)
    signed_all = jnp.concatenate(signed_rows, axis=0).astype(jnp.bfloat16)
    grad_all = jnp.dot(signed_all, arrived_ref[...], preferred_element_type=jnp.float32)
    grad = {}
    for k in range(3):
        for c in range(3):
            grad[k, c] = grad_all[k * n_el:(k + 1) * n_el, c * modes:(c + 1) * modes]

    def corner_rows(a, c):
        return pl.ds(c * 8 * n_el + a * n_el, n_el)

    h = {}
    for k in range(3):
        for c in range(3):
            acc = G[0][k] * disp[0, c]
            for a in range(1, 8):
                acc = acc + G[a][k] * disp[a, c]
            h[k, c] = acc
    stiff = stiff_ref[...]
    omega = omega_ref[...]
    vol = h[0, 0] + h[1, 1] + h[2, 2]
    lam = 1.0 + stiff * vol ** 2 - 2.0 / 3.0
    press = vol + stiff * vol ** 3 / 3.0 - 2.0 / 3.0 * vol
    stress = {}
    for k in range(3):
        for c in range(3):
            s = h[k, c] + h[c, k]
            if k == c:
                s = s + press
            stress[k, c] = s
    force_acc = jnp.zeros((n_el, modes), jnp.float32)
    for a in range(8):
        for c in range(3):
            f = G[a][0] * stress[0, c] + G[a][1] * stress[1, c] + G[a][2] * stress[2, c]
            f = f + 0.25 * disp[a, c]
            wf = (f * omega).astype(jnp.bfloat16).astype(jnp.float32)
            force_acc = force_acc + v_ref[corner_rows(a, c), :].astype(jnp.float32) * wf
    trace = grad[0, 0] + grad[1, 1] + grad[2, 2]
    for a in range(8):
        for c in range(3):
            img = G[a][0] * (grad[0, c] + grad[c, 0])
            img = img + G[a][1] * (grad[1, c] + grad[c, 1])
            img = img + G[a][2] * (grad[2, c] + grad[c, 2])
            img = img + (lam * G[a][c]) * trace
            img = img + 0.25 * v_ref[corner_rows(a, c), :].astype(jnp.float32)
            w_ref[corner_rows(a, c), :] = (omega * img).astype(jnp.bfloat16)
    tangent = lax.dot_general(
        v_ref[...], w_ref[...], (((0,), (0,)), ((), ())), preferred_element_type=jnp.float32
    )
    scale = scale_ref[0:1, 0:1]
    out_ref[pl.ds(0, modes), :] = tangent * scale
    force_row = jnp.sum(force_acc, axis=0, keepdims=True) * scale
    out_ref[pl.ds(modes, 8), :] = jnp.concatenate(
        [force_row, jnp.zeros((7, modes), jnp.float32)], axis=0
    )


def element_stage(arrived3, slot, state, omega, stiff, scale):
    n_el = slot.shape[1]
    modes = arrived3.shape[1] // 3
    comp = jnp.arange(3 * modes) // modes
    state_blocks = jnp.where(
        comp[:, None] == jnp.arange(128)[None, :], jnp.tile(state, 3)[:, None], jnp.zeros((), state.dtype)
    )
    vmem = pltpu.MemorySpace.VMEM if hasattr(pltpu, "MemorySpace") else pltpu.TPUMemorySpace.VMEM
    return pl.pallas_call(
        element_body,
        out_shape=jax.ShapeDtypeStruct((modes + 8, modes), jnp.float32),
        in_specs=[pl.BlockSpec(memory_space=vmem)] * 6,
        out_specs=pl.BlockSpec(memory_space=vmem),
        scratch_shapes=[
            pltpu.VMEM((24 * n_el, modes), jnp.bfloat16),
            pltpu.VMEM((24 * n_el, modes), jnp.bfloat16),
        ],
    )(arrived3, slot.reshape(8 * n_el, 1), state_blocks, omega.reshape(n_el, 1), stiff.reshape(n_el, 1),
      jnp.broadcast_to(scale, (8, 128)))


def gather_body(basis_ref, rows_ref, out_ref):
    nodes = basis_ref.shape[1]
    n_rows = rows_ref.shape[1]
    node = lax.broadcasted_iota(jnp.int32, (nodes, n_rows), 0)
    onehot_t = (node == rows_ref[...]).astype(jnp.bfloat16)
    picked = lax.dot_general(
        onehot_t, basis_ref[0], (((0,), (0,)), ((), ())), preferred_element_type=jnp.float32
    )
    out_ref[...] = picked.astype(jnp.bfloat16)


def gather_rows(by_component, rows):
    comps, nodes, modes = by_component.shape
    n_rows = rows.shape[0]
    return pl.pallas_call(
        gather_body,
        out_shape=jax.ShapeDtypeStruct((n_rows, comps * modes), jnp.bfloat16),
        grid=(comps,),
        in_specs=[
            pl.BlockSpec((1, nodes, modes), lambda c: (c, 0, 0)),
            pl.BlockSpec((1, n_rows), lambda c: (0, 0)),
        ],
        out_specs=pl.BlockSpec((n_rows, modes), lambda c: (0, c)),
    )(by_component, rows.reshape(1, n_rows))

def local(basis, send_rows, elem_slot, set_size, elem_weight, element_stiffening, state, load):
    basis_modes = basis.shape[2]
    n_elem = lax.psum(1, "elem")
    n_blk = lax.psum(1, "blk")
    by_component = jnp.transpose(basis, (1, 0, 2))
    outgoing = gather_rows(by_component, send_rows[0, 0])
    arrived = lax.all_to_all(outgoing, "elem", split_axis=0, concat_axis=0, tiled=True)
    element_count = elem_slot.shape[1]
    set_index = lax.axis_index("elem")
    block_index = lax.axis_index("blk")
    live = lax.dynamic_index_in_dim(set_size, set_index, keepdims=False)
    position = block_index * element_count + jnp.arange(element_count, dtype=jnp.int32)
    weights = jnp.where(position < live, elem_weight, jnp.zeros_like(elem_weight))
    scale = lax.rsqrt(24.0 * jnp.sum(set_size).astype(jnp.float32))
    stacked = element_stage(arrived, elem_slot, state, weights, element_stiffening, scale)
    rows = basis_modes // n_elem
    cols = basis_modes // n_blk
    n_y = n_blk // 2
    core = block_index % 2
    chip = block_index // 2
    by_dest = stacked.reshape(basis_modes + 8, n_y, 2, cols)
    pair = [(b, b ^ 1) for b in range(n_blk)]
    sent = lax.dynamic_index_in_dim(by_dest, 1 - core, axis=2, keepdims=False)
    kept = lax.dynamic_index_in_dim(by_dest, core, axis=2, keepdims=False)
    chip_sum = kept + lax.ppermute(sent, "blk", pair)
    halfway = lax.dynamic_index_in_dim(chip_sum, chip, axis=1, keepdims=False)
    for shift in range(1, n_y):
        ring = [(2 * y + c, 2 * ((y + shift) % n_y) + c) for y in range(n_y) for c in range(2)]
        piece = lax.dynamic_index_in_dim(chip_sum, (chip + shift) % n_y, axis=1, keepdims=False)
        halfway = halfway + lax.ppermute(piece, "blk", ring)
    force_cols = halfway[basis_modes] - jnp.where(set_index == 0, load, jnp.zeros_like(load))
    tangent_rows = halfway[:basis_modes].reshape(n_elem, rows, cols)
    chunks = jnp.concatenate(
        [tangent_rows, jnp.broadcast_to(force_cols[None, None, :], (n_elem, 1, cols))], axis=1
    )
    arrived_chunks = lax.all_to_all(chunks, "elem", split_axis=0, concat_axis=0, tiled=True)
    mine = jnp.sum(arrived_chunks, axis=0)
    return (mine[:rows], mine[rows])


def solution(mesh):
    in_specs = (
        P("elem", None, None),
        P("elem", "blk", None),
        P(None, ("elem", "blk")),
        P(),
        P(("elem", "blk")),
        P(("elem", "blk")),
        P(),
        P("blk"),
    )
    out_specs = (P("elem", "blk"), P("blk"))
    return jax.shard_map(local, mesh=mesh, in_specs=in_specs, out_specs=out_specs, check_vma=False)
```

```python
import jax
import jax.numpy as jnp
from jax import lax
from jax.experimental import pallas as pl
from jax.experimental.pallas import tpu as pltpu
from jax.sharding import PartitionSpec as P

G = [[(2 * ((a >> k) & 1) - 1) * 0.25 for k in range(3)] for a in range(8)]


def element_body(arrived_ref, slot_ref, state_ref, omega_ref, stiff_ref, scale_ref, out_ref, v_ref, w_ref):
    n_el = omega_ref.shape[0]
    n_slot = arrived_ref.shape[0]
    modes = out_ref.shape[1]
    slots = slot_ref[...]
    lane = lax.broadcasted_iota(jnp.int32, (8 * n_el, n_slot), 1)
    onehot = (slots == lane).astype(jnp.bfloat16)
    corners = jnp.dot(onehot, arrived_ref[...], preferred_element_type=jnp.float32).astype(jnp.bfloat16)
    for c in range(3):
        v_ref[pl.ds(c * 8 * n_el, 8 * n_el), :] = corners[:, c * modes:(c + 1) * modes]
    disp_all = jnp.dot(corners, state_ref[...], preferred_element_type=jnp.float32)
    disp = {}
    for a in range(8):
        for c in range(3):
            disp[a, c] = disp_all[a * n_el:(a + 1) * n_el, c:c + 1]
    lane_el = lane[:n_el]
    signed_rows = []
    for k in range(3):
        signed = None
        for a in range(8):
            term = jnp.where(slots[a * n_el:(a + 1) * n_el] == lane_el, G[a][k], 0.0)
            signed = term if signed is None else signed + term
        signed_rows.append(signed)
    signed_all = jnp.concatenate(signed_rows, axis=0).astype(jnp.bfloat16)
    grad_all = jnp.dot(signed_all, arrived_ref[...], preferred_element_type=jnp.float32)
    grad = {}
    for k in range(3):
        for c in range(3):
            grad[k, c] = grad_all[k * n_el:(k + 1) * n_el, c * modes:(c + 1) * modes]

    def corner_rows(a, c):
        return pl.ds(c * 8 * n_el + a * n_el, n_el)

    h = {}
    for k in range(3):
        for c in range(3):
            acc = G[0][k] * disp[0, c]
            for a in range(1, 8):
                acc = acc + G[a][k] * disp[a, c]
            h[k, c] = acc
    stiff = stiff_ref[...]
    omega = omega_ref[...]
    vol = h[0, 0] + h[1, 1] + h[2, 2]
    lam = 1.0 + stiff * vol ** 2 - 2.0 / 3.0
    press = vol + stiff * vol ** 3 / 3.0 - 2.0 / 3.0 * vol
    stress = {}
    for k in range(3):
        for c in range(3):
            s = h[k, c] + h[c, k]
            if k == c:
                s = s + press
            stress[k, c] = s
    force_acc = jnp.zeros((n_el, modes), jnp.float32)
    for a in range(8):
        for c in range(3):
            f = G[a][0] * stress[0, c] + G[a][1] * stress[1, c] + G[a][2] * stress[2, c]
            f = f + 0.25 * disp[a, c]
            wf = (f * omega).astype(jnp.bfloat16).astype(jnp.float32)
            force_acc = force_acc + v_ref[corner_rows(a, c), :].astype(jnp.float32) * wf
    trace = grad[0, 0] + grad[1, 1] + grad[2, 2]
    for a in range(8):
        for c in range(3):
            img = G[a][0] * (grad[0, c] + grad[c, 0])
            img = img + G[a][1] * (grad[1, c] + grad[c, 1])
            img = img + G[a][2] * (grad[2, c] + grad[c, 2])
            img = img + (lam * G[a][c]) * trace
            img = img + 0.25 * v_ref[corner_rows(a, c), :].astype(jnp.float32)
            w_ref[corner_rows(a, c), :] = (omega * img).astype(jnp.bfloat16)
    tangent = lax.dot_general(
        v_ref[...], w_ref[...], (((0,), (0,)), ((), ())), preferred_element_type=jnp.float32
    )
    scale = scale_ref[0:1, 0:1]
    out_ref[pl.ds(0, modes), :] = tangent * scale
    force_row = jnp.sum(force_acc, axis=0, keepdims=True) * scale
    out_ref[pl.ds(modes, 8), :] = jnp.concatenate(
        [force_row, jnp.zeros((7, modes), jnp.float32)], axis=0
    )


def element_stage(arrived3, slot, state, omega, stiff, scale):
    n_el = slot.shape[1]
    modes = arrived3.shape[1] // 3
    comp = jnp.arange(3 * modes) // modes
    state_blocks = jnp.where(
        comp[:, None] == jnp.arange(128)[None, :], jnp.tile(state, 3)[:, None], jnp.zeros((), state.dtype)
    )
    vmem = pltpu.MemorySpace.VMEM if hasattr(pltpu, "MemorySpace") else pltpu.TPUMemorySpace.VMEM
    return pl.pallas_call(
        element_body,
        out_shape=jax.ShapeDtypeStruct((modes + 8, modes), jnp.float32),
        in_specs=[pl.BlockSpec(memory_space=vmem)] * 6,
        out_specs=pl.BlockSpec(memory_space=vmem),
        scratch_shapes=[
            pltpu.VMEM((24 * n_el, modes), jnp.bfloat16),
            pltpu.VMEM((24 * n_el, modes), jnp.bfloat16),
        ],
    )(arrived3, slot.reshape(8 * n_el, 1), state_blocks, omega.reshape(n_el, 1), stiff.reshape(n_el, 1),
      jnp.broadcast_to(scale, (8, 128)))


def gather_body(basis_ref, rows_ref, out_ref):
    nodes = basis_ref.shape[1]
    n_rows = rows_ref.shape[1]
    node = lax.broadcasted_iota(jnp.int32, (nodes, n_rows), 0)
    onehot_t = (node == rows_ref[...]).astype(jnp.bfloat16)
    picked = lax.dot_general(
        onehot_t, basis_ref[0], (((0,), (0,)), ((), ())), preferred_element_type=jnp.float32
    )
    out_ref[...] = picked.astype(jnp.bfloat16)


def gather_rows(by_component, rows):
    comps, nodes, modes = by_component.shape
    n_rows = rows.shape[0]
    return pl.pallas_call(
        gather_body,
        out_shape=jax.ShapeDtypeStruct((n_rows, comps * modes), jnp.bfloat16),
        grid=(comps,),
        in_specs=[
            pl.BlockSpec((1, nodes, modes), lambda c: (c, 0, 0)),
            pl.BlockSpec((1, n_rows), lambda c: (0, 0)),
        ],
        out_specs=pl.BlockSpec((n_rows, modes), lambda c: (0, c)),
    )(by_component, rows.reshape(1, n_rows))

def local(basis, send_rows, elem_slot, set_size, elem_weight, element_stiffening, state, load):
    basis_modes = basis.shape[2]
    n_elem = lax.psum(1, "elem")
    n_blk = lax.psum(1, "blk")
    by_component = jnp.transpose(basis, (1, 0, 2))
    outgoing = gather_rows(by_component, send_rows[0, 0])
    arrived = lax.all_to_all(outgoing, "elem", split_axis=0, concat_axis=0, tiled=True)
    element_count = elem_slot.shape[1]
    set_index = lax.axis_index("elem")
    block_index = lax.axis_index("blk")
    live = lax.dynamic_index_in_dim(set_size, set_index, keepdims=False)
    position = block_index * element_count + jnp.arange(element_count, dtype=jnp.int32)
    weights = jnp.where(position < live, elem_weight, jnp.zeros_like(elem_weight))
    scale = lax.rsqrt(24.0 * jnp.sum(set_size).astype(jnp.float32))
    stacked = element_stage(arrived, elem_slot, state, weights, element_stiffening, scale)
    rows = basis_modes // n_elem
    cols = basis_modes // n_blk
    n_y = n_blk // 2
    core = block_index % 2
    chip = block_index // 2
    by_dest = stacked.reshape(basis_modes + 8, n_y, 2, cols)
    pair = [(b, b ^ 1) for b in range(n_blk)]
    sent = lax.dynamic_index_in_dim(by_dest, 1 - core, axis=2, keepdims=False)
    kept = lax.dynamic_index_in_dim(by_dest, core, axis=2, keepdims=False)
    chip_sum = kept + lax.ppermute(sent, "blk", pair)
    halfway = lax.dynamic_index_in_dim(chip_sum, chip, axis=1, keepdims=False)
    for shift in range(1, n_y):
        ring = [(2 * y + c, 2 * ((y + shift) % n_y) + c) for y in range(n_y) for c in range(2)]
        piece = lax.dynamic_index_in_dim(chip_sum, (chip + shift) % n_y, axis=1, keepdims=False)
        halfway = halfway + lax.ppermute(piece, "blk", ring)
    force_cols = halfway[basis_modes] - jnp.where(set_index == 0, load, jnp.zeros_like(load))
    tangent_rows = halfway[:basis_modes].reshape(n_elem, rows, cols)
    chunks = jnp.concatenate(
        [tangent_rows, jnp.broadcast_to(force_cols[None, None, :], (n_elem, 1, cols))], axis=1
    )
    flat = chunks.reshape(n_elem, (rows + 1) * cols)
    arrived_chunks = lax.all_to_all(flat, "elem", split_axis=0, concat_axis=0, tiled=True)
    mine = jnp.sum(arrived_chunks, axis=0).reshape(rows + 1, cols)
    return (mine[:rows], mine[rows])


def solution(mesh):
    in_specs = (
        P("elem", None, None),
        P("elem", "blk", None),
        P(None, ("elem", "blk")),
        P(),
        P(("elem", "blk")),
        P(("elem", "blk")),
        P(),
        P("blk"),
    )
    out_specs = (P("elem", "blk"), P("blk"))
    return jax.shard_map(local, mesh=mesh, in_specs=in_specs, out_specs=out_specs, check_vma=False)
```

```python
import jax
import jax.numpy as jnp
from jax import lax
from jax.experimental import pallas as pl
from jax.experimental.pallas import tpu as pltpu
from jax.sharding import PartitionSpec as P

G = [[(2 * ((a >> k) & 1) - 1) * 0.25 for k in range(3)] for a in range(8)]


def element_body(arrived_ref, slot_ref, state_ref, omega_ref, stiff_ref, scale_ref, out_ref, v_ref, w_ref):
    n_el = omega_ref.shape[0]
    n_slot = arrived_ref.shape[0]
    modes = out_ref.shape[1]
    slots = slot_ref[...]
    lane = lax.broadcasted_iota(jnp.int32, (8 * n_el, n_slot), 1)
    onehot = (slots == lane).astype(jnp.bfloat16)
    corners = jnp.dot(onehot, arrived_ref[...], preferred_element_type=jnp.float32).astype(jnp.bfloat16)
    for c in range(3):
        v_ref[pl.ds(c * 8 * n_el, 8 * n_el), :] = corners[:, c * modes:(c + 1) * modes]
    disp_all = jnp.dot(corners, state_ref[...], preferred_element_type=jnp.float32)
    disp = {}
    for a in range(8):
        for c in range(3):
            disp[a, c] = disp_all[a * n_el:(a + 1) * n_el, c:c + 1]
    lane_el = lane[:n_el]
    signed_rows = []
    for k in range(3):
        signed = None
        for a in range(8):
            term = jnp.where(slots[a * n_el:(a + 1) * n_el] == lane_el, G[a][k], 0.0)
            signed = term if signed is None else signed + term
        signed_rows.append(signed)
    signed_all = jnp.concatenate(signed_rows, axis=0).astype(jnp.bfloat16)
    grad_all = jnp.dot(signed_all, arrived_ref[...], preferred_element_type=jnp.float32)
    grad = {}
    for k in range(3):
        for c in range(3):
            grad[k, c] = grad_all[k * n_el:(k + 1) * n_el, c * modes:(c + 1) * modes]

    def corner_rows(a, c):
        return pl.ds(c * 8 * n_el + a * n_el, n_el)

    h = {}
    for k in range(3):
        for c in range(3):
            acc = G[0][k] * disp[0, c]
            for a in range(1, 8):
                acc = acc + G[a][k] * disp[a, c]
            h[k, c] = acc
    stiff = stiff_ref[...]
    omega = omega_ref[...]
    vol = h[0, 0] + h[1, 1] + h[2, 2]
    lam = 1.0 + stiff * vol ** 2 - 2.0 / 3.0
    press = vol + stiff * vol ** 3 / 3.0 - 2.0 / 3.0 * vol
    stress = {}
    for k in range(3):
        for c in range(3):
            s = h[k, c] + h[c, k]
            if k == c:
                s = s + press
            stress[k, c] = s
    force_acc = jnp.zeros((n_el, modes), jnp.float32)
    for a in range(8):
        for c in range(3):
            f = G[a][0] * stress[0, c] + G[a][1] * stress[1, c] + G[a][2] * stress[2, c]
            f = f + 0.25 * disp[a, c]
            wf = (f * omega).astype(jnp.bfloat16).astype(jnp.float32)
            force_acc = force_acc + v_ref[corner_rows(a, c), :].astype(jnp.float32) * wf
    trace = grad[0, 0] + grad[1, 1] + grad[2, 2]
    for a in range(8):
        for c in range(3):
            img = G[a][0] * (grad[0, c] + grad[c, 0])
            img = img + G[a][1] * (grad[1, c] + grad[c, 1])
            img = img + G[a][2] * (grad[2, c] + grad[c, 2])
            img = img + (lam * G[a][c]) * trace
            img = img + 0.25 * v_ref[corner_rows(a, c), :].astype(jnp.float32)
            w_ref[corner_rows(a, c), :] = (omega * img).astype(jnp.bfloat16)
    tangent = lax.dot_general(
        v_ref[...], w_ref[...], (((0,), (0,)), ((), ())), preferred_element_type=jnp.float32
    )
    scale = scale_ref[0:1, 0:1]
    out_ref[pl.ds(0, modes), :] = tangent * scale
    force_row = jnp.sum(force_acc, axis=0, keepdims=True) * scale
    out_ref[pl.ds(modes, 8), :] = jnp.concatenate(
        [force_row, jnp.zeros((7, modes), jnp.float32)], axis=0
    )


def element_stage(arrived3, slot, state, omega, stiff, scale):
    n_el = slot.shape[1]
    modes = arrived3.shape[1] // 3
    comp = jnp.arange(3 * modes) // modes
    state_blocks = jnp.where(
        comp[:, None] == jnp.arange(128)[None, :], jnp.tile(state, 3)[:, None], jnp.zeros((), state.dtype)
    )
    vmem = pltpu.MemorySpace.VMEM if hasattr(pltpu, "MemorySpace") else pltpu.TPUMemorySpace.VMEM
    return pl.pallas_call(
        element_body,
        out_shape=jax.ShapeDtypeStruct((modes + 8, modes), jnp.float32),
        in_specs=[pl.BlockSpec(memory_space=vmem)] * 6,
        out_specs=pl.BlockSpec(memory_space=vmem),
        scratch_shapes=[
            pltpu.VMEM((24 * n_el, modes), jnp.bfloat16),
            pltpu.VMEM((24 * n_el, modes), jnp.bfloat16),
        ],
    )(arrived3, slot.reshape(8 * n_el, 1), state_blocks, omega.reshape(n_el, 1), stiff.reshape(n_el, 1),
      jnp.broadcast_to(scale, (8, 128)))


def gather_body(basis_ref, rows_ref, out_ref):
    comps, nodes, modes = basis_ref.shape
    n_rows = rows_ref.shape[1]
    node = lax.broadcasted_iota(jnp.int32, (nodes, n_rows), 0)
    onehot_t = (node == rows_ref[...]).astype(jnp.bfloat16)
    for c in range(comps):
        picked = lax.dot_general(
            onehot_t, basis_ref[c], (((0,), (0,)), ((), ())), preferred_element_type=jnp.float32
        )
        out_ref[:, pl.ds(c * modes, modes)] = picked.astype(jnp.bfloat16)


def gather_rows(by_component, rows):
    comps, nodes, modes = by_component.shape
    n_rows = rows.shape[0]
    vmem = pltpu.MemorySpace.VMEM if hasattr(pltpu, "MemorySpace") else pltpu.TPUMemorySpace.VMEM
    return pl.pallas_call(
        gather_body,
        out_shape=jax.ShapeDtypeStruct((n_rows, comps * modes), jnp.bfloat16),
        in_specs=[pl.BlockSpec(memory_space=vmem)] * 2,
        out_specs=pl.BlockSpec(memory_space=vmem),
    )(by_component, rows.reshape(1, n_rows))

def local(basis, send_rows, elem_slot, set_size, elem_weight, element_stiffening, state, load):
    basis_modes = basis.shape[2]
    n_elem = lax.psum(1, "elem")
    n_blk = lax.psum(1, "blk")
    by_component = jnp.transpose(basis, (1, 0, 2))
    outgoing = gather_rows(by_component, send_rows[0, 0])
    arrived = lax.all_to_all(outgoing, "elem", split_axis=0, concat_axis=0, tiled=True)
    element_count = elem_slot.shape[1]
    set_index = lax.axis_index("elem")
    block_index = lax.axis_index("blk")
    live = lax.dynamic_index_in_dim(set_size, set_index, keepdims=False)
    position = block_index * element_count + jnp.arange(element_count, dtype=jnp.int32)
    weights = jnp.where(position < live, elem_weight, jnp.zeros_like(elem_weight))
    scale = lax.rsqrt(24.0 * jnp.sum(set_size).astype(jnp.float32))
    stacked = element_stage(arrived, elem_slot, state, weights, element_stiffening, scale)
    rows = basis_modes // n_elem
    cols = basis_modes // n_blk
    n_y = n_blk // 2
    core = block_index % 2
    chip = block_index // 2
    by_dest = stacked.reshape(basis_modes + 8, n_y, 2, cols)
    pair = [(b, b ^ 1) for b in range(n_blk)]
    sent = lax.dynamic_index_in_dim(by_dest, 1 - core, axis=2, keepdims=False)
    kept = lax.dynamic_index_in_dim(by_dest, core, axis=2, keepdims=False)
    chip_sum = kept + lax.ppermute(sent, "blk", pair)
    halfway = lax.dynamic_index_in_dim(chip_sum, chip, axis=1, keepdims=False)
    for shift in range(1, n_y):
        ring = [(2 * y + c, 2 * ((y + shift) % n_y) + c) for y in range(n_y) for c in range(2)]
        piece = lax.dynamic_index_in_dim(chip_sum, (chip + shift) % n_y, axis=1, keepdims=False)
        halfway = halfway + lax.ppermute(piece, "blk", ring)
    force_cols = halfway[basis_modes] - jnp.where(set_index == 0, load, jnp.zeros_like(load))
    tangent_rows = halfway[:basis_modes].reshape(n_elem, rows, cols)
    chunks = jnp.concatenate(
        [tangent_rows, jnp.broadcast_to(force_cols[None, None, :], (n_elem, 1, cols))], axis=1
    )
    flat = chunks.reshape(n_elem, (rows + 1) * cols)
    arrived_chunks = lax.all_to_all(flat, "elem", split_axis=0, concat_axis=0, tiled=True)
    mine = jnp.sum(arrived_chunks, axis=0).reshape(rows + 1, cols)
    return (mine[:rows], mine[rows])


def solution(mesh):
    in_specs = (
        P("elem", None, None),
        P("elem", "blk", None),
        P(None, ("elem", "blk")),
        P(),
        P(("elem", "blk")),
        P(("elem", "blk")),
        P(),
        P("blk"),
    )
    out_specs = (P("elem", "blk"), P("blk"))
    return jax.shard_map(local, mesh=mesh, in_specs=in_specs, out_specs=out_specs, check_vma=False)
```

```python
import jax
import jax.numpy as jnp
from jax import lax
from jax.experimental import pallas as pl
from jax.experimental.pallas import tpu as pltpu
from jax.sharding import PartitionSpec as P

G = [[(2 * ((a >> k) & 1) - 1) * 0.25 for k in range(3)] for a in range(8)]


def element_body(arrived_ref, slot_ref, state_ref, omega_ref, stiff_ref, scale_ref, out_ref, v_ref, w_ref):
    n_el = omega_ref.shape[0]
    n_slot = arrived_ref.shape[0]
    modes = out_ref.shape[1]
    slots = slot_ref[...]
    lane = lax.broadcasted_iota(jnp.int32, (8 * n_el, n_slot), 1)
    onehot = (slots == lane).astype(jnp.bfloat16)
    corners = jnp.dot(onehot, arrived_ref[...], preferred_element_type=jnp.float32).astype(jnp.bfloat16)
    for c in range(3):
        v_ref[pl.ds(c * 8 * n_el, 8 * n_el), :] = corners[:, c * modes:(c + 1) * modes]
    disp_all = jnp.dot(corners, state_ref[...], preferred_element_type=jnp.float32)
    disp = {}
    for a in range(8):
        for c in range(3):
            disp[a, c] = disp_all[a * n_el:(a + 1) * n_el, c:c + 1]
    lane_el = lane[:n_el]
    signed_rows = []
    for k in range(3):
        signed = None
        for a in range(8):
            term = jnp.where(slots[a * n_el:(a + 1) * n_el] == lane_el, G[a][k], 0.0)
            signed = term if signed is None else signed + term
        signed_rows.append(signed)
    signed_all = jnp.concatenate(signed_rows, axis=0).astype(jnp.bfloat16)
    grad_all = jnp.dot(signed_all, arrived_ref[...], preferred_element_type=jnp.float32)
    grad = {}
    for k in range(3):
        for c in range(3):
            grad[k, c] = grad_all[k * n_el:(k + 1) * n_el, c * modes:(c + 1) * modes]

    def corner_rows(a, c):
        return pl.ds(c * 8 * n_el + a * n_el, n_el)

    h = {}
    for k in range(3):
        for c in range(3):
            acc = G[0][k] * disp[0, c]
            for a in range(1, 8):
                acc = acc + G[a][k] * disp[a, c]
            h[k, c] = acc
    stiff = stiff_ref[...]
    omega = omega_ref[...]
    vol = h[0, 0] + h[1, 1] + h[2, 2]
    lam = 1.0 + stiff * vol ** 2 - 2.0 / 3.0
    press = vol + stiff * vol ** 3 / 3.0 - 2.0 / 3.0 * vol
    stress = {}
    for k in range(3):
        for c in range(3):
            s = h[k, c] + h[c, k]
            if k == c:
                s = s + press
            stress[k, c] = s
    force_acc = jnp.zeros((n_el, modes), jnp.float32)
    for a in range(8):
        for c in range(3):
            f = G[a][0] * stress[0, c] + G[a][1] * stress[1, c] + G[a][2] * stress[2, c]
            f = f + 0.25 * disp[a, c]
            wf = (f * omega).astype(jnp.bfloat16).astype(jnp.float32)
            force_acc = force_acc + v_ref[corner_rows(a, c), :].astype(jnp.float32) * wf
    trace = grad[0, 0] + grad[1, 1] + grad[2, 2]
    for a in range(8):
        for c in range(3):
            img = G[a][0] * (grad[0, c] + grad[c, 0])
            img = img + G[a][1] * (grad[1, c] + grad[c, 1])
            img = img + G[a][2] * (grad[2, c] + grad[c, 2])
            img = img + (lam * G[a][c]) * trace
            img = img + 0.25 * v_ref[corner_rows(a, c), :].astype(jnp.float32)
            w_ref[corner_rows(a, c), :] = (omega * img).astype(jnp.bfloat16)
    tangent = lax.dot_general(
        v_ref[...], w_ref[...], (((0,), (0,)), ((), ())), preferred_element_type=jnp.float32
    )
    scale = scale_ref[0:1, 0:1]
    out_ref[pl.ds(0, modes), :] = tangent * scale
    force_row = jnp.sum(force_acc, axis=0, keepdims=True) * scale
    out_ref[pl.ds(modes, 8), :] = jnp.concatenate(
        [force_row, jnp.zeros((7, modes), jnp.float32)], axis=0
    )


def element_stage(arrived3, slot, state, omega, stiff, scale):
    n_el = slot.shape[1]
    modes = arrived3.shape[1] // 3
    comp = jnp.arange(3 * modes) // modes
    state_blocks = jnp.where(
        comp[:, None] == jnp.arange(128)[None, :], jnp.tile(state, 3)[:, None], jnp.zeros((), state.dtype)
    )
    vmem = pltpu.MemorySpace.VMEM if hasattr(pltpu, "MemorySpace") else pltpu.TPUMemorySpace.VMEM
    return pl.pallas_call(
        element_body,
        out_shape=jax.ShapeDtypeStruct((modes + 8, modes), jnp.float32),
        in_specs=[pl.BlockSpec(memory_space=vmem)] * 6,
        out_specs=pl.BlockSpec(memory_space=vmem),
        scratch_shapes=[
            pltpu.VMEM((24 * n_el, modes), jnp.bfloat16),
            pltpu.VMEM((24 * n_el, modes), jnp.bfloat16),
        ],
    )(arrived3, slot.reshape(8 * n_el, 1), state_blocks, omega.reshape(n_el, 1), stiff.reshape(n_el, 1),
      jnp.broadcast_to(scale, (8, 128)))


def gather_body(basis_ref, rows_ref, out_ref):
    comps, nodes, modes = basis_ref.shape
    n_rows = rows_ref.shape[1]
    rows_col = jnp.transpose(jnp.broadcast_to(rows_ref[...], (8, n_rows)))[:, 0:1]
    node = lax.broadcasted_iota(jnp.int32, (n_rows, nodes), 1)
    onehot = (rows_col == node).astype(jnp.bfloat16)
    for c in range(comps):
        picked = jnp.dot(onehot, basis_ref[c], preferred_element_type=jnp.float32)
        out_ref[:, pl.ds(c * modes, modes)] = picked.astype(jnp.bfloat16)


def gather_rows(by_component, rows):
    comps, nodes, modes = by_component.shape
    n_rows = rows.shape[0]
    vmem = pltpu.MemorySpace.VMEM if hasattr(pltpu, "MemorySpace") else pltpu.TPUMemorySpace.VMEM
    return pl.pallas_call(
        gather_body,
        out_shape=jax.ShapeDtypeStruct((n_rows, comps * modes), jnp.bfloat16),
        in_specs=[pl.BlockSpec(memory_space=vmem)] * 2,
        out_specs=pl.BlockSpec(memory_space=vmem),
    )(by_component, rows.reshape(1, n_rows))

def local(basis, send_rows, elem_slot, set_size, elem_weight, element_stiffening, state, load):
    basis_modes = basis.shape[2]
    n_elem = lax.psum(1, "elem")
    n_blk = lax.psum(1, "blk")
    by_component = jnp.transpose(basis, (1, 0, 2))
    outgoing = gather_rows(by_component, send_rows[0, 0])
    arrived = lax.all_to_all(outgoing, "elem", split_axis=0, concat_axis=0, tiled=True)
    element_count = elem_slot.shape[1]
    set_index = lax.axis_index("elem")
    block_index = lax.axis_index("blk")
    live = lax.dynamic_index_in_dim(set_size, set_index, keepdims=False)
    position = block_index * element_count + jnp.arange(element_count, dtype=jnp.int32)
    weights = jnp.where(position < live, elem_weight, jnp.zeros_like(elem_weight))
    scale = lax.rsqrt(24.0 * jnp.sum(set_size).astype(jnp.float32))
    stacked = element_stage(arrived, elem_slot, state, weights, element_stiffening, scale)
    rows = basis_modes // n_elem
    cols = basis_modes // n_blk
    n_y = n_blk // 2
    core = block_index % 2
    chip = block_index // 2
    by_dest = stacked.reshape(basis_modes + 8, n_y, 2, cols)
    pair = [(b, b ^ 1) for b in range(n_blk)]
    sent = lax.dynamic_index_in_dim(by_dest, 1 - core, axis=2, keepdims=False)
    kept = lax.dynamic_index_in_dim(by_dest, core, axis=2, keepdims=False)
    chip_sum = kept + lax.ppermute(sent, "blk", pair)
    halfway = lax.dynamic_index_in_dim(chip_sum, chip, axis=1, keepdims=False)
    for shift in range(1, n_y):
        ring = [(2 * y + c, 2 * ((y + shift) % n_y) + c) for y in range(n_y) for c in range(2)]
        piece = lax.dynamic_index_in_dim(chip_sum, (chip + shift) % n_y, axis=1, keepdims=False)
        halfway = halfway + lax.ppermute(piece, "blk", ring)
    force_cols = halfway[basis_modes] - jnp.where(set_index == 0, load, jnp.zeros_like(load))
    tangent_rows = halfway[:basis_modes].reshape(n_elem, rows, cols)
    chunks = jnp.concatenate(
        [tangent_rows, jnp.broadcast_to(force_cols[None, None, :], (n_elem, 1, cols))], axis=1
    )
    flat = chunks.reshape(n_elem, (rows + 1) * cols)
    arrived_chunks = lax.all_to_all(flat, "elem", split_axis=0, concat_axis=0, tiled=True)
    mine = jnp.sum(arrived_chunks, axis=0).reshape(rows + 1, cols)
    return (mine[:rows], mine[rows])


def solution(mesh):
    in_specs = (
        P("elem", None, None),
        P("elem", "blk", None),
        P(None, ("elem", "blk")),
        P(),
        P(("elem", "blk")),
        P(("elem", "blk")),
        P(),
        P("blk"),
    )
    out_specs = (P("elem", "blk"), P("blk"))
    return jax.shard_map(local, mesh=mesh, in_specs=in_specs, out_specs=out_specs, check_vma=False)
```

```python
import jax
import jax.numpy as jnp
from jax import lax
from jax.experimental import pallas as pl
from jax.experimental.pallas import tpu as pltpu
from jax.sharding import PartitionSpec as P

G = [[(2 * ((a >> k) & 1) - 1) * 0.25 for k in range(3)] for a in range(8)]


def element_body(arrived_ref, onehot_ref, signed_ref, state_ref, omega_ref, stiff_ref, scale_ref, out_ref, v_ref, w_ref):
    n_el = omega_ref.shape[0]
    modes = out_ref.shape[1]
    onehot = onehot_ref[...]
    corners = jnp.dot(onehot, arrived_ref[...], preferred_element_type=jnp.float32).astype(jnp.bfloat16)
    for c in range(3):
        v_ref[pl.ds(c * 8 * n_el, 8 * n_el), :] = corners[:, c * modes:(c + 1) * modes]
    disp_all = jnp.dot(corners, state_ref[...], preferred_element_type=jnp.float32)
    disp = {}
    for a in range(8):
        for c in range(3):
            disp[a, c] = disp_all[a * n_el:(a + 1) * n_el, c:c + 1]
    signed_all = signed_ref[...]
    grad_all = jnp.dot(signed_all, arrived_ref[...], preferred_element_type=jnp.float32)
    grad = {}
    for k in range(3):
        for c in range(3):
            grad[k, c] = grad_all[k * n_el:(k + 1) * n_el, c * modes:(c + 1) * modes]

    def corner_rows(a, c):
        return pl.ds(c * 8 * n_el + a * n_el, n_el)

    h = {}
    for k in range(3):
        for c in range(3):
            acc = G[0][k] * disp[0, c]
            for a in range(1, 8):
                acc = acc + G[a][k] * disp[a, c]
            h[k, c] = acc
    stiff = stiff_ref[...]
    omega = omega_ref[...]
    vol = h[0, 0] + h[1, 1] + h[2, 2]
    lam = 1.0 + stiff * vol ** 2 - 2.0 / 3.0
    press = vol + stiff * vol ** 3 / 3.0 - 2.0 / 3.0 * vol
    stress = {}
    for k in range(3):
        for c in range(3):
            s = h[k, c] + h[c, k]
            if k == c:
                s = s + press
            stress[k, c] = s
    force_acc = jnp.zeros((n_el, modes), jnp.float32)
    for a in range(8):
        for c in range(3):
            f = G[a][0] * stress[0, c] + G[a][1] * stress[1, c] + G[a][2] * stress[2, c]
            f = f + 0.25 * disp[a, c]
            wf = (f * omega).astype(jnp.bfloat16).astype(jnp.float32)
            force_acc = force_acc + v_ref[corner_rows(a, c), :].astype(jnp.float32) * wf
    trace = grad[0, 0] + grad[1, 1] + grad[2, 2]
    for a in range(8):
        for c in range(3):
            img = G[a][0] * (grad[0, c] + grad[c, 0])
            img = img + G[a][1] * (grad[1, c] + grad[c, 1])
            img = img + G[a][2] * (grad[2, c] + grad[c, 2])
            img = img + (lam * G[a][c]) * trace
            img = img + 0.25 * v_ref[corner_rows(a, c), :].astype(jnp.float32)
            w_ref[corner_rows(a, c), :] = (omega * img).astype(jnp.bfloat16)
    tangent = lax.dot_general(
        v_ref[...], w_ref[...], (((0,), (0,)), ((), ())), preferred_element_type=jnp.float32
    )
    scale = scale_ref[0:1, 0:1]
    out_ref[pl.ds(0, modes), :] = tangent * scale
    force_row = jnp.sum(force_acc, axis=0, keepdims=True) * scale
    out_ref[pl.ds(modes, 8), :] = jnp.concatenate(
        [force_row, jnp.zeros((7, modes), jnp.float32)], axis=0
    )


def element_stage(arrived3, slot, state, omega, stiff, scale):
    n_el = slot.shape[1]
    n_slot = arrived3.shape[0]
    lane = jnp.arange(n_slot, dtype=jnp.int32)[None, :]
    onehot = (slot.reshape(8 * n_el, 1) == lane).astype(jnp.bfloat16)
    signed = jnp.concatenate(
        [sum(jnp.where(slot[a][:, None] == lane, G[a][k], 0.0) for a in range(8)) for k in range(3)], axis=0
    ).astype(jnp.bfloat16)
    modes = arrived3.shape[1] // 3
    comp = jnp.arange(3 * modes) // modes
    state_blocks = jnp.where(
        comp[:, None] == jnp.arange(128)[None, :], jnp.tile(state, 3)[:, None], jnp.zeros((), state.dtype)
    )
    vmem = pltpu.MemorySpace.VMEM if hasattr(pltpu, "MemorySpace") else pltpu.TPUMemorySpace.VMEM
    return pl.pallas_call(
        element_body,
        out_shape=jax.ShapeDtypeStruct((modes + 8, modes), jnp.float32),
        in_specs=[pl.BlockSpec(memory_space=vmem)] * 7,
        out_specs=pl.BlockSpec(memory_space=vmem),
        scratch_shapes=[
            pltpu.VMEM((24 * n_el, modes), jnp.bfloat16),
            pltpu.VMEM((24 * n_el, modes), jnp.bfloat16),
        ],
    )(arrived3, onehot, signed, state_blocks, omega.reshape(n_el, 1), stiff.reshape(n_el, 1),
      jnp.broadcast_to(scale, (8, 128)))


def gather_body(basis_ref, rows_ref, out_ref):
    comps, nodes, modes = basis_ref.shape
    n_rows = rows_ref.shape[1]
    node = lax.broadcasted_iota(jnp.int32, (nodes, n_rows), 0)
    onehot_t = (node == rows_ref[...]).astype(jnp.bfloat16)
    for c in range(comps):
        picked = lax.dot_general(
            onehot_t, basis_ref[c], (((0,), (0,)), ((), ())), preferred_element_type=jnp.float32
        )
        out_ref[:, pl.ds(c * modes, modes)] = picked.astype(jnp.bfloat16)


def gather_rows(by_component, rows):
    comps, nodes, modes = by_component.shape
    n_rows = rows.shape[0]
    vmem = pltpu.MemorySpace.VMEM if hasattr(pltpu, "MemorySpace") else pltpu.TPUMemorySpace.VMEM
    return pl.pallas_call(
        gather_body,
        out_shape=jax.ShapeDtypeStruct((n_rows, comps * modes), jnp.bfloat16),
        in_specs=[pl.BlockSpec(memory_space=vmem)] * 2,
        out_specs=pl.BlockSpec(memory_space=vmem),
    )(by_component, rows.reshape(1, n_rows))

def local(basis, send_rows, elem_slot, set_size, elem_weight, element_stiffening, state, load):
    basis_modes = basis.shape[2]
    n_elem = lax.psum(1, "elem")
    n_blk = lax.psum(1, "blk")
    by_component = jnp.transpose(basis, (1, 0, 2))
    outgoing = gather_rows(by_component, send_rows[0, 0])
    arrived = lax.all_to_all(outgoing, "elem", split_axis=0, concat_axis=0, tiled=True)
    element_count = elem_slot.shape[1]
    set_index = lax.axis_index("elem")
    block_index = lax.axis_index("blk")
    live = lax.dynamic_index_in_dim(set_size, set_index, keepdims=False)
    position = block_index * element_count + jnp.arange(element_count, dtype=jnp.int32)
    weights = jnp.where(position < live, elem_weight, jnp.zeros_like(elem_weight))
    scale = lax.rsqrt(24.0 * jnp.sum(set_size).astype(jnp.float32))
    stacked = element_stage(arrived, elem_slot, state, weights, element_stiffening, scale)
    rows = basis_modes // n_elem
    cols = basis_modes // n_blk
    n_y = n_blk // 2
    core = block_index % 2
    chip = block_index // 2
    by_dest = stacked.reshape(basis_modes + 8, n_y, 2, cols)
    pair = [(b, b ^ 1) for b in range(n_blk)]
    sent = lax.dynamic_index_in_dim(by_dest, 1 - core, axis=2, keepdims=False)
    kept = lax.dynamic_index_in_dim(by_dest, core, axis=2, keepdims=False)
    chip_sum = kept + lax.ppermute(sent, "blk", pair)
    halfway = lax.dynamic_index_in_dim(chip_sum, chip, axis=1, keepdims=False)
    for shift in range(1, n_y):
        ring = [(2 * y + c, 2 * ((y + shift) % n_y) + c) for y in range(n_y) for c in range(2)]
        piece = lax.dynamic_index_in_dim(chip_sum, (chip + shift) % n_y, axis=1, keepdims=False)
        halfway = halfway + lax.ppermute(piece, "blk", ring)
    force_cols = halfway[basis_modes] - jnp.where(set_index == 0, load, jnp.zeros_like(load))
    tangent_rows = halfway[:basis_modes].reshape(n_elem, rows, cols)
    chunks = jnp.concatenate(
        [tangent_rows, jnp.broadcast_to(force_cols[None, None, :], (n_elem, 1, cols))], axis=1
    )
    flat = chunks.reshape(n_elem, (rows + 1) * cols)
    arrived_chunks = lax.all_to_all(flat, "elem", split_axis=0, concat_axis=0, tiled=True)
    mine = jnp.sum(arrived_chunks, axis=0).reshape(rows + 1, cols)
    return (mine[:rows], mine[rows])


def solution(mesh):
    in_specs = (
        P("elem", None, None),
        P("elem", "blk", None),
        P(None, ("elem", "blk")),
        P(),
        P(("elem", "blk")),
        P(("elem", "blk")),
        P(),
        P("blk"),
    )
    out_specs = (P("elem", "blk"), P("blk"))
    return jax.shard_map(local, mesh=mesh, in_specs=in_specs, out_specs=out_specs, check_vma=False)
```

```python
import jax
import jax.numpy as jnp
from jax import lax
from jax.experimental import pallas as pl
from jax.experimental.pallas import tpu as pltpu
from jax.sharding import PartitionSpec as P

G = [[(2 * ((a >> k) & 1) - 1) * 0.25 for k in range(3)] for a in range(8)]


def element_body(arrived_ref, onehot_ref, signed_ref, state_ref, omega_ref, stiff_ref, scale_ref, out_ref, v_ref, w_ref):
    n_el = omega_ref.shape[0]
    modes = out_ref.shape[1]
    onehot = onehot_ref[...]
    corners = jnp.dot(onehot, arrived_ref[...], preferred_element_type=jnp.float32).astype(jnp.bfloat16)
    for c in range(3):
        v_ref[pl.ds(c * 8 * n_el, 8 * n_el), :] = corners[:, c * modes:(c + 1) * modes]
    disp_all = jnp.dot(corners, state_ref[...], preferred_element_type=jnp.float32)
    disp = {}
    for a in range(8):
        for c in range(3):
            disp[a, c] = disp_all[a * n_el:(a + 1) * n_el, c:c + 1]
    signed_all = signed_ref[...]
    grad_all = jnp.dot(signed_all, arrived_ref[...], preferred_element_type=jnp.float32)
    grad = {}
    for k in range(3):
        for c in range(3):
            grad[k, c] = grad_all[k * n_el:(k + 1) * n_el, c * modes:(c + 1) * modes]

    def corner_rows(a, c):
        return pl.ds(c * 8 * n_el + a * n_el, n_el)

    h = {}
    for k in range(3):
        for c in range(3):
            acc = G[0][k] * disp[0, c]
            for a in range(1, 8):
                acc = acc + G[a][k] * disp[a, c]
            h[k, c] = acc
    stiff = stiff_ref[...]
    omega = omega_ref[...]
    vol = h[0, 0] + h[1, 1] + h[2, 2]
    lam = 1.0 + stiff * vol ** 2 - 2.0 / 3.0
    press = vol + stiff * vol ** 3 / 3.0 - 2.0 / 3.0 * vol
    stress = {}
    for k in range(3):
        for c in range(3):
            s = h[k, c] + h[c, k]
            if k == c:
                s = s + press
            stress[k, c] = s
    force_acc = jnp.zeros((n_el, modes), jnp.float32)
    for a in range(8):
        for c in range(3):
            f = G[a][0] * stress[0, c] + G[a][1] * stress[1, c] + G[a][2] * stress[2, c]
            f = f + 0.25 * disp[a, c]
            wf = (f * omega).astype(jnp.bfloat16).astype(jnp.float32)
            force_acc = force_acc + v_ref[corner_rows(a, c), :].astype(jnp.float32) * wf
    trace = grad[0, 0] + grad[1, 1] + grad[2, 2]
    for a in range(8):
        for c in range(3):
            img = G[a][0] * (grad[0, c] + grad[c, 0])
            img = img + G[a][1] * (grad[1, c] + grad[c, 1])
            img = img + G[a][2] * (grad[2, c] + grad[c, 2])
            img = img + (lam * G[a][c]) * trace
            img = img + 0.25 * v_ref[corner_rows(a, c), :].astype(jnp.float32)
            w_ref[corner_rows(a, c), :] = (omega * img).astype(jnp.bfloat16)
    tangent = lax.dot_general(
        v_ref[...], w_ref[...], (((0,), (0,)), ((), ())), preferred_element_type=jnp.float32
    )
    scale = scale_ref[0:1, 0:1]
    out_ref[pl.ds(0, modes), :] = tangent * scale
    force_row = jnp.sum(force_acc, axis=0, keepdims=True) * scale
    out_ref[pl.ds(modes, 8), :] = jnp.concatenate(
        [force_row, jnp.zeros((7, modes), jnp.float32)], axis=0
    )


def element_stage(arrived3, slot, state, omega, stiff, scale):
    n_el = slot.shape[1]
    n_slot = arrived3.shape[0]
    lane = jnp.arange(n_slot, dtype=jnp.int32)[None, :]
    onehot = (slot.reshape(8 * n_el, 1) == lane).astype(jnp.bfloat16)
    signed = jnp.concatenate(
        [sum(jnp.where(slot[a][:, None] == lane, G[a][k], 0.0) for a in range(8)) for k in range(3)], axis=0
    ).astype(jnp.bfloat16)
    modes = arrived3.shape[1] // 3
    comp = jnp.arange(3 * modes) // modes
    state_blocks = jnp.where(
        comp[:, None] == jnp.arange(128)[None, :], jnp.tile(state, 3)[:, None], jnp.zeros((), state.dtype)
    )
    vmem = pltpu.MemorySpace.VMEM if hasattr(pltpu, "MemorySpace") else pltpu.TPUMemorySpace.VMEM
    return pl.pallas_call(
        element_body,
        out_shape=jax.ShapeDtypeStruct((modes + 8, modes), jnp.float32),
        in_specs=[pl.BlockSpec(memory_space=vmem)] * 7,
        out_specs=pl.BlockSpec(memory_space=vmem),
        scratch_shapes=[
            pltpu.VMEM((24 * n_el, modes), jnp.bfloat16),
            pltpu.VMEM((24 * n_el, modes), jnp.bfloat16),
        ],
    )(arrived3, onehot, signed, state_blocks, omega.reshape(n_el, 1), stiff.reshape(n_el, 1),
      jnp.broadcast_to(scale, (8, 128)))


def gather_body(basis_ref, rows_ref, out_ref):
    comps, nodes, modes = basis_ref.shape
    n_rows = rows_ref.shape[1]
    node = lax.broadcasted_iota(jnp.int32, (nodes, n_rows), 0)
    onehot_t = (node == rows_ref[...]).astype(jnp.bfloat16)
    for c in range(comps):
        picked = lax.dot_general(
            onehot_t, basis_ref[c], (((0,), (0,)), ((), ())), preferred_element_type=jnp.float32
        )
        out_ref[:, pl.ds(c * modes, modes)] = picked.astype(jnp.bfloat16)


def gather_rows(by_component, rows):
    comps, nodes, modes = by_component.shape
    n_rows = rows.shape[0]
    vmem = pltpu.MemorySpace.VMEM if hasattr(pltpu, "MemorySpace") else pltpu.TPUMemorySpace.VMEM
    return pl.pallas_call(
        gather_body,
        out_shape=jax.ShapeDtypeStruct((n_rows, comps * modes), jnp.bfloat16),
        in_specs=[pl.BlockSpec(memory_space=vmem)] * 2,
        out_specs=pl.BlockSpec(memory_space=vmem),
    )(by_component, rows.reshape(1, n_rows))

def local(basis, send_rows, elem_slot, set_size, elem_weight, element_stiffening, state, load):
    basis_modes = basis.shape[2]
    n_elem = lax.psum(1, "elem")
    n_blk = lax.psum(1, "blk")
    by_component = jnp.transpose(basis, (1, 0, 2))
    outgoing = gather_rows(by_component, send_rows[0, 0])
    arrived = lax.all_to_all(outgoing, "elem", split_axis=0, concat_axis=0, tiled=True)
    element_count = elem_slot.shape[1]
    set_index = lax.axis_index("elem")
    block_index = lax.axis_index("blk")
    live = lax.dynamic_index_in_dim(set_size, set_index, keepdims=False)
    position = block_index * element_count + jnp.arange(element_count, dtype=jnp.int32)
    weights = jnp.where(position < live, elem_weight, jnp.zeros_like(elem_weight))
    scale = lax.rsqrt(24.0 * jnp.sum(set_size).astype(jnp.float32))
    stacked = element_stage(arrived, elem_slot, state, weights, element_stiffening, scale)
    rows = basis_modes // n_elem
    cols = basis_modes // n_blk
    n_y = n_blk // 2
    core = block_index % 2
    chip = block_index // 2
    by_dest = stacked.reshape(basis_modes + 8, n_y, 2, cols)
    pair = [(b, b ^ 1) for b in range(n_blk)]
    sent = lax.dynamic_index_in_dim(by_dest, 1 - core, axis=2, keepdims=False)
    kept = lax.dynamic_index_in_dim(by_dest, core, axis=2, keepdims=False)
    chip_sum = kept + lax.ppermute(sent, "blk", pair)
    halfway = lax.dynamic_index_in_dim(chip_sum, chip, axis=1, keepdims=False)
    for shift in sorted(range(1, n_y), key=lambda d: -min(d, n_y - d)):
        ring = [(2 * y + c, 2 * ((y + shift) % n_y) + c) for y in range(n_y) for c in range(2)]
        piece = lax.dynamic_index_in_dim(chip_sum, (chip + shift) % n_y, axis=1, keepdims=False)
        halfway = halfway + lax.ppermute(piece, "blk", ring)
    force_cols = halfway[basis_modes] - jnp.where(set_index == 0, load, jnp.zeros_like(load))
    tangent_rows = halfway[:basis_modes].reshape(n_elem, rows, cols)
    chunks = jnp.concatenate(
        [tangent_rows, jnp.broadcast_to(force_cols[None, None, :], (n_elem, 1, cols))], axis=1
    )
    flat = chunks.reshape(n_elem, (rows + 1) * cols)
    arrived_chunks = lax.all_to_all(flat, "elem", split_axis=0, concat_axis=0, tiled=True)
    mine = jnp.sum(arrived_chunks, axis=0).reshape(rows + 1, cols)
    return (mine[:rows], mine[rows])


def solution(mesh):
    in_specs = (
        P("elem", None, None),
        P("elem", "blk", None),
        P(None, ("elem", "blk")),
        P(),
        P(("elem", "blk")),
        P(("elem", "blk")),
        P(),
        P("blk"),
    )
    out_specs = (P("elem", "blk"), P("blk"))
    return jax.shard_map(local, mesh=mesh, in_specs=in_specs, out_specs=out_specs, check_vma=False)
```

```python
import jax
import jax.numpy as jnp
from jax import lax
from jax.experimental import pallas as pl
from jax.experimental.pallas import tpu as pltpu
from jax.sharding import PartitionSpec as P

G = [[(2 * ((a >> k) & 1) - 1) * 0.25 for k in range(3)] for a in range(8)]


def element_body(arrived_ref, onehot_ref, signed_ref, state_ref, omega_ref, stiff_ref, scale_ref, out_ref, v_ref, w_ref):
    n_el = omega_ref.shape[0]
    modes = out_ref.shape[2] * 2
    onehot = onehot_ref[...]
    corners = jnp.dot(onehot, arrived_ref[...], preferred_element_type=jnp.float32).astype(jnp.bfloat16)
    for c in range(3):
        v_ref[pl.ds(c * 8 * n_el, 8 * n_el), :] = corners[:, c * modes:(c + 1) * modes]
    disp_all = jnp.dot(corners, state_ref[...], preferred_element_type=jnp.float32)
    disp = {}
    for a in range(8):
        for c in range(3):
            disp[a, c] = disp_all[a * n_el:(a + 1) * n_el, c:c + 1]
    signed_all = signed_ref[...]
    grad_all = jnp.dot(signed_all, arrived_ref[...], preferred_element_type=jnp.float32)
    grad = {}
    for k in range(3):
        for c in range(3):
            grad[k, c] = grad_all[k * n_el:(k + 1) * n_el, c * modes:(c + 1) * modes]

    def corner_rows(a, c):
        return pl.ds(c * 8 * n_el + a * n_el, n_el)

    h = {}
    for k in range(3):
        for c in range(3):
            acc = G[0][k] * disp[0, c]
            for a in range(1, 8):
                acc = acc + G[a][k] * disp[a, c]
            h[k, c] = acc
    stiff = stiff_ref[...]
    omega = omega_ref[...]
    vol = h[0, 0] + h[1, 1] + h[2, 2]
    lam = 1.0 + stiff * vol ** 2 - 2.0 / 3.0
    press = vol + stiff * vol ** 3 / 3.0 - 2.0 / 3.0 * vol
    stress = {}
    for k in range(3):
        for c in range(3):
            s = h[k, c] + h[c, k]
            if k == c:
                s = s + press
            stress[k, c] = s
    force_acc = jnp.zeros((n_el, modes), jnp.float32)
    for a in range(8):
        for c in range(3):
            f = G[a][0] * stress[0, c] + G[a][1] * stress[1, c] + G[a][2] * stress[2, c]
            f = f + 0.25 * disp[a, c]
            wf = (f * omega).astype(jnp.bfloat16).astype(jnp.float32)
            force_acc = force_acc + v_ref[corner_rows(a, c), :].astype(jnp.float32) * wf
    trace = grad[0, 0] + grad[1, 1] + grad[2, 2]
    for a in range(8):
        for c in range(3):
            img = G[a][0] * (grad[0, c] + grad[c, 0])
            img = img + G[a][1] * (grad[1, c] + grad[c, 1])
            img = img + G[a][2] * (grad[2, c] + grad[c, 2])
            img = img + (lam * G[a][c]) * trace
            img = img + 0.25 * v_ref[corner_rows(a, c), :].astype(jnp.float32)
            w_ref[corner_rows(a, c), :] = (omega * img).astype(jnp.bfloat16)
    tangent = lax.dot_general(
        v_ref[...], w_ref[...], (((0,), (0,)), ((), ())), preferred_element_type=jnp.float32
    )
    scale = scale_ref[0:1, 0:1]
    tangent = tangent * scale
    force_rows = jnp.concatenate(
        [jnp.sum(force_acc, axis=0, keepdims=True) * scale, jnp.zeros((7, modes), jnp.float32)], axis=0
    )
    width = modes // 8
    for half in range(2):
        for y in range(4):
            src = (2 * y + half) * width
            out_ref[half, pl.ds(0, modes), pl.ds(y * width, width)] = tangent[:, src:src + width]
            out_ref[half, pl.ds(modes, 8), pl.ds(y * width, width)] = force_rows[:, src:src + width]


def element_stage(arrived3, slot, state, omega, stiff, scale):
    n_el = slot.shape[1]
    n_slot = arrived3.shape[0]
    lane = jnp.arange(n_slot, dtype=jnp.int32)[None, :]
    onehot = (slot.reshape(8 * n_el, 1) == lane).astype(jnp.bfloat16)
    signed = jnp.concatenate(
        [sum(jnp.where(slot[a][:, None] == lane, G[a][k], 0.0) for a in range(8)) for k in range(3)], axis=0
    ).astype(jnp.bfloat16)
    modes = arrived3.shape[1] // 3
    comp = jnp.arange(3 * modes) // modes
    state_blocks = jnp.where(
        comp[:, None] == jnp.arange(128)[None, :], jnp.tile(state, 3)[:, None], jnp.zeros((), state.dtype)
    )
    vmem = pltpu.MemorySpace.VMEM if hasattr(pltpu, "MemorySpace") else pltpu.TPUMemorySpace.VMEM
    return pl.pallas_call(
        element_body,
        out_shape=jax.ShapeDtypeStruct((2, modes + 8, modes // 2), jnp.float32),
        in_specs=[pl.BlockSpec(memory_space=vmem)] * 7,
        out_specs=pl.BlockSpec(memory_space=vmem),
        scratch_shapes=[
            pltpu.VMEM((24 * n_el, modes), jnp.bfloat16),
            pltpu.VMEM((24 * n_el, modes), jnp.bfloat16),
        ],
    )(arrived3, onehot, signed, state_blocks, omega.reshape(n_el, 1), stiff.reshape(n_el, 1),
      jnp.broadcast_to(scale, (8, 128)))


def gather_body(basis_ref, rows_ref, out_ref):
    comps, nodes, modes = basis_ref.shape
    n_rows = rows_ref.shape[1]
    node = lax.broadcasted_iota(jnp.int32, (nodes, n_rows), 0)
    onehot_t = (node == rows_ref[...]).astype(jnp.bfloat16)
    for c in range(comps):
        picked = lax.dot_general(
            onehot_t, basis_ref[c], (((0,), (0,)), ((), ())), preferred_element_type=jnp.float32
        )
        out_ref[:, pl.ds(c * modes, modes)] = picked.astype(jnp.bfloat16)


def gather_rows(by_component, rows):
    comps, nodes, modes = by_component.shape
    n_rows = rows.shape[0]
    vmem = pltpu.MemorySpace.VMEM if hasattr(pltpu, "MemorySpace") else pltpu.TPUMemorySpace.VMEM
    return pl.pallas_call(
        gather_body,
        out_shape=jax.ShapeDtypeStruct((n_rows, comps * modes), jnp.bfloat16),
        in_specs=[pl.BlockSpec(memory_space=vmem)] * 2,
        out_specs=pl.BlockSpec(memory_space=vmem),
    )(by_component, rows.reshape(1, n_rows))

def local(basis, send_rows, elem_slot, set_size, elem_weight, element_stiffening, state, load):
    basis_modes = basis.shape[2]
    n_elem = lax.psum(1, "elem")
    n_blk = lax.psum(1, "blk")
    by_component = jnp.transpose(basis, (1, 0, 2))
    outgoing = gather_rows(by_component, send_rows[0, 0])
    arrived = lax.all_to_all(outgoing, "elem", split_axis=0, concat_axis=0, tiled=True)
    element_count = elem_slot.shape[1]
    set_index = lax.axis_index("elem")
    block_index = lax.axis_index("blk")
    live = lax.dynamic_index_in_dim(set_size, set_index, keepdims=False)
    position = block_index * element_count + jnp.arange(element_count, dtype=jnp.int32)
    weights = jnp.where(position < live, elem_weight, jnp.zeros_like(elem_weight))
    scale = lax.rsqrt(24.0 * jnp.sum(set_size).astype(jnp.float32))
    stacked = element_stage(arrived, elem_slot, state, weights, element_stiffening, scale)
    rows = basis_modes // n_elem
    cols = basis_modes // n_blk
    n_y = n_blk // 2
    core = block_index % 2
    chip = block_index // 2
    pair = [(b, b ^ 1) for b in range(n_blk)]
    sent = lax.dynamic_index_in_dim(stacked, 1 - core, axis=0, keepdims=False)
    kept = lax.dynamic_index_in_dim(stacked, core, axis=0, keepdims=False)
    chip_sum = (kept + lax.ppermute(sent, "blk", pair)).reshape(basis_modes + 8, n_y, cols)
    halfway = lax.dynamic_index_in_dim(chip_sum, chip, axis=1, keepdims=False)
    for shift in range(1, n_y):
        ring = [(2 * y + c, 2 * ((y + shift) % n_y) + c) for y in range(n_y) for c in range(2)]
        piece = lax.dynamic_index_in_dim(chip_sum, (chip + shift) % n_y, axis=1, keepdims=False)
        halfway = halfway + lax.ppermute(piece, "blk", ring)
    force_cols = halfway[basis_modes] - jnp.where(set_index == 0, load, jnp.zeros_like(load))
    tangent_rows = halfway[:basis_modes].reshape(n_elem, rows, cols)
    chunks = jnp.concatenate(
        [tangent_rows, jnp.broadcast_to(force_cols[None, None, :], (n_elem, 1, cols))], axis=1
    )
    flat = chunks.reshape(n_elem, (rows + 1) * cols)
    arrived_chunks = lax.all_to_all(flat, "elem", split_axis=0, concat_axis=0, tiled=True)
    mine = jnp.sum(arrived_chunks, axis=0).reshape(rows + 1, cols)
    return (mine[:rows], mine[rows])


def solution(mesh):
    in_specs = (
        P("elem", None, None),
        P("elem", "blk", None),
        P(None, ("elem", "blk")),
        P(),
        P(("elem", "blk")),
        P(("elem", "blk")),
        P(),
        P("blk"),
    )
    out_specs = (P("elem", "blk"), P("blk"))
    return jax.shard_map(local, mesh=mesh, in_specs=in_specs, out_specs=out_specs, check_vma=False)
```

```python
import jax
import jax.numpy as jnp
from jax import lax
from jax.experimental import pallas as pl
from jax.experimental.pallas import tpu as pltpu
from jax.sharding import PartitionSpec as P

G = [[(2 * ((a >> k) & 1) - 1) * 0.25 for k in range(3)] for a in range(8)]


def element_body(arrived_ref, onehot_ref, signed_ref, state_ref, omega_ref, stiff_ref, scale_ref, out_ref, v_ref, w_ref):
    n_el = omega_ref.shape[0]
    modes = out_ref.shape[1]
    onehot = onehot_ref[...]
    corners = jnp.dot(onehot, arrived_ref[...], preferred_element_type=jnp.float32).astype(jnp.bfloat16)
    for c in range(3):
        v_ref[pl.ds(c * 8 * n_el, 8 * n_el), :] = corners[:, c * modes:(c + 1) * modes]
    disp_all = jnp.dot(corners, state_ref[...], preferred_element_type=jnp.float32)
    disp = {}
    for a in range(8):
        for c in range(3):
            disp[a, c] = disp_all[a * n_el:(a + 1) * n_el, c:c + 1]
    signed_all = signed_ref[...]
    grad_all = jnp.dot(signed_all, arrived_ref[...], preferred_element_type=jnp.float32)
    grad = {}
    for k in range(3):
        for c in range(3):
            grad[k, c] = grad_all[k * n_el:(k + 1) * n_el, c * modes:(c + 1) * modes]

    def corner_rows(a, c):
        return pl.ds(c * 8 * n_el + a * n_el, n_el)

    h = {}
    for k in range(3):
        for c in range(3):
            acc = G[0][k] * disp[0, c]
            for a in range(1, 8):
                acc = acc + G[a][k] * disp[a, c]
            h[k, c] = acc
    stiff = stiff_ref[...]
    omega = omega_ref[...]
    vol = h[0, 0] + h[1, 1] + h[2, 2]
    lam = 1.0 + stiff * vol ** 2 - 2.0 / 3.0
    press = vol + stiff * vol ** 3 / 3.0 - 2.0 / 3.0 * vol
    stress = {}
    for k in range(3):
        for c in range(3):
            s = h[k, c] + h[c, k]
            if k == c:
                s = s + press
            stress[k, c] = s
    force_acc = jnp.zeros((n_el, modes), jnp.float32)
    for a in range(8):
        for c in range(3):
            f = G[a][0] * stress[0, c] + G[a][1] * stress[1, c] + G[a][2] * stress[2, c]
            f = f + 0.25 * disp[a, c]
            wf = (f * omega).astype(jnp.bfloat16).astype(jnp.float32)
            force_acc = force_acc + v_ref[corner_rows(a, c), :].astype(jnp.float32) * wf
    trace = grad[0, 0] + grad[1, 1] + grad[2, 2]
    for a in range(8):
        for c in range(3):
            img = G[a][0] * (grad[0, c] + grad[c, 0])
            img = img + G[a][1] * (grad[1, c] + grad[c, 1])
            img = img + G[a][2] * (grad[2, c] + grad[c, 2])
            img = img + (lam * G[a][c]) * trace
            img = img + 0.25 * v_ref[corner_rows(a, c), :].astype(jnp.float32)
            w_ref[corner_rows(a, c), :] = (omega * img).astype(jnp.bfloat16)
    tangent = lax.dot_general(
        v_ref[...], w_ref[...], (((0,), (0,)), ((), ())), preferred_element_type=jnp.float32
    )
    scale = scale_ref[0:1, 0:1]
    out_ref[pl.ds(0, modes), :] = tangent * scale
    force_row = jnp.sum(force_acc, axis=0, keepdims=True) * scale
    out_ref[pl.ds(modes, 8), :] = jnp.concatenate(
        [force_row, jnp.zeros((7, modes), jnp.float32)], axis=0
    )


def element_stage(arrived3, slot, state, omega, stiff, scale):
    n_el = slot.shape[1]
    n_slot = arrived3.shape[0]
    lane = jnp.arange(n_slot, dtype=jnp.int32)[None, :]
    onehot = (slot.reshape(8 * n_el, 1) == lane).astype(jnp.bfloat16)
    signed = jnp.concatenate(
        [sum(jnp.where(slot[a][:, None] == lane, G[a][k], 0.0) for a in range(8)) for k in range(3)], axis=0
    ).astype(jnp.bfloat16)
    modes = arrived3.shape[1] // 3
    comp = jnp.arange(3 * modes) // modes
    state_blocks = jnp.where(
        comp[:, None] == jnp.arange(8)[None, :], jnp.tile(state, 3)[:, None], jnp.zeros((), state.dtype)
    )
    vmem = pltpu.MemorySpace.VMEM if hasattr(pltpu, "MemorySpace") else pltpu.TPUMemorySpace.VMEM
    return pl.pallas_call(
        element_body,
        out_shape=jax.ShapeDtypeStruct((modes + 8, modes), jnp.float32),
        in_specs=[pl.BlockSpec(memory_space=vmem)] * 7,
        out_specs=pl.BlockSpec(memory_space=vmem),
        scratch_shapes=[
            pltpu.VMEM((24 * n_el, modes), jnp.bfloat16),
            pltpu.VMEM((24 * n_el, modes), jnp.bfloat16),
        ],
    )(arrived3, onehot, signed, state_blocks, omega.reshape(n_el, 1), stiff.reshape(n_el, 1),
      jnp.broadcast_to(scale, (8, 128)))


def gather_body(basis_ref, rows_ref, out_ref):
    comps, nodes, modes = basis_ref.shape
    n_rows = rows_ref.shape[1]
    node = lax.broadcasted_iota(jnp.int32, (nodes, n_rows), 0)
    onehot_t = (node == rows_ref[...]).astype(jnp.bfloat16)
    for c in range(comps):
        picked = lax.dot_general(
            onehot_t, basis_ref[c], (((0,), (0,)), ((), ())), preferred_element_type=jnp.float32
        )
        out_ref[:, pl.ds(c * modes, modes)] = picked.astype(jnp.bfloat16)


def gather_rows(by_component, rows):
    comps, nodes, modes = by_component.shape
    n_rows = rows.shape[0]
    vmem = pltpu.MemorySpace.VMEM if hasattr(pltpu, "MemorySpace") else pltpu.TPUMemorySpace.VMEM
    return pl.pallas_call(
        gather_body,
        out_shape=jax.ShapeDtypeStruct((n_rows, comps * modes), jnp.bfloat16),
        in_specs=[pl.BlockSpec(memory_space=vmem)] * 2,
        out_specs=pl.BlockSpec(memory_space=vmem),
    )(by_component, rows.reshape(1, n_rows))

def local(basis, send_rows, elem_slot, set_size, elem_weight, element_stiffening, state, load):
    basis_modes = basis.shape[2]
    n_elem = lax.psum(1, "elem")
    n_blk = lax.psum(1, "blk")
    by_component = jnp.transpose(basis, (1, 0, 2))
    outgoing = gather_rows(by_component, send_rows[0, 0])
    arrived = lax.all_to_all(outgoing, "elem", split_axis=0, concat_axis=0, tiled=True)
    element_count = elem_slot.shape[1]
    set_index = lax.axis_index("elem")
    block_index = lax.axis_index("blk")
    live = lax.dynamic_index_in_dim(set_size, set_index, keepdims=False)
    position = block_index * element_count + jnp.arange(element_count, dtype=jnp.int32)
    weights = jnp.where(position < live, elem_weight, jnp.zeros_like(elem_weight))
    scale = lax.rsqrt(24.0 * jnp.sum(set_size).astype(jnp.float32))
    stacked = element_stage(arrived, elem_slot, state, weights, element_stiffening, scale)
    rows = basis_modes // n_elem
    cols = basis_modes // n_blk
    n_y = n_blk // 2
    core = block_index % 2
    chip = block_index // 2
    by_dest = stacked.reshape(basis_modes + 8, n_y, 2, cols)
    pair = [(b, b ^ 1) for b in range(n_blk)]
    sent = lax.dynamic_index_in_dim(by_dest, 1 - core, axis=2, keepdims=False)
    kept = lax.dynamic_index_in_dim(by_dest, core, axis=2, keepdims=False)
    chip_sum = kept + lax.ppermute(sent, "blk", pair)
    halfway = lax.dynamic_index_in_dim(chip_sum, chip, axis=1, keepdims=False)
    for shift in range(1, n_y):
        ring = [(2 * y + c, 2 * ((y + shift) % n_y) + c) for y in range(n_y) for c in range(2)]
        piece = lax.dynamic_index_in_dim(chip_sum, (chip + shift) % n_y, axis=1, keepdims=False)
        halfway = halfway + lax.ppermute(piece, "blk", ring)
    force_cols = halfway[basis_modes] - jnp.where(set_index == 0, load, jnp.zeros_like(load))
    tangent_rows = halfway[:basis_modes].reshape(n_elem, rows, cols)
    chunks = jnp.concatenate(
        [tangent_rows, jnp.broadcast_to(force_cols[None, None, :], (n_elem, 1, cols))], axis=1
    )
    flat = chunks.reshape(n_elem, (rows + 1) * cols)
    arrived_chunks = lax.all_to_all(flat, "elem", split_axis=0, concat_axis=0, tiled=True)
    mine = jnp.sum(arrived_chunks, axis=0).reshape(rows + 1, cols)
    return (mine[:rows], mine[rows])


def solution(mesh):
    in_specs = (
        P("elem", None, None),
        P("elem", "blk", None),
        P(None, ("elem", "blk")),
        P(),
        P(("elem", "blk")),
        P(("elem", "blk")),
        P(),
        P("blk"),
    )
    out_specs = (P("elem", "blk"), P("blk"))
    return jax.shard_map(local, mesh=mesh, in_specs=in_specs, out_specs=out_specs, check_vma=False)
```
